128 devices in a mesh: gx: 8 (over y_hi, z), gy: 8 (over x, y_lo), gz: 2 (over core).
Axes of the slice: x: 4, y: 4 (y_hi: 2, y_lo: 2; y = y_hi * 2 + y_lo), z: 4, core: 2. Of those that a mesh axis runs over, the one named last changes fastest.
Arguments:
- populations0: bfloat16 [26, 16, 64, 1024], P(None, 'gz', 'gx', 'gy'), may hold values from 0 to 1, as said below
- populations1: bfloat16 [26, 16, 64, 1024], P(None, 'gz', 'gx', 'gy'), may hold values from 0 to 1, as said below
- cotangent: float32 [26, 16, 64, 1024], P(None, 'gz', 'gx', 'gy'), may hold values from -6 to 6
Outputs:
- gradient: float32 [26, 16, 64, 1024], P(None, 'gz', 'gx', 'gy')
The draws below stay inside these ranges and needn't reach their ends.
Inputs may be any that keep to these rules, and one draw needn't show every extreme that they name: `populations0`: every entry is positive; in every cell the 7 phase populations sum to between 0.1 and 1.3. `populations1`: every entry is positive; in every cell the 7 phase populations sum to between 0.1 and 1.3.
All inputs are finite; a program needn't handle non-finite values.
Results may differ from the reference program's by a relative error of at most 0.0003.
Values sent between devices are 32-bit elements; how exact they have to be, the bound alone decides.
No kernel may reach another device: no remote copies, remote signals or barrier semaphores. Data moves between devices by JAX's collectives and lax.ppermute only.
A program may use at most 64 MiB of HBM per device.

```python
import jax
import jax.numpy as jnp
import numpy as np
from jax import lax

NZ = 16
NX = 64
NY = 1024


VELOCITY = np.array([[0, 0, 0], [1, 0, 0], [-1, 0, 0], [0, 1, 0], [0, -1, 0], [0, 0, 1], [0, 0, -1], [1, 1, 0], [-1, -1, 0], [1, -1, 0], [-1, 1, 0], [1, 0, 1], [-1, 0, -1], [1, 0, -1], [-1, 0, 1], [0, 1, 1], [0, -1, -1], [0, 1, -1], [0, -1, 1]])


FLOW_WEIGHT = [1.0 / 3.0] + [1.0 / 18.0] * 6 + [1.0 / 36.0] * 12


PHASE_WEIGHT = [0.25] + [0.125] * 6


def expand_drawn(weights):
    values = [float(entry) for entry in list(weights)]
    return jnp.asarray(values, jnp.float32).reshape((-1, 1, 1, 1))


def draw_state(key):
    subkeys = jax.random.split(key, 6)
    extent = (NZ, NX, NY)
    fraction = jax.random.uniform(subkeys[0], extent, jnp.float32, 0.2, 0.8)
    velocity = jnp.clip(0.04 * jax.random.normal(subkeys[1], (3,) + extent, jnp.float32), -0.1, 0.1)
    pressure = jax.random.uniform(subkeys[2], extent, jnp.float32, 0.8, 1.2)
    density = 0.2 + 0.8 * fraction
    along_flow = expand_drawn(VELOCITY[:, 0]) * velocity[0] + expand_drawn(VELOCITY[:, 1]) * velocity[1] + expand_drawn(VELOCITY[:, 2]) * velocity[2]
    speed_square = velocity[0] * velocity[0] + velocity[1] * velocity[1] + velocity[2] * velocity[2]
    flow_noise = jax.random.uniform(subkeys[3], (19,) + extent, jnp.float32, 0.85, 1.15)
    phase_noise = jax.random.uniform(subkeys[4], (7,) + extent, jnp.float32, 0.85, 1.15)
    flow_part = expand_drawn(FLOW_WEIGHT) * (pressure + density * (3.0 * along_flow + 4.5 * along_flow * along_flow - 1.5 * speed_square)) * flow_noise
    phase_part = expand_drawn(PHASE_WEIGHT) * fraction * (1.0 + 4.0 * along_flow[:7]) * phase_noise
    return jnp.concatenate([flow_part, phase_part], 0).astype(jnp.bfloat16)


def draw_populations0(key, part):
    return draw_state(jax.random.fold_in(key, 11))


def draw_populations1(key, part):
    return draw_state(jax.random.fold_in(key, 12))


def levels(stream_key, dims, cuts, smallest, top_value):
    level = 1.0
    for dim, parts in cuts:
        heights = jax.random.uniform(jax.random.fold_in(jax.random.fold_in(stream_key, 6), dim), (parts,), jnp.float32, smallest / len(cuts), top_value / len(cuts))
        level = level * jnp.repeat(jnp.exp(heights), dims[dim] // parts).reshape((-1,) + (1,) * (len(dims) - 1 - dim))
    return level


def scatter_about(stream_key, shape, spread, limit, shards=(), held_as=jnp.bfloat16):
    result = spread * jax.random.normal(stream_key, shape, jnp.float32)
    if shards:
        result = result * levels(stream_key, shape, shards, -0.22, 0.18)
    return jnp.clip(result, -limit, limit).astype(held_as)


def setup_inputs(seed: int = 0) -> dict:
    streams_of = jax.random.split(jax.random.key(seed), 4)
    return {
        "populations0": draw_populations0(jax.random.fold_in(streams_of[3], 71), 0),
        "populations1": draw_populations1(jax.random.fold_in(streams_of[3], 71), 0),
        "cotangent": scatter_about(streams_of[2], (26, NZ, NX, NY), 1.0, 6.0, ((1, 2), (2, 8), (3, 8)), jnp.float32),
    }


VELOCITY = np.array([[0, 0, 0], [1, 0, 0], [-1, 0, 0], [0, 1, 0], [0, -1, 0], [0, 0, 1], [0, 0, -1], [1, 1, 0], [-1, -1, 0], [1, -1, 0], [-1, 1, 0], [1, 0, 1], [-1, 0, -1], [1, 0, -1], [-1, 0, 1], [0, 1, 1], [0, -1, -1], [0, 1, -1], [0, -1, 1]])
OPPOSITE = [0, 2, 1, 4, 3, 6, 5, 8, 7, 10, 9, 12, 11, 14, 13, 16, 15, 18, 17]
FLOW_WEIGHT = [1.0 / 3.0] + [1.0 / 18.0] * 6 + [1.0 / 36.0] * 12
PHASE_WEIGHT = [0.25] + [0.125] * 6
VELOCITY_ALL = np.concatenate([VELOCITY, VELOCITY[:7]], 0)
OPPOSITE_ALL = OPPOSITE + [19 + mirror for mirror in OPPOSITE[:7]]
WELL_DEPTH = 0.3
STIFFNESS = 0.6
SHARPEN = 0.3
PHASE_RATE = 1.4
UNITS = ((1, 0, 0), (0, 1, 0), (0, 0, 1))

def expand(weights, rank):
    values = [float(entry) for entry in list(weights)]
    return jnp.asarray(values, jnp.float32).reshape((-1,) + (1,) * rank)

def along(velocity_table, vector):
    rank = vector.ndim - 1
    total = expand(velocity_table[:, 0], rank) * vector[0]
    for direction in range(1, 3):
        total = total + expand(velocity_table[:, direction], rank) * vector[direction]
    return total

def collide(populations, phase_grad, potential_grad):
    rank = populations.ndim - 1
    flow_part = populations[:19]
    phase_part = populations[19:]
    fraction = lax.optimization_barrier(jnp.sum(phase_part, 0))
    density = 0.2 + 0.8 * fraction
    pressure = lax.optimization_barrier(jnp.sum(flow_part, 0))
    body_force = -fraction[None] * potential_grad
    momentum = jnp.stack([lax.optimization_barrier(jnp.sum(expand(VELOCITY[:, direction], rank) * flow_part, 0)) for direction in range(3)])
    velocity = (momentum + 0.5 * body_force) / density[None]
    along_flow = along(VELOCITY, velocity)
    speed_square = lax.optimization_barrier(jnp.sum(velocity * velocity, 0))
    relax_rate = 1.1 + 0.5 * fraction
    flow_equil = expand(FLOW_WEIGHT, rank) * (pressure + density * (3.0 * along_flow + 4.5 * along_flow * along_flow - 1.5 * speed_square))
    along_force = along(VELOCITY, body_force)
    speed_force = lax.optimization_barrier(jnp.sum(velocity * body_force, 0))
    source = expand(FLOW_WEIGHT, rank) * (3.0 * (along_force - speed_force) + 9.0 * along_flow * along_force)
    flow_post = flow_part - relax_rate * (flow_part - flow_equil) + (1.0 - 0.5 * relax_rate) * source
    magnitude = jnp.sqrt(lax.optimization_barrier(jnp.sum(phase_grad * phase_grad, 0)) + 0.0625)
    normal = phase_grad / magnitude
    along_normal = along(VELOCITY[:7], normal)
    phase_equil = expand(PHASE_WEIGHT, rank) * (fraction * (1.0 + 4.0 * along_flow[:7]) + 4.0 * SHARPEN * fraction * (1.0 - fraction) * along_normal)
    phase_post = phase_part - PHASE_RATE * (phase_part - phase_equil)
    return jnp.concatenate([flow_post, phase_post], 0)

def neighbour(values, offset):
    height = values.shape[0]
    padded = jnp.pad(values, ((1, 1), (0, 0), (0, 0)))
    shifted = padded[1 + offset[0]:1 + offset[0] + height]
    return jnp.roll(shifted, (-offset[1], -offset[2]), axis=(1, 2))

def negate(offset):
    return tuple((-entry for entry in offset))

def gradient(values):
    return jnp.stack([(neighbour(values, unit) - neighbour(values, negate(unit))) * 0.5 for unit in UNITS])

def laplace(values):
    total = -6.0 * values
    for unit in UNITS:
        total = total + neighbour(values, unit) + neighbour(values, negate(unit))
    return total

def well_term(fraction):
    return 4.0 * WELL_DEPTH * fraction * (fraction - 1.0) * (fraction - 0.5)

def phase_fields(fraction):
    potential = well_term(fraction) - STIFFNESS * laplace(fraction)
    return (gradient(fraction), gradient(potential))

def stream(post):
    height = post.shape[1]
    outputs = []
    for member in range(26):
        step_z, step_x, step_y = (int(entry) for entry in VELOCITY_ALL[member])
        values = jnp.roll(post[member], (step_x, step_y), axis=(1, 2))
        padded = jnp.pad(values, ((1, 1), (0, 0), (0, 0)))
        values = padded[1 - step_z:1 - step_z + height]
        if step_z == 1:
            values = values.at[0].set(post[OPPOSITE_ALL[member], 0])
        elif step_z == -1:
            values = values.at[height - 1].set(post[OPPOSITE_ALL[member], height - 1])
        outputs.append(values)
    return jnp.stack(outputs)

def plane_adjoint(plane_items):
    populations, phase_grad, potential_grad, arrived = plane_items
    pullback = jax.vjp(collide, populations, phase_grad, potential_grad)[1]
    return pullback(arrived)

def adjoint_step(stored, adjoint):
    populations = stored.astype(jnp.float32)
    fraction = lax.optimization_barrier(jnp.sum(populations[19:], 0))
    (phase_grad, potential_grad), phase_pullback = jax.vjp(phase_fields, fraction)
    stream_pullback = jax.vjp(stream, populations)[1]
    arrived, = stream_pullback(adjoint)
    planes = lax.map(plane_adjoint, (jnp.moveaxis(populations, 1, 0), jnp.moveaxis(phase_grad, 1, 0), jnp.moveaxis(potential_grad, 1, 0), jnp.moveaxis(arrived, 1, 0)))
    restored = [jnp.moveaxis(piece, 0, 1) for piece in planes]
    phase_adjoint, = phase_pullback((restored[1], restored[2]))
    return jnp.concatenate([restored[0][:19], restored[0][19:] + phase_adjoint[None]], 0)

def reference(populations0, populations1, cotangent):
    adjoint1 = adjoint_step(populations1, cotangent)
    return adjoint_step(populations0, adjoint1)
```

```python
import jax
import jax.numpy as jnp
import numpy as np
from jax import lax
from jax.sharding import PartitionSpec as P

VELOCITY = np.array(
    [
        [0, 0, 0],
        [1, 0, 0],
        [-1, 0, 0],
        [0, 1, 0],
        [0, -1, 0],
        [0, 0, 1],
        [0, 0, -1],
        [1, 1, 0],
        [-1, -1, 0],
        [1, -1, 0],
        [-1, 1, 0],
        [1, 0, 1],
        [-1, 0, -1],
        [1, 0, -1],
        [-1, 0, 1],
        [0, 1, 1],
        [0, -1, -1],
        [0, 1, -1],
        [0, -1, 1],
    ]
)
OPPOSITE = [0, 2, 1, 4, 3, 6, 5, 8, 7, 10, 9, 12, 11, 14, 13, 16, 15, 18, 17]
FLOW_WEIGHT = [1.0 / 3.0] + [1.0 / 18.0] * 6 + [1.0 / 36.0] * 12
PHASE_WEIGHT = [0.25] + [0.125] * 6
VELOCITY_ALL = np.concatenate([VELOCITY, VELOCITY[:7]], 0)
OPPOSITE_ALL = OPPOSITE + [19 + mirror for mirror in OPPOSITE[:7]]
WELL_DEPTH = 0.3
STIFFNESS = 0.6
SHARPEN = 0.3
PHASE_RATE = 1.4
UNITS = ((1, 0, 0), (0, 1, 0), (0, 0, 1))
CENTER = (0, 0, 0)


def expand(weights, rank):
    values = [float(entry) for entry in list(weights)]
    return jnp.asarray(values, jnp.float32).reshape((-1,) + (1,) * rank)


def along(velocity_table, vector):
    rank = vector.ndim - 1
    total = expand(velocity_table[:, 0], rank) * vector[0]
    for direction in range(1, 3):
        total = total + expand(velocity_table[:, direction], rank) * vector[direction]
    return total


def collide(populations, phase_grad, potential_grad):
    rank = populations.ndim - 1
    flow_part = populations[:19]
    phase_part = populations[19:]
    fraction = jnp.sum(phase_part, 0)
    density = 0.2 + 0.8 * fraction
    pressure = jnp.sum(flow_part, 0)
    body_force = -fraction[None] * potential_grad
    momentum = jnp.stack(
        [jnp.sum(expand(VELOCITY[:, direction], rank) * flow_part, 0) for direction in range(3)]
    )
    velocity = (momentum + 0.5 * body_force) / density[None]
    along_flow = along(VELOCITY, velocity)
    speed_square = jnp.sum(velocity * velocity, 0)
    relax_rate = 1.1 + 0.5 * fraction
    flow_equil = expand(FLOW_WEIGHT, rank) * (
        pressure + density * (3.0 * along_flow + 4.5 * along_flow * along_flow - 1.5 * speed_square)
    )
    along_force = along(VELOCITY, body_force)
    speed_force = jnp.sum(velocity * body_force, 0)
    source = expand(FLOW_WEIGHT, rank) * (
        3.0 * (along_force - speed_force) + 9.0 * along_flow * along_force
    )
    flow_post = (
        flow_part - relax_rate * (flow_part - flow_equil) + (1.0 - 0.5 * relax_rate) * source
    )
    magnitude = jnp.sqrt(jnp.sum(phase_grad * phase_grad, 0) + 0.0625)
    normal = phase_grad / magnitude
    along_normal = along(VELOCITY[:7], normal)
    phase_equil = expand(PHASE_WEIGHT, rank) * (
        fraction * (1.0 + 4.0 * along_flow[:7])
        + 4.0 * SHARPEN * fraction * (1.0 - fraction) * along_normal
    )
    phase_post = phase_part - PHASE_RATE * (phase_part - phase_equil)
    return jnp.concatenate([flow_post, phase_post], 0)


def wall_zero(extended, width, vertical_dim):
    height = extended.shape[vertical_dim]
    layer_index = lax.broadcasted_iota(jnp.int32, (height,), 0)
    position = lax.axis_index("gz")
    bricks = lax.axis_size("gz")
    bottom_wall = jnp.logical_and(layer_index < width, position == 0)
    top_wall = jnp.logical_and(layer_index >= height - width, position == bricks - 1)
    inside = jnp.where(jnp.logical_or(bottom_wall, top_wall), 0.0, 1.0).astype(extended.dtype)
    extent = [1] * extended.ndim
    extent[vertical_dim] = height
    return extended * inside.reshape(extent)


def offset_view(extended, margin, offset, extent):
    return extended[
        ...,
        margin + offset[0] : margin + offset[0] + extent[0],
        margin + offset[1] : margin + offset[1] + extent[1],
        margin + offset[2] : margin + offset[2] + extent[2],
    ]


def negate(offset):
    return tuple((-entry for entry in offset))


def gradient(extended, margin, extent):
    return jnp.stack(
        [
            (
                offset_view(extended, margin, unit, extent)
                - offset_view(extended, margin, negate(unit), extent)
            )
            * 0.5
            for unit in UNITS
        ]
    )


def laplace(extended, margin, extent):
    total = -6.0 * offset_view(extended, margin, CENTER, extent)
    for unit in UNITS:
        total = (
            total
            + offset_view(extended, margin, unit, extent)
            + offset_view(extended, margin, negate(unit), extent)
        )
    return total


def spread(extended, margin, extent):
    total = jnp.zeros(extent, jnp.float32)
    for direction in range(3):
        unit = UNITS[direction]
        total = (
            total
            + (
                offset_view(extended[direction], margin, negate(unit), extent)
                - offset_view(extended[direction], margin, unit, extent)
            )
            * 0.5
        )
    return total


def well_term(fraction):
    return 4.0 * WELL_DEPTH * fraction * (fraction - 1.0) * (fraction - 0.5)


def well_slope(fraction):
    return 4.0 * WELL_DEPTH * (3.0 * fraction * fraction - 3.0 * fraction + 0.5)


def bounce(arrived, adjoint):
    height = adjoint.shape[1]
    layer_index = lax.broadcasted_iota(jnp.int32, (height,), 0)
    position = lax.axis_index("gz")
    bricks = lax.axis_size("gz")
    bottom_wall = jnp.logical_and(layer_index == 0, position == 0).reshape((1, height, 1, 1))
    top_wall = jnp.logical_and(layer_index == height - 1, position == bricks - 1).reshape(
        (1, height, 1, 1)
    )
    rising = jnp.asarray((VELOCITY_ALL[:, 0] == 1).reshape((26, 1, 1, 1)))
    falling = jnp.asarray((VELOCITY_ALL[:, 0] == -1).reshape((26, 1, 1, 1)))
    reflect = jnp.logical_or(
        jnp.logical_and(rising, top_wall), jnp.logical_and(falling, bottom_wall)
    )
    flipped = jnp.stack([adjoint[mirror] for mirror in OPPOSITE_ALL])
    return jnp.where(reflect, flipped, arrived)


AXES = ("gz", "gx", "gy")
FACES = tuple(
    tuple(sign if a == axis else 0 for a in range(3)) for axis in range(3) for sign in (1, -1)
)
EDGES = tuple(
    tuple(sa if a == first else (sb if a == second else 0) for a in range(3))
    for first in range(3)
    for second in range(first + 1, 3)
    for sa in (1, -1)
    for sb in (1, -1)
)


def pairs_for(offset):
    order = (1, 2, 0)
    sizes = [lax.axis_size(AXES[a]) for a in order]
    shift = [offset[a] for a in order]
    pairs = []
    for i in range(sizes[0]):
        for j in range(sizes[1]):
            for k in range(sizes[2]):
                target = [(c - o) % n for c, o, n in zip((i, j, k), shift, sizes)]
                pairs.append((((i * sizes[1]) + j) * sizes[2] + k, ((target[0] * sizes[1]) + target[1]) * sizes[2] + target[2]))
    return pairs


def send_slice(values, offset, width):
    lead = values.ndim - 3
    index = [slice(None)] * lead
    for a in range(3):
        length = values.shape[lead + a]
        if offset[a] == 1:
            index.append(slice(0, width))
        elif offset[a] == -1:
            index.append(slice(length - width, length))
        else:
            index.append(slice(None))
    return values[tuple(index)]


def exchange(requests):
    results = [dict() for _ in requests]
    for offset in FACES + EDGES:
        is_edge = sum(abs(entry) for entry in offset) == 2
        parts, shapes = [], []
        for r, (values, width, with_edges, select) in enumerate(requests):
            if is_edge and not with_edges:
                continue
            fields = select(offset)
            if not fields:
                continue
            piece = send_slice(values, offset, width)
            piece = jnp.concatenate([piece[k : k + 1] for k in fields], 0)
            parts.append(piece.reshape(-1))
            shapes.append((r, fields, piece.shape))
        if not parts:
            continue
        got = lax.ppermute(jnp.concatenate(parts), ("gx", "gy", "gz"), pairs_for(offset))
        start = 0
        for r, fields, shape in shapes:
            size = int(np.prod(shape))
            results[r][offset] = (fields, got[start : start + size].reshape(shape))
            start += size
    return results


def assemble(center, pieces, width):
    lead = center.ndim - 3
    extended = jnp.pad(center, [(0, 0)] * lead + [(width, width)] * 3)
    for offset, (fields, piece) in pieces.items():
        start = [0] * lead
        for a in range(3):
            length = center.shape[lead + a]
            start.append(width + length if offset[a] == 1 else (0 if offset[a] == -1 else width))
        if fields == list(range(fields[0], fields[0] + len(fields))):
            extended = lax.dynamic_update_slice(extended, piece, [fields[0]] + start[1:])
        else:
            for i, k in enumerate(fields):
                extended = lax.dynamic_update_slice(extended, piece[i : i + 1], [k] + start[1:])
    return extended


def all_fields(count):
    return lambda offset: list(range(count))


def streamed_fields(offset):
    chosen = []
    for member in range(26):
        velocity = VELOCITY_ALL[member]
        if all(o == 0 or o == int(v) for o, v in zip(offset, velocity)):
            chosen.append(member)
    return chosen


def own_axis_fields(offset):
    if sum(abs(entry) for entry in offset) != 1:
        return []
    return [int(np.argmax(np.abs(offset)))]


def shift_along(values, halo, axis, sign):
    length = values.shape[axis]
    if sign == 1:
        return jnp.concatenate([lax.slice_in_dim(values, 1, length, axis=axis), halo], axis)
    return jnp.concatenate([halo, lax.slice_in_dim(values, 0, length - 1, axis=axis)], axis)


def stream_adjoint(adjoint, pieces):
    def piece_of(offset, member):
        fields, piece = pieces[offset]
        return piece[fields.index(member)]

    arrived = []
    for member in range(26):
        velocity = [int(entry) for entry in VELOCITY_ALL[member]]
        moving = [a for a in range(3) if velocity[a] != 0]
        values = adjoint[member]
        if len(moving) == 1:
            a = moving[0]
            values = shift_along(values, piece_of(tuple(velocity), member), a, velocity[a])
        elif len(moving) == 2:
            a, b = moving
            face_a = tuple(velocity[i] if i == a else 0 for i in range(3))
            face_b = tuple(velocity[i] if i == b else 0 for i in range(3))
            first = shift_along(values, piece_of(face_a, member), a, velocity[a])
            halo_b = shift_along(piece_of(face_b, member), piece_of(tuple(velocity), member), a, velocity[a])
            values = shift_along(first, halo_b, b, velocity[b])
        arrived.append(values)
    return bounce(jnp.stack(arrived), adjoint)


def phase_fields(fraction_ext, extent):
    box = tuple(n + 2 for n in extent)
    inner = fraction_ext[1:-1, 1:-1, 1:-1]
    potential_box = wall_zero(well_term(inner) - STIFFNESS * laplace(fraction_ext, 1, box), 1, 0)
    return gradient(fraction_ext, 2, extent), gradient(potential_box, 1, extent)


def collide_adjoint(populations, phase_grad, potential_grad, arrived):
    pullback = jax.vjp(collide, populations, phase_grad, potential_grad)[1]
    return pullback(arrived)


def phase_adjoint(fraction, adjoint_pgrad, adjoint_mgrad, extent):
    pgrad_pieces, mgrad_pieces = exchange(
        [(adjoint_pgrad, 1, False, own_axis_fields), (adjoint_mgrad, 2, True, all_fields(3))]
    )
    mgrad_ext = wall_zero(assemble(adjoint_mgrad, mgrad_pieces, 2), 2, 1)
    box = tuple(n + 2 for n in extent)
    mu_box = wall_zero(spread(mgrad_ext, 1, box), 1, 0)
    pgrad_ext = wall_zero(assemble(adjoint_pgrad, pgrad_pieces, 1), 1, 1)
    return (
        well_slope(fraction) * mu_box[1:-1, 1:-1, 1:-1]
        - STIFFNESS * laplace(mu_box, 1, extent)
        + spread(pgrad_ext, 1, extent)
    )


def finish(adjoint_pops, adjoint_phase):
    return jnp.concatenate([adjoint_pops[:19], adjoint_pops[19:] + adjoint_phase[None]], 0)


def local(populations0, populations1, cotangent):
    states = [populations1.astype(jnp.float32), populations0.astype(jnp.float32)]
    fractions = jnp.stack([jnp.sum(state[19:], 0) for state in states])
    extent = fractions.shape[1:]
    fraction_pieces, cotangent_pieces = exchange(
        [(fractions, 2, True, all_fields(2)), (cotangent, 1, True, streamed_fields)]
    )
    fraction_ext = wall_zero(assemble(fractions, fraction_pieces, 2), 2, 1)
    fields1 = phase_fields(fraction_ext[0], extent)
    fields0 = phase_fields(fraction_ext[1], extent)

    arrived = stream_adjoint(cotangent, cotangent_pieces)
    pops, pgrad_adj, mgrad_adj = collide_adjoint(states[0], *fields1, arrived)
    adjoint1 = finish(pops, phase_adjoint(fractions[0], pgrad_adj, mgrad_adj, extent))

    adjoint1_pieces, = exchange([(adjoint1, 1, True, streamed_fields)])
    arrived = stream_adjoint(adjoint1, adjoint1_pieces)
    pops, pgrad_adj, mgrad_adj = collide_adjoint(states[1], *fields0, arrived)
    return finish(pops, phase_adjoint(fractions[1], pgrad_adj, mgrad_adj, extent))


def solution(mesh):
    return jax.shard_map(
        local,
        mesh=mesh,
        in_specs=(P(None, "gz", "gx", "gy"), P(None, "gz", "gx", "gy"), P(None, "gz", "gx", "gy")),
        out_specs=P(None, "gz", "gx", "gy"),
        check_vma=False,
    )
```

```python
import jax
import jax.numpy as jnp
import numpy as np
from jax import lax
from jax.sharding import PartitionSpec as P

VELOCITY = np.array(
    [
        [0, 0, 0],
        [1, 0, 0],
        [-1, 0, 0],
        [0, 1, 0],
        [0, -1, 0],
        [0, 0, 1],
        [0, 0, -1],
        [1, 1, 0],
        [-1, -1, 0],
        [1, -1, 0],
        [-1, 1, 0],
        [1, 0, 1],
        [-1, 0, -1],
        [1, 0, -1],
        [-1, 0, 1],
        [0, 1, 1],
        [0, -1, -1],
        [0, 1, -1],
        [0, -1, 1],
    ]
)
OPPOSITE = [0, 2, 1, 4, 3, 6, 5, 8, 7, 10, 9, 12, 11, 14, 13, 16, 15, 18, 17]
FLOW_WEIGHT = [1.0 / 3.0] + [1.0 / 18.0] * 6 + [1.0 / 36.0] * 12
PHASE_WEIGHT = [0.25] + [0.125] * 6
VELOCITY_ALL = np.concatenate([VELOCITY, VELOCITY[:7]], 0)
OPPOSITE_ALL = OPPOSITE + [19 + mirror for mirror in OPPOSITE[:7]]
WELL_DEPTH = 0.3
STIFFNESS = 0.6
SHARPEN = 0.3
PHASE_RATE = 1.4
UNITS = ((1, 0, 0), (0, 1, 0), (0, 0, 1))
CENTER = (0, 0, 0)


def expand(weights, rank):
    values = [float(entry) for entry in list(weights)]
    return jnp.asarray(values, jnp.float32).reshape((-1,) + (1,) * rank)


def along(velocity_table, vector):
    rank = vector.ndim - 1
    total = expand(velocity_table[:, 0], rank) * vector[0]
    for direction in range(1, 3):
        total = total + expand(velocity_table[:, direction], rank) * vector[direction]
    return total


def collide(populations, phase_grad, potential_grad):
    rank = populations.ndim - 1
    flow_part = populations[:19]
    phase_part = populations[19:]
    fraction = jnp.sum(phase_part, 0)
    density = 0.2 + 0.8 * fraction
    pressure = jnp.sum(flow_part, 0)
    body_force = -fraction[None] * potential_grad
    momentum = jnp.stack(
        [jnp.sum(expand(VELOCITY[:, direction], rank) * flow_part, 0) for direction in range(3)]
    )
    velocity = (momentum + 0.5 * body_force) / density[None]
    along_flow = along(VELOCITY, velocity)
    speed_square = jnp.sum(velocity * velocity, 0)
    relax_rate = 1.1 + 0.5 * fraction
    flow_equil = expand(FLOW_WEIGHT, rank) * (
        pressure + density * (3.0 * along_flow + 4.5 * along_flow * along_flow - 1.5 * speed_square)
    )
    along_force = along(VELOCITY, body_force)
    speed_force = jnp.sum(velocity * body_force, 0)
    source = expand(FLOW_WEIGHT, rank) * (
        3.0 * (along_force - speed_force) + 9.0 * along_flow * along_force
    )
    flow_post = (
        flow_part - relax_rate * (flow_part - flow_equil) + (1.0 - 0.5 * relax_rate) * source
    )
    magnitude = jnp.sqrt(jnp.sum(phase_grad * phase_grad, 0) + 0.0625)
    normal = phase_grad / magnitude
    along_normal = along(VELOCITY[:7], normal)
    phase_equil = expand(PHASE_WEIGHT, rank) * (
        fraction * (1.0 + 4.0 * along_flow[:7])
        + 4.0 * SHARPEN * fraction * (1.0 - fraction) * along_normal
    )
    phase_post = phase_part - PHASE_RATE * (phase_part - phase_equil)
    return jnp.concatenate([flow_post, phase_post], 0)


def wall_zero(extended, width, vertical_dim):
    height = extended.shape[vertical_dim]
    layer_index = lax.broadcasted_iota(jnp.int32, (height,), 0)
    position = lax.axis_index("gz")
    bricks = lax.axis_size("gz")
    bottom_wall = jnp.logical_and(layer_index < width, position == 0)
    top_wall = jnp.logical_and(layer_index >= height - width, position == bricks - 1)
    inside = jnp.where(jnp.logical_or(bottom_wall, top_wall), 0.0, 1.0).astype(extended.dtype)
    extent = [1] * extended.ndim
    extent[vertical_dim] = height
    return extended * inside.reshape(extent)


def offset_view(extended, margin, offset, extent):
    return extended[
        ...,
        margin + offset[0] : margin + offset[0] + extent[0],
        margin + offset[1] : margin + offset[1] + extent[1],
        margin + offset[2] : margin + offset[2] + extent[2],
    ]


def negate(offset):
    return tuple((-entry for entry in offset))


def gradient(extended, margin, extent):
    return jnp.stack(
        [
            (
                offset_view(extended, margin, unit, extent)
                - offset_view(extended, margin, negate(unit), extent)
            )
            * 0.5
            for unit in UNITS
        ]
    )


def laplace(extended, margin, extent):
    total = -6.0 * offset_view(extended, margin, CENTER, extent)
    for unit in UNITS:
        total = (
            total
            + offset_view(extended, margin, unit, extent)
            + offset_view(extended, margin, negate(unit), extent)
        )
    return total


def spread(extended, margin, extent):
    total = jnp.zeros(extent, jnp.float32)
    for direction in range(3):
        unit = UNITS[direction]
        total = (
            total
            + (
                offset_view(extended[direction], margin, negate(unit), extent)
                - offset_view(extended[direction], margin, unit, extent)
            )
            * 0.5
        )
    return total


def well_term(fraction):
    return 4.0 * WELL_DEPTH * fraction * (fraction - 1.0) * (fraction - 0.5)


def well_slope(fraction):
    return 4.0 * WELL_DEPTH * (3.0 * fraction * fraction - 3.0 * fraction + 0.5)


def bounce(arrived, adjoint):
    height = adjoint.shape[1]
    layer_index = lax.broadcasted_iota(jnp.int32, (height,), 0)
    position = lax.axis_index("gz")
    bricks = lax.axis_size("gz")
    bottom_wall = jnp.logical_and(layer_index == 0, position == 0).reshape((1, height, 1, 1))
    top_wall = jnp.logical_and(layer_index == height - 1, position == bricks - 1).reshape(
        (1, height, 1, 1)
    )
    rising = jnp.asarray((VELOCITY_ALL[:, 0] == 1).reshape((26, 1, 1, 1)))
    falling = jnp.asarray((VELOCITY_ALL[:, 0] == -1).reshape((26, 1, 1, 1)))
    reflect = jnp.logical_or(
        jnp.logical_and(rising, top_wall), jnp.logical_and(falling, bottom_wall)
    )
    flipped = jnp.stack([adjoint[mirror] for mirror in OPPOSITE_ALL])
    return jnp.where(reflect, flipped, arrived)


def extended_2(shard, sides, width):
    for axis, dim in sides:
        count, length = (lax.axis_size(axis), shard.shape[dim])
        last = lax.slice_in_dim(shard, length - width, length, axis=dim)
        first = lax.slice_in_dim(shard, 0, width, axis=dim)
        if axis == "gz" and count == 2:
            lower = lax.axis_index(axis) == 0
            swapped = lax.ppermute(jnp.where(lower, last, first), axis, [(0, 1), (1, 0)])
            before, after = swapped, swapped
        else:
            up = [(i, (i + 1) % count) for i in range(count)]
            down = [(j, i) for i, j in up]
            before = lax.ppermute(last, axis, up)
            after = lax.ppermute(first, axis, down)
        shard = jnp.concatenate([before, shard, after], axis=dim)
    return shard


SIDES = (("gx", 2), ("gy", 3), ("gz", 1))


def stream_adjoint(extended, margin, adjoint, extent):
    arrived = jnp.stack(
        [
            offset_view(
                extended[member],
                margin,
                tuple((int(entry) for entry in VELOCITY_ALL[member])),
                extent,
            )
            for member in range(26)
        ]
    )
    return bounce(arrived, adjoint)


def phase_fields(fraction_ext, extent):
    box = tuple(n + 2 for n in extent)
    inner = fraction_ext[1:-1, 1:-1, 1:-1]
    potential_box = wall_zero(well_term(inner) - STIFFNESS * laplace(fraction_ext, 1, box), 1, 0)
    return gradient(fraction_ext, 2, extent), gradient(potential_box, 1, extent)


def collide_adjoint(populations, phase_grad, potential_grad, arrived):
    pullback = jax.vjp(collide, populations, phase_grad, potential_grad)[1]
    return pullback(arrived)


def phase_adjoint(fraction, adjoint_pgrad, adjoint_mgrad, extent):
    combined = jnp.concatenate([adjoint_pgrad, adjoint_mgrad], 0)
    combined_ext = wall_zero(extended_2(combined, SIDES, 2), 2, 1)
    box = tuple(n + 2 for n in extent)
    mu_box = wall_zero(spread(combined_ext[3:], 1, box), 1, 0)
    return (
        well_slope(fraction) * mu_box[1:-1, 1:-1, 1:-1]
        - STIFFNESS * laplace(mu_box, 1, extent)
        + spread(combined_ext[:3], 2, extent)
    )


def finish(adjoint_pops, adjoint_phase):
    return jnp.concatenate([adjoint_pops[:19], adjoint_pops[19:] + adjoint_phase[None]], 0)


def local(populations0, populations1, cotangent):
    states = [populations1.astype(jnp.float32), populations0.astype(jnp.float32)]
    fractions = jnp.stack([jnp.sum(state[19:], 0) for state in states])
    extent = fractions.shape[1:]
    first_ext = extended_2(jnp.concatenate([fractions, cotangent], 0), SIDES, 2)
    fraction_ext = wall_zero(first_ext[:2], 2, 1)
    fields1 = phase_fields(fraction_ext[0], extent)
    fields0 = phase_fields(fraction_ext[1], extent)

    arrived = stream_adjoint(first_ext[2:], 2, cotangent, extent)
    pops, pgrad_adj, mgrad_adj = collide_adjoint(states[0], *fields1, arrived)
    adjoint1 = finish(pops, phase_adjoint(fractions[0], pgrad_adj, mgrad_adj, extent))

    arrived = stream_adjoint(extended_2(adjoint1, SIDES, 1), 1, adjoint1, extent)
    pops, pgrad_adj, mgrad_adj = collide_adjoint(states[1], *fields0, arrived)
    return finish(pops, phase_adjoint(fractions[1], pgrad_adj, mgrad_adj, extent))


def solution(mesh):
    return jax.shard_map(
        local,
        mesh=mesh,
        in_specs=(P(None, "gz", "gx", "gy"), P(None, "gz", "gx", "gy"), P(None, "gz", "gx", "gy")),
        out_specs=P(None, "gz", "gx", "gy"),
        check_vma=False,
    )
```

```python
import jax
import jax.numpy as jnp
import numpy as np
from jax import lax
from jax.sharding import PartitionSpec as P

VELOCITY = np.array(
    [
        [0, 0, 0],
        [1, 0, 0],
        [-1, 0, 0],
        [0, 1, 0],
        [0, -1, 0],
        [0, 0, 1],
        [0, 0, -1],
        [1, 1, 0],
        [-1, -1, 0],
        [1, -1, 0],
        [-1, 1, 0],
        [1, 0, 1],
        [-1, 0, -1],
        [1, 0, -1],
        [-1, 0, 1],
        [0, 1, 1],
        [0, -1, -1],
        [0, 1, -1],
        [0, -1, 1],
    ]
)
OPPOSITE = [0, 2, 1, 4, 3, 6, 5, 8, 7, 10, 9, 12, 11, 14, 13, 16, 15, 18, 17]
FLOW_WEIGHT = [1.0 / 3.0] + [1.0 / 18.0] * 6 + [1.0 / 36.0] * 12
PHASE_WEIGHT = [0.25] + [0.125] * 6
VELOCITY_ALL = np.concatenate([VELOCITY, VELOCITY[:7]], 0)
OPPOSITE_ALL = OPPOSITE + [19 + mirror for mirror in OPPOSITE[:7]]
WELL_DEPTH = 0.3
STIFFNESS = 0.6
SHARPEN = 0.3
PHASE_RATE = 1.4
UNITS = ((1, 0, 0), (0, 1, 0), (0, 0, 1))
CENTER = (0, 0, 0)


def expand(weights, rank):
    values = [float(entry) for entry in list(weights)]
    return jnp.asarray(values, jnp.float32).reshape((-1,) + (1,) * rank)


def along(velocity_table, vector):
    rank = vector.ndim - 1
    total = expand(velocity_table[:, 0], rank) * vector[0]
    for direction in range(1, 3):
        total = total + expand(velocity_table[:, direction], rank) * vector[direction]
    return total


def collide(populations, phase_grad, potential_grad):
    rank = populations.ndim - 1
    flow_part = populations[:19]
    phase_part = populations[19:]
    fraction = jnp.sum(phase_part, 0)
    density = 0.2 + 0.8 * fraction
    pressure = jnp.sum(flow_part, 0)
    body_force = -fraction[None] * potential_grad
    momentum = jnp.stack(
        [jnp.sum(expand(VELOCITY[:, direction], rank) * flow_part, 0) for direction in range(3)]
    )
    velocity = (momentum + 0.5 * body_force) / density[None]
    along_flow = along(VELOCITY, velocity)
    speed_square = jnp.sum(velocity * velocity, 0)
    relax_rate = 1.1 + 0.5 * fraction
    flow_equil = expand(FLOW_WEIGHT, rank) * (
        pressure + density * (3.0 * along_flow + 4.5 * along_flow * along_flow - 1.5 * speed_square)
    )
    along_force = along(VELOCITY, body_force)
    speed_force = jnp.sum(velocity * body_force, 0)
    source = expand(FLOW_WEIGHT, rank) * (
        3.0 * (along_force - speed_force) + 9.0 * along_flow * along_force
    )
    flow_post = (
        flow_part - relax_rate * (flow_part - flow_equil) + (1.0 - 0.5 * relax_rate) * source
    )
    magnitude = jnp.sqrt(jnp.sum(phase_grad * phase_grad, 0) + 0.0625)
    normal = phase_grad / magnitude
    along_normal = along(VELOCITY[:7], normal)
    phase_equil = expand(PHASE_WEIGHT, rank) * (
        fraction * (1.0 + 4.0 * along_flow[:7])
        + 4.0 * SHARPEN * fraction * (1.0 - fraction) * along_normal
    )
    phase_post = phase_part - PHASE_RATE * (phase_part - phase_equil)
    return jnp.concatenate([flow_post, phase_post], 0)


def wall_zero(extended, width, vertical_dim):
    height = extended.shape[vertical_dim]
    layer_index = lax.broadcasted_iota(jnp.int32, (height,), 0)
    position = lax.axis_index("gz")
    bricks = lax.axis_size("gz")
    bottom_wall = jnp.logical_and(layer_index < width, position == 0)
    top_wall = jnp.logical_and(layer_index >= height - width, position == bricks - 1)
    inside = jnp.where(jnp.logical_or(bottom_wall, top_wall), 0.0, 1.0).astype(extended.dtype)
    extent = [1] * extended.ndim
    extent[vertical_dim] = height
    return extended * inside.reshape(extent)


def offset_view(extended, margin, offset, extent):
    return extended[
        ...,
        margin + offset[0] : margin + offset[0] + extent[0],
        margin + offset[1] : margin + offset[1] + extent[1],
        margin + offset[2] : margin + offset[2] + extent[2],
    ]


def negate(offset):
    return tuple((-entry for entry in offset))


def gradient(extended, margin, extent):
    return jnp.stack(
        [
            (
                offset_view(extended, margin, unit, extent)
                - offset_view(extended, margin, negate(unit), extent)
            )
            * 0.5
            for unit in UNITS
        ]
    )


def laplace(extended, margin, extent):
    total = -6.0 * offset_view(extended, margin, CENTER, extent)
    for unit in UNITS:
        total = (
            total
            + offset_view(extended, margin, unit, extent)
            + offset_view(extended, margin, negate(unit), extent)
        )
    return total


def spread(extended, margin, extent):
    total = jnp.zeros(extent, jnp.float32)
    for direction in range(3):
        unit = UNITS[direction]
        total = (
            total
            + (
                offset_view(extended[direction], margin, negate(unit), extent)
                - offset_view(extended[direction], margin, unit, extent)
            )
            * 0.5
        )
    return total


def well_term(fraction):
    return 4.0 * WELL_DEPTH * fraction * (fraction - 1.0) * (fraction - 0.5)


def well_slope(fraction):
    return 4.0 * WELL_DEPTH * (3.0 * fraction * fraction - 3.0 * fraction + 0.5)


def bounce(arrived, adjoint):
    height = adjoint.shape[1]
    layer_index = lax.broadcasted_iota(jnp.int32, (height,), 0)
    position = lax.axis_index("gz")
    bricks = lax.axis_size("gz")
    bottom_wall = jnp.logical_and(layer_index == 0, position == 0).reshape((1, height, 1, 1))
    top_wall = jnp.logical_and(layer_index == height - 1, position == bricks - 1).reshape(
        (1, height, 1, 1)
    )
    rising = jnp.asarray((VELOCITY_ALL[:, 0] == 1).reshape((26, 1, 1, 1)))
    falling = jnp.asarray((VELOCITY_ALL[:, 0] == -1).reshape((26, 1, 1, 1)))
    reflect = jnp.logical_or(
        jnp.logical_and(rising, top_wall), jnp.logical_and(falling, bottom_wall)
    )
    flipped = jnp.stack([adjoint[mirror] for mirror in OPPOSITE_ALL])
    return jnp.where(reflect, flipped, arrived)


def extended_2(shard, sides, width):
    for axis, dim in sides:
        count, length = (lax.axis_size(axis), shard.shape[dim])
        last = lax.slice_in_dim(shard, length - width, length, axis=dim)
        first = lax.slice_in_dim(shard, 0, width, axis=dim)
        if axis == "gz" and count == 2:
            lower = lax.axis_index(axis) == 0
            swapped = lax.ppermute(jnp.where(lower, last, first), axis, [(0, 1), (1, 0)])
            before, after = swapped, swapped
        else:
            up = [(i, (i + 1) % count) for i in range(count)]
            down = [(j, i) for i, j in up]
            before = lax.ppermute(last, axis, up)
            after = lax.ppermute(first, axis, down)
        shard = jnp.concatenate([before, shard, after], axis=dim)
    return shard


SIDES = (("gx", 2), ("gy", 3), ("gz", 1))


def stream_adjoint(extended, margin, adjoint, extent):
    arrived = jnp.stack(
        [
            offset_view(
                extended[member],
                margin,
                tuple((int(entry) for entry in VELOCITY_ALL[member])),
                extent,
            )
            for member in range(26)
        ]
    )
    return bounce(arrived, adjoint)


def phase_fields(fraction_ext, extent):
    box = tuple(n + 2 for n in extent)
    inner = fraction_ext[1:-1, 1:-1, 1:-1]
    potential_box = wall_zero(well_term(inner) - STIFFNESS * laplace(fraction_ext, 1, box), 1, 0)
    return gradient(fraction_ext, 2, extent), gradient(potential_box, 1, extent)


def collide_adjoint(populations, phase_grad, potential_grad, arrived):
    pullback = jax.vjp(collide, populations, phase_grad, potential_grad)[1]
    return pullback(arrived)


def phase_adjoint(fraction, adjoint_pgrad, adjoint_mgrad, extra, extent):
    combined = jnp.concatenate([adjoint_pgrad, adjoint_mgrad, extra], 0)
    extended = extended_2(combined, SIDES, 2)
    combined_ext = wall_zero(extended[:6], 2, 1)
    box = tuple(n + 2 for n in extent)
    mu_box = wall_zero(spread(combined_ext[3:6], 1, box), 1, 0)
    adjoint_phase = (
        well_slope(fraction) * mu_box[1:-1, 1:-1, 1:-1]
        - STIFFNESS * laplace(mu_box, 1, extent)
        + spread(combined_ext[:3], 2, extent)
    )
    return adjoint_phase, extended[6:]


def face_shifts(values):
    shifted = {}
    for axis, dim in SIDES:
        count, length = (lax.axis_size(axis), values.shape[dim - 1])
        last = lax.slice_in_dim(values, length - 1, length, axis=dim - 1)
        first = lax.slice_in_dim(values, 0, 1, axis=dim - 1)
        if axis == "gz" and count == 2:
            lower = lax.axis_index(axis) == 0
            swapped = lax.ppermute(jnp.where(lower, last, first), axis, [(0, 1), (1, 0)])
            before, after = swapped, swapped
        else:
            up = [(i, (i + 1) % count) for i in range(count)]
            down = [(j, i) for i, j in up]
            before = lax.ppermute(last, axis, up)
            after = lax.ppermute(first, axis, down)
        plus = tuple(1 if a == dim - 1 else 0 for a in range(3))
        shifted[plus] = shift_along(values, after, dim - 1, 1)
        shifted[negate(plus)] = shift_along(values, before, dim - 1, -1)
    return shifted


def shift_along(values, halo, axis, sign):
    length = values.shape[axis]
    if sign == 1:
        return jnp.concatenate([lax.slice_in_dim(values, 1, length, axis=axis), halo], axis)
    return jnp.concatenate([halo, lax.slice_in_dim(values, 0, length - 1, axis=axis)], axis)


def finish(adjoint_pops, adjoint_phase):
    return jnp.concatenate([adjoint_pops[:19], adjoint_pops[19:] + adjoint_phase[None]], 0)


def local(populations0, populations1, cotangent):
    states = [populations1.astype(jnp.float32), populations0.astype(jnp.float32)]
    fractions = jnp.stack([jnp.sum(state[19:], 0) for state in states])
    extent = fractions.shape[1:]
    first_ext = extended_2(jnp.concatenate([fractions, cotangent], 0), SIDES, 2)
    fraction_ext = wall_zero(first_ext[:2], 2, 1)
    fields1 = phase_fields(fraction_ext[0], extent)
    fields0 = phase_fields(fraction_ext[1], extent)

    arrived = stream_adjoint(first_ext[2:], 2, cotangent, extent)
    pops, pgrad_adj, mgrad_adj = collide_adjoint(states[0], *fields1, arrived)
    adjoint_phase, pops_ext = phase_adjoint(fractions[0], pgrad_adj, mgrad_adj, pops, extent)
    adjoint1 = finish(pops, adjoint_phase)

    phase_shifted = face_shifts(adjoint_phase)
    arrived = []
    for member in range(26):
        velocity = tuple(int(entry) for entry in VELOCITY_ALL[member])
        values = offset_view(pops_ext[member], 2, velocity, extent)
        if member >= 19:
            values = values + (adjoint_phase if member == 19 else phase_shifted[velocity])
        arrived.append(values)
    arrived = bounce(jnp.stack(arrived), adjoint1)
    pops, pgrad_adj, mgrad_adj = collide_adjoint(states[1], *fields0, arrived)
    adjoint_phase, _ = phase_adjoint(fractions[1], pgrad_adj, mgrad_adj, pops[:0], extent)
    return finish(pops, adjoint_phase)


def solution(mesh):
    return jax.shard_map(
        local,
        mesh=mesh,
        in_specs=(P(None, "gz", "gx", "gy"), P(None, "gz", "gx", "gy"), P(None, "gz", "gx", "gy")),
        out_specs=P(None, "gz", "gx", "gy"),
        check_vma=False,
    )
```

```python
import jax
import jax.numpy as jnp
import numpy as np
from jax import lax
from jax.sharding import PartitionSpec as P

VELOCITY = np.array(
    [
        [0, 0, 0],
        [1, 0, 0],
        [-1, 0, 0],
        [0, 1, 0],
        [0, -1, 0],
        [0, 0, 1],
        [0, 0, -1],
        [1, 1, 0],
        [-1, -1, 0],
        [1, -1, 0],
        [-1, 1, 0],
        [1, 0, 1],
        [-1, 0, -1],
        [1, 0, -1],
        [-1, 0, 1],
        [0, 1, 1],
        [0, -1, -1],
        [0, 1, -1],
        [0, -1, 1],
    ]
)
OPPOSITE = [0, 2, 1, 4, 3, 6, 5, 8, 7, 10, 9, 12, 11, 14, 13, 16, 15, 18, 17]
FLOW_WEIGHT = [1.0 / 3.0] + [1.0 / 18.0] * 6 + [1.0 / 36.0] * 12
PHASE_WEIGHT = [0.25] + [0.125] * 6
VELOCITY_ALL = np.concatenate([VELOCITY, VELOCITY[:7]], 0)
OPPOSITE_ALL = OPPOSITE + [19 + mirror for mirror in OPPOSITE[:7]]
WELL_DEPTH = 0.3
STIFFNESS = 0.6
SHARPEN = 0.3
PHASE_RATE = 1.4
UNITS = ((1, 0, 0), (0, 1, 0), (0, 0, 1))
CENTER = (0, 0, 0)


def expand(weights, rank):
    values = [float(entry) for entry in list(weights)]
    return jnp.asarray(values, jnp.float32).reshape((-1,) + (1,) * rank)


def along(velocity_table, vector):
    rank = vector.ndim - 1
    total = expand(velocity_table[:, 0], rank) * vector[0]
    for direction in range(1, 3):
        total = total + expand(velocity_table[:, direction], rank) * vector[direction]
    return total


def collide(populations, phase_grad, potential_grad):
    rank = populations.ndim - 1
    flow_part = populations[:19]
    phase_part = populations[19:]
    fraction = jnp.sum(phase_part, 0)
    density = 0.2 + 0.8 * fraction
    pressure = jnp.sum(flow_part, 0)
    body_force = -fraction[None] * potential_grad
    momentum = jnp.stack(
        [jnp.sum(expand(VELOCITY[:, direction], rank) * flow_part, 0) for direction in range(3)]
    )
    velocity = (momentum + 0.5 * body_force) / density[None]
    along_flow = along(VELOCITY, velocity)
    speed_square = jnp.sum(velocity * velocity, 0)
    relax_rate = 1.1 + 0.5 * fraction
    flow_equil = expand(FLOW_WEIGHT, rank) * (
        pressure + density * (3.0 * along_flow + 4.5 * along_flow * along_flow - 1.5 * speed_square)
    )
    along_force = along(VELOCITY, body_force)
    speed_force = jnp.sum(velocity * body_force, 0)
    source = expand(FLOW_WEIGHT, rank) * (
        3.0 * (along_force - speed_force) + 9.0 * along_flow * along_force
    )
    flow_post = (
        flow_part - relax_rate * (flow_part - flow_equil) + (1.0 - 0.5 * relax_rate) * source
    )
    magnitude = jnp.sqrt(jnp.sum(phase_grad * phase_grad, 0) + 0.0625)
    normal = phase_grad / magnitude
    along_normal = along(VELOCITY[:7], normal)
    phase_equil = expand(PHASE_WEIGHT, rank) * (
        fraction * (1.0 + 4.0 * along_flow[:7])
        + 4.0 * SHARPEN * fraction * (1.0 - fraction) * along_normal
    )
    phase_post = phase_part - PHASE_RATE * (phase_part - phase_equil)
    return jnp.concatenate([flow_post, phase_post], 0)


def wall_zero(extended, width, vertical_dim):
    height = extended.shape[vertical_dim]
    layer_index = lax.broadcasted_iota(jnp.int32, (height,), 0)
    position = lax.axis_index("gz")
    bricks = lax.axis_size("gz")
    bottom_wall = jnp.logical_and(layer_index < width, position == 0)
    top_wall = jnp.logical_and(layer_index >= height - width, position == bricks - 1)
    inside = jnp.where(jnp.logical_or(bottom_wall, top_wall), 0.0, 1.0).astype(extended.dtype)
    extent = [1] * extended.ndim
    extent[vertical_dim] = height
    return extended * inside.reshape(extent)


def offset_view(extended, margin, offset, extent):
    return extended[
        ...,
        margin + offset[0] : margin + offset[0] + extent[0],
        margin + offset[1] : margin + offset[1] + extent[1],
        margin + offset[2] : margin + offset[2] + extent[2],
    ]


def negate(offset):
    return tuple((-entry for entry in offset))


def gradient(extended, margin, extent):
    return jnp.stack(
        [
            (
                offset_view(extended, margin, unit, extent)
                - offset_view(extended, margin, negate(unit), extent)
            )
            * 0.5
            for unit in UNITS
        ]
    )


def laplace(extended, margin, extent):
    total = -6.0 * offset_view(extended, margin, CENTER, extent)
    for unit in UNITS:
        total = (
            total
            + offset_view(extended, margin, unit, extent)
            + offset_view(extended, margin, negate(unit), extent)
        )
    return total


def spread(extended, margin, extent):
    total = jnp.zeros(extent, jnp.float32)
    for direction in range(3):
        unit = UNITS[direction]
        total = (
            total
            + (
                offset_view(extended[direction], margin, negate(unit), extent)
                - offset_view(extended[direction], margin, unit, extent)
            )
            * 0.5
        )
    return total


def well_term(fraction):
    return 4.0 * WELL_DEPTH * fraction * (fraction - 1.0) * (fraction - 0.5)


def well_slope(fraction):
    return 4.0 * WELL_DEPTH * (3.0 * fraction * fraction - 3.0 * fraction + 0.5)


def bounce(arrived, adjoint):
    height = adjoint.shape[1]
    layer_index = lax.broadcasted_iota(jnp.int32, (height,), 0)
    position = lax.axis_index("gz")
    bricks = lax.axis_size("gz")
    bottom_wall = jnp.logical_and(layer_index == 0, position == 0).reshape((1, height, 1, 1))
    top_wall = jnp.logical_and(layer_index == height - 1, position == bricks - 1).reshape(
        (1, height, 1, 1)
    )
    rising = jnp.asarray((VELOCITY_ALL[:, 0] == 1).reshape((26, 1, 1, 1)))
    falling = jnp.asarray((VELOCITY_ALL[:, 0] == -1).reshape((26, 1, 1, 1)))
    reflect = jnp.logical_or(
        jnp.logical_and(rising, top_wall), jnp.logical_and(falling, bottom_wall)
    )
    flipped = jnp.stack([adjoint[mirror] for mirror in OPPOSITE_ALL])
    return jnp.where(reflect, flipped, arrived)


def neighbour_data(piece, axes, shift):
    sizes = [lax.axis_size(axis) for axis in axes]
    pairs = []
    for flat in range(int(np.prod(sizes))):
        index = np.unravel_index(flat, sizes)
        target = [(i - s) % n for i, s, n in zip(index, shift, sizes)]
        pairs.append((flat, int(np.ravel_multi_index(target, sizes))))
    return lax.ppermute(piece, axes if len(axes) > 1 else axes[0], pairs)


def side_slice(values, dim, side, width):
    length = values.shape[dim]
    if side == 1:
        return lax.slice_in_dim(values, 0, width, axis=dim)
    return lax.slice_in_dim(values, length - width, length, axis=dim)


def vertical_halos(values, width, dim):
    count = lax.axis_size("gz")
    last = side_slice(values, dim, -1, width)
    first = side_slice(values, dim, 1, width)
    if count == 2:
        lower = lax.axis_index("gz") == 0
        swapped = neighbour_data(jnp.where(lower, last, first), ("gz",), (1,))
        return swapped, swapped
    return neighbour_data(last, ("gz",), (-1,)), neighbour_data(first, ("gz",), (1,))


def extended_2(shard, sides, width):
    del sides
    xdim, ydim, zdim = 2, 3, 1
    face = {}
    for axis, dim in (("gx", xdim), ("gy", ydim)):
        for side in (1, -1):
            face[axis, side] = neighbour_data(side_slice(shard, dim, side, width), (axis,), (side,))
    corner = {}
    for sx in (1, -1):
        for sy in (1, -1):
            piece = side_slice(side_slice(shard, xdim, sx, width), ydim, sy, width)
            corner[sx, sy] = neighbour_data(piece, ("gx", "gy"), (sx, sy))
    rows = [
        jnp.concatenate([corner[-1, -1], face["gx", -1], corner[-1, 1]], ydim),
        jnp.concatenate([face["gy", -1], shard, face["gy", 1]], ydim),
        jnp.concatenate([corner[1, -1], face["gx", 1], corner[1, 1]], ydim),
    ]
    block = jnp.concatenate(rows, xdim)
    before, after = vertical_halos(block, width, zdim)
    return jnp.concatenate([before, block, after], zdim)


SIDES = (("gx", 2), ("gy", 3), ("gz", 1))


def stream_adjoint(extended, margin, adjoint, extent):
    arrived = jnp.stack(
        [
            offset_view(
                extended[member],
                margin,
                tuple((int(entry) for entry in VELOCITY_ALL[member])),
                extent,
            )
            for member in range(26)
        ]
    )
    return bounce(arrived, adjoint)


def phase_fields(fraction_ext, extent):
    box = tuple(n + 2 for n in extent)
    inner = fraction_ext[1:-1, 1:-1, 1:-1]
    potential_box = wall_zero(well_term(inner) - STIFFNESS * laplace(fraction_ext, 1, box), 1, 0)
    return gradient(fraction_ext, 2, extent), gradient(potential_box, 1, extent)


def collide_adjoint(populations, phase_grad, potential_grad, arrived):
    pullback = jax.vjp(collide, populations, phase_grad, potential_grad)[1]
    return pullback(arrived)


def phase_adjoint(fraction, adjoint_pgrad, adjoint_mgrad, extra, extent):
    combined = jnp.concatenate([adjoint_pgrad, adjoint_mgrad, extra], 0)
    extended = extended_2(combined, SIDES, 2)
    combined_ext = wall_zero(extended[:6], 2, 1)
    box = tuple(n + 2 for n in extent)
    mu_box = wall_zero(spread(combined_ext[3:6], 1, box), 1, 0)
    adjoint_phase = (
        well_slope(fraction) * mu_box[1:-1, 1:-1, 1:-1]
        - STIFFNESS * laplace(mu_box, 1, extent)
        + spread(combined_ext[:3], 2, extent)
    )
    return adjoint_phase, extended[6:]


def face_shifts(values):
    shifted = {}
    for axis, dim in SIDES:
        d = dim - 1
        if axis == "gz":
            before, after = vertical_halos(values, 1, d)
        else:
            after = neighbour_data(side_slice(values, d, 1, 1), (axis,), (1,))
            before = neighbour_data(side_slice(values, d, -1, 1), (axis,), (-1,))
        plus = tuple(1 if a == d else 0 for a in range(3))
        shifted[plus] = shift_along(values, after, d, 1)
        shifted[negate(plus)] = shift_along(values, before, d, -1)
    return shifted


def shift_along(values, halo, axis, sign):
    length = values.shape[axis]
    if sign == 1:
        return jnp.concatenate([lax.slice_in_dim(values, 1, length, axis=axis), halo], axis)
    return jnp.concatenate([halo, lax.slice_in_dim(values, 0, length - 1, axis=axis)], axis)


def finish(adjoint_pops, adjoint_phase):
    return jnp.concatenate([adjoint_pops[:19], adjoint_pops[19:] + adjoint_phase[None]], 0)


def local(populations0, populations1, cotangent):
    states = [populations1.astype(jnp.float32), populations0.astype(jnp.float32)]
    fractions = jnp.stack([jnp.sum(state[19:], 0) for state in states])
    extent = fractions.shape[1:]
    first_ext = extended_2(jnp.concatenate([fractions, cotangent], 0), SIDES, 2)
    fraction_ext = wall_zero(first_ext[:2], 2, 1)
    fields1 = phase_fields(fraction_ext[0], extent)
    fields0 = phase_fields(fraction_ext[1], extent)

    arrived = stream_adjoint(first_ext[2:], 2, cotangent, extent)
    pops, pgrad_adj, mgrad_adj = collide_adjoint(states[0], *fields1, arrived)
    adjoint_phase, pops_ext = phase_adjoint(fractions[0], pgrad_adj, mgrad_adj, pops, extent)
    adjoint1 = finish(pops, adjoint_phase)

    phase_shifted = face_shifts(adjoint_phase)
    arrived = []
    for member in range(26):
        velocity = tuple(int(entry) for entry in VELOCITY_ALL[member])
        values = offset_view(pops_ext[member], 2, velocity, extent)
        if member >= 19:
            values = values + (adjoint_phase if member == 19 else phase_shifted[velocity])
        arrived.append(values)
    arrived = bounce(jnp.stack(arrived), adjoint1)
    pops, pgrad_adj, mgrad_adj = collide_adjoint(states[1], *fields0, arrived)
    adjoint_phase, _ = phase_adjoint(fractions[1], pgrad_adj, mgrad_adj, pops[:0], extent)
    return finish(pops, adjoint_phase)


def solution(mesh):
    return jax.shard_map(
        local,
        mesh=mesh,
        in_specs=(P(None, "gz", "gx", "gy"), P(None, "gz", "gx", "gy"), P(None, "gz", "gx", "gy")),
        out_specs=P(None, "gz", "gx", "gy"),
        check_vma=False,
    )
```

```python
import jax
import jax.numpy as jnp
import numpy as np
from jax import lax
from jax.sharding import PartitionSpec as P

VELOCITY = np.array(
    [
        [0, 0, 0],
        [1, 0, 0],
        [-1, 0, 0],
        [0, 1, 0],
        [0, -1, 0],
        [0, 0, 1],
        [0, 0, -1],
        [1, 1, 0],
        [-1, -1, 0],
        [1, -1, 0],
        [-1, 1, 0],
        [1, 0, 1],
        [-1, 0, -1],
        [1, 0, -1],
        [-1, 0, 1],
        [0, 1, 1],
        [0, -1, -1],
        [0, 1, -1],
        [0, -1, 1],
    ]
)
OPPOSITE = [0, 2, 1, 4, 3, 6, 5, 8, 7, 10, 9, 12, 11, 14, 13, 16, 15, 18, 17]
FLOW_WEIGHT = [1.0 / 3.0] + [1.0 / 18.0] * 6 + [1.0 / 36.0] * 12
PHASE_WEIGHT = [0.25] + [0.125] * 6
VELOCITY_ALL = np.concatenate([VELOCITY, VELOCITY[:7]], 0)
OPPOSITE_ALL = OPPOSITE + [19 + mirror for mirror in OPPOSITE[:7]]
WELL_DEPTH = 0.3
STIFFNESS = 0.6
SHARPEN = 0.3
PHASE_RATE = 1.4
UNITS = ((1, 0, 0), (0, 1, 0), (0, 0, 1))
CENTER = (0, 0, 0)


def expand(weights, rank):
    values = [float(entry) for entry in list(weights)]
    return jnp.asarray(values, jnp.float32).reshape((-1,) + (1,) * rank)


def along(velocity_table, vector):
    rank = vector.ndim - 1
    total = expand(velocity_table[:, 0], rank) * vector[0]
    for direction in range(1, 3):
        total = total + expand(velocity_table[:, direction], rank) * vector[direction]
    return total


def collide(populations, phase_grad, potential_grad):
    rank = populations.ndim - 1
    flow_part = populations[:19]
    phase_part = populations[19:]
    fraction = jnp.sum(phase_part, 0)
    density = 0.2 + 0.8 * fraction
    pressure = jnp.sum(flow_part, 0)
    body_force = -fraction[None] * potential_grad
    momentum = jnp.stack(
        [jnp.sum(expand(VELOCITY[:, direction], rank) * flow_part, 0) for direction in range(3)]
    )
    velocity = (momentum + 0.5 * body_force) / density[None]
    along_flow = along(VELOCITY, velocity)
    speed_square = jnp.sum(velocity * velocity, 0)
    relax_rate = 1.1 + 0.5 * fraction
    flow_equil = expand(FLOW_WEIGHT, rank) * (
        pressure + density * (3.0 * along_flow + 4.5 * along_flow * along_flow - 1.5 * speed_square)
    )
    along_force = along(VELOCITY, body_force)
    speed_force = jnp.sum(velocity * body_force, 0)
    source = expand(FLOW_WEIGHT, rank) * (
        3.0 * (along_force - speed_force) + 9.0 * along_flow * along_force
    )
    flow_post = (
        flow_part - relax_rate * (flow_part - flow_equil) + (1.0 - 0.5 * relax_rate) * source
    )
    magnitude = jnp.sqrt(jnp.sum(phase_grad * phase_grad, 0) + 0.0625)
    normal = phase_grad / magnitude
    along_normal = along(VELOCITY[:7], normal)
    phase_equil = expand(PHASE_WEIGHT, rank) * (
        fraction * (1.0 + 4.0 * along_flow[:7])
        + 4.0 * SHARPEN * fraction * (1.0 - fraction) * along_normal
    )
    phase_post = phase_part - PHASE_RATE * (phase_part - phase_equil)
    return jnp.concatenate([flow_post, phase_post], 0)


def wall_zero(extended, width, vertical_dim):
    height = extended.shape[vertical_dim]
    layer_index = lax.broadcasted_iota(jnp.int32, (height,), 0)
    position = lax.axis_index("gz")
    bricks = lax.axis_size("gz")
    bottom_wall = jnp.logical_and(layer_index < width, position == 0)
    top_wall = jnp.logical_and(layer_index >= height - width, position == bricks - 1)
    inside = jnp.where(jnp.logical_or(bottom_wall, top_wall), 0.0, 1.0).astype(extended.dtype)
    extent = [1] * extended.ndim
    extent[vertical_dim] = height
    return extended * inside.reshape(extent)


def offset_view(extended, margin, offset, extent):
    return extended[
        ...,
        margin + offset[0] : margin + offset[0] + extent[0],
        margin + offset[1] : margin + offset[1] + extent[1],
        margin + offset[2] : margin + offset[2] + extent[2],
    ]


def negate(offset):
    return tuple((-entry for entry in offset))


def gradient(extended, margin, extent):
    return jnp.stack(
        [
            (
                offset_view(extended, margin, unit, extent)
                - offset_view(extended, margin, negate(unit), extent)
            )
            * 0.5
            for unit in UNITS
        ]
    )


def laplace(extended, margin, extent):
    total = -6.0 * offset_view(extended, margin, CENTER, extent)
    for unit in UNITS:
        total = (
            total
            + offset_view(extended, margin, unit, extent)
            + offset_view(extended, margin, negate(unit), extent)
        )
    return total


def spread(extended, margin, extent):
    total = jnp.zeros(extent, jnp.float32)
    for direction in range(3):
        unit = UNITS[direction]
        total = (
            total
            + (
                offset_view(extended[direction], margin, negate(unit), extent)
                - offset_view(extended[direction], margin, unit, extent)
            )
            * 0.5
        )
    return total


def well_term(fraction):
    return 4.0 * WELL_DEPTH * fraction * (fraction - 1.0) * (fraction - 0.5)


def well_slope(fraction):
    return 4.0 * WELL_DEPTH * (3.0 * fraction * fraction - 3.0 * fraction + 0.5)


def bounce(arrived, adjoint):
    height = adjoint.shape[1]
    layer_index = lax.broadcasted_iota(jnp.int32, (height,), 0)
    position = lax.axis_index("gz")
    bricks = lax.axis_size("gz")
    bottom_wall = jnp.logical_and(layer_index == 0, position == 0).reshape((1, height, 1, 1))
    top_wall = jnp.logical_and(layer_index == height - 1, position == bricks - 1).reshape(
        (1, height, 1, 1)
    )
    rising = jnp.asarray((VELOCITY_ALL[:, 0] == 1).reshape((26, 1, 1, 1)))
    falling = jnp.asarray((VELOCITY_ALL[:, 0] == -1).reshape((26, 1, 1, 1)))
    reflect = jnp.logical_or(
        jnp.logical_and(rising, top_wall), jnp.logical_and(falling, bottom_wall)
    )
    flipped = jnp.stack([adjoint[mirror] for mirror in OPPOSITE_ALL])
    return jnp.where(reflect, flipped, arrived)


def crossing(count, lead, dim):
    def chosen(side):
        grid = dim - 1
        if side == 0:
            picked = [m for m in range(26) if VELOCITY_ALL[m][grid] != 0]
        else:
            picked = [m for m in range(26) if VELOCITY_ALL[m][grid] == side]
        return list(range(lead)) + [lead + m for m in picked if lead + m < count]

    return chosen


def pick(values, fields):
    return jnp.concatenate([values[k : k + 1] for k in fields], 0)


def spread_fields(piece, fields, count):
    parts = []
    for k in range(count):
        if k in fields:
            i = fields.index(k)
            parts.append(piece[i : i + 1])
        else:
            parts.append(jnp.zeros((1,) + piece.shape[1:], piece.dtype))
    return jnp.concatenate(parts, 0)


def extended_2(shard, sides, width, lead=None):
    count = shard.shape[0]
    for axis, dim in sides:
        size, length = (lax.axis_size(axis), shard.shape[dim])
        chosen = crossing(count, count if lead is None else lead, dim)
        last = lax.slice_in_dim(shard, length - width, length, axis=dim)
        first = lax.slice_in_dim(shard, 0, width, axis=dim)
        if axis == "gz" and size == 2:
            fields = chosen(0)
            lower = lax.axis_index(axis) == 0
            swapped = lax.ppermute(
                jnp.where(lower, pick(last, fields), pick(first, fields)), axis, [(0, 1), (1, 0)]
            )
            before = after = spread_fields(swapped, fields, count)
        else:
            up = [(i, (i + 1) % size) for i in range(size)]
            down = [(j, i) for i, j in up]
            before = spread_fields(lax.ppermute(pick(last, chosen(-1)), axis, up), chosen(-1), count)
            after = spread_fields(lax.ppermute(pick(first, chosen(1)), axis, down), chosen(1), count)
        shard = jnp.concatenate([before, shard, after], axis=dim)
    return shard


SIDES = (("gx", 2), ("gy", 3), ("gz", 1))


def stream_adjoint(extended, margin, adjoint, extent):
    arrived = jnp.stack(
        [
            offset_view(
                extended[member],
                margin,
                tuple((int(entry) for entry in VELOCITY_ALL[member])),
                extent,
            )
            for member in range(26)
        ]
    )
    return bounce(arrived, adjoint)


def phase_fields(fraction_ext, extent):
    box = tuple(n + 2 for n in extent)
    inner = fraction_ext[1:-1, 1:-1, 1:-1]
    potential_box = wall_zero(well_term(inner) - STIFFNESS * laplace(fraction_ext, 1, box), 1, 0)
    return gradient(fraction_ext, 2, extent), gradient(potential_box, 1, extent)


def collide_adjoint(populations, phase_grad, potential_grad, arrived):
    pullback = jax.vjp(collide, populations, phase_grad, potential_grad)[1]
    return pullback(arrived)


def phase_adjoint(fraction, adjoint_pgrad, adjoint_mgrad, extra, extent):
    combined = jnp.concatenate([adjoint_pgrad, adjoint_mgrad, extra], 0)
    extended = extended_2(combined, SIDES, 2, lead=6)
    combined_ext = wall_zero(extended[:6], 2, 1)
    box = tuple(n + 2 for n in extent)
    mu_box = wall_zero(spread(combined_ext[3:6], 1, box), 1, 0)
    adjoint_phase = (
        well_slope(fraction) * mu_box[1:-1, 1:-1, 1:-1]
        - STIFFNESS * laplace(mu_box, 1, extent)
        + spread(combined_ext[:3], 2, extent)
    )
    return adjoint_phase, extended[6:]


def face_shifts(values):
    shifted = {}
    for axis, dim in SIDES:
        count, length = (lax.axis_size(axis), values.shape[dim - 1])
        last = lax.slice_in_dim(values, length - 1, length, axis=dim - 1)
        first = lax.slice_in_dim(values, 0, 1, axis=dim - 1)
        if axis == "gz" and count == 2:
            lower = lax.axis_index(axis) == 0
            swapped = lax.ppermute(jnp.where(lower, last, first), axis, [(0, 1), (1, 0)])
            before, after = swapped, swapped
        else:
            up = [(i, (i + 1) % count) for i in range(count)]
            down = [(j, i) for i, j in up]
            before = lax.ppermute(last, axis, up)
            after = lax.ppermute(first, axis, down)
        plus = tuple(1 if a == dim - 1 else 0 for a in range(3))
        shifted[plus] = shift_along(values, after, dim - 1, 1)
        shifted[negate(plus)] = shift_along(values, before, dim - 1, -1)
    return shifted


def shift_along(values, halo, axis, sign):
    length = values.shape[axis]
    if sign == 1:
        return jnp.concatenate([lax.slice_in_dim(values, 1, length, axis=axis), halo], axis)
    return jnp.concatenate([halo, lax.slice_in_dim(values, 0, length - 1, axis=axis)], axis)


def finish(adjoint_pops, adjoint_phase):
    return jnp.concatenate([adjoint_pops[:19], adjoint_pops[19:] + adjoint_phase[None]], 0)


def local(populations0, populations1, cotangent):
    states = [populations1.astype(jnp.float32), populations0.astype(jnp.float32)]
    fractions = jnp.stack([jnp.sum(state[19:], 0) for state in states])
    extent = fractions.shape[1:]
    first_ext = extended_2(jnp.concatenate([fractions, cotangent], 0), SIDES, 2, lead=2)
    fraction_ext = wall_zero(first_ext[:2], 2, 1)
    fields1 = phase_fields(fraction_ext[0], extent)
    fields0 = phase_fields(fraction_ext[1], extent)

    arrived = stream_adjoint(first_ext[2:], 2, cotangent, extent)
    pops, pgrad_adj, mgrad_adj = collide_adjoint(states[0], *fields1, arrived)
    adjoint_phase, pops_ext = phase_adjoint(fractions[0], pgrad_adj, mgrad_adj, pops, extent)
    adjoint1 = finish(pops, adjoint_phase)

    phase_shifted = face_shifts(adjoint_phase)
    arrived = []
    for member in range(26):
        velocity = tuple(int(entry) for entry in VELOCITY_ALL[member])
        values = offset_view(pops_ext[member], 2, velocity, extent)
        if member >= 19:
            values = values + (adjoint_phase if member == 19 else phase_shifted[velocity])
        arrived.append(values)
    arrived = bounce(jnp.stack(arrived), adjoint1)
    pops, pgrad_adj, mgrad_adj = collide_adjoint(states[1], *fields0, arrived)
    adjoint_phase, _ = phase_adjoint(fractions[1], pgrad_adj, mgrad_adj, pops[:0], extent)
    return finish(pops, adjoint_phase)


def solution(mesh):
    return jax.shard_map(
        local,
        mesh=mesh,
        in_specs=(P(None, "gz", "gx", "gy"), P(None, "gz", "gx", "gy"), P(None, "gz", "gx", "gy")),
        out_specs=P(None, "gz", "gx", "gy"),
        check_vma=False,
    )
```

```python
import jax
import jax.numpy as jnp
import numpy as np
from jax import lax
from jax.sharding import PartitionSpec as P

VELOCITY = np.array(
    [
        [0, 0, 0],
        [1, 0, 0],
        [-1, 0, 0],
        [0, 1, 0],
        [0, -1, 0],
        [0, 0, 1],
        [0, 0, -1],
        [1, 1, 0],
        [-1, -1, 0],
        [1, -1, 0],
        [-1, 1, 0],
        [1, 0, 1],
        [-1, 0, -1],
        [1, 0, -1],
        [-1, 0, 1],
        [0, 1, 1],
        [0, -1, -1],
        [0, 1, -1],
        [0, -1, 1],
    ]
)
OPPOSITE = [0, 2, 1, 4, 3, 6, 5, 8, 7, 10, 9, 12, 11, 14, 13, 16, 15, 18, 17]
FLOW_WEIGHT = [1.0 / 3.0] + [1.0 / 18.0] * 6 + [1.0 / 36.0] * 12
PHASE_WEIGHT = [0.25] + [0.125] * 6
VELOCITY_ALL = np.concatenate([VELOCITY, VELOCITY[:7]], 0)
OPPOSITE_ALL = OPPOSITE + [19 + mirror for mirror in OPPOSITE[:7]]
WELL_DEPTH = 0.3
STIFFNESS = 0.6
SHARPEN = 0.3
PHASE_RATE = 1.4
UNITS = ((1, 0, 0), (0, 1, 0), (0, 0, 1))
CENTER = (0, 0, 0)


def expand(weights, rank):
    values = [float(entry) for entry in list(weights)]
    return jnp.asarray(values, jnp.float32).reshape((-1,) + (1,) * rank)


def along(velocity_table, vector):
    rank = vector.ndim - 1
    total = expand(velocity_table[:, 0], rank) * vector[0]
    for direction in range(1, 3):
        total = total + expand(velocity_table[:, direction], rank) * vector[direction]
    return total


def collide(populations, phase_grad, potential_grad):
    rank = populations.ndim - 1
    flow_part = populations[:19]
    phase_part = populations[19:]
    fraction = jnp.sum(phase_part, 0)
    density = 0.2 + 0.8 * fraction
    pressure = jnp.sum(flow_part, 0)
    body_force = -fraction[None] * potential_grad
    momentum = jnp.stack(
        [jnp.sum(expand(VELOCITY[:, direction], rank) * flow_part, 0) for direction in range(3)]
    )
    velocity = (momentum + 0.5 * body_force) / density[None]
    along_flow = along(VELOCITY, velocity)
    speed_square = jnp.sum(velocity * velocity, 0)
    relax_rate = 1.1 + 0.5 * fraction
    flow_equil = expand(FLOW_WEIGHT, rank) * (
        pressure + density * (3.0 * along_flow + 4.5 * along_flow * along_flow - 1.5 * speed_square)
    )
    along_force = along(VELOCITY, body_force)
    speed_force = jnp.sum(velocity * body_force, 0)
    source = expand(FLOW_WEIGHT, rank) * (
        3.0 * (along_force - speed_force) + 9.0 * along_flow * along_force
    )
    flow_post = (
        flow_part - relax_rate * (flow_part - flow_equil) + (1.0 - 0.5 * relax_rate) * source
    )
    magnitude = jnp.sqrt(jnp.sum(phase_grad * phase_grad, 0) + 0.0625)
    normal = phase_grad / magnitude
    along_normal = along(VELOCITY[:7], normal)
    phase_equil = expand(PHASE_WEIGHT, rank) * (
        fraction * (1.0 + 4.0 * along_flow[:7])
        + 4.0 * SHARPEN * fraction * (1.0 - fraction) * along_normal
    )
    phase_post = phase_part - PHASE_RATE * (phase_part - phase_equil)
    return jnp.concatenate([flow_post, phase_post], 0)


def wall_zero(extended, width, vertical_dim):
    height = extended.shape[vertical_dim]
    layer_index = lax.broadcasted_iota(jnp.int32, (height,), 0)
    position = lax.axis_index("gz")
    bricks = lax.axis_size("gz")
    bottom_wall = jnp.logical_and(layer_index < width, position == 0)
    top_wall = jnp.logical_and(layer_index >= height - width, position == bricks - 1)
    inside = jnp.where(jnp.logical_or(bottom_wall, top_wall), 0.0, 1.0).astype(extended.dtype)
    extent = [1] * extended.ndim
    extent[vertical_dim] = height
    return extended * inside.reshape(extent)


def offset_view(extended, margin, offset, extent):
    return extended[
        ...,
        margin + offset[0] : margin + offset[0] + extent[0],
        margin + offset[1] : margin + offset[1] + extent[1],
        margin + offset[2] : margin + offset[2] + extent[2],
    ]


def negate(offset):
    return tuple((-entry for entry in offset))


def gradient(extended, margin, extent):
    return jnp.stack(
        [
            (
                offset_view(extended, margin, unit, extent)
                - offset_view(extended, margin, negate(unit), extent)
            )
            * 0.5
            for unit in UNITS
        ]
    )


def laplace(extended, margin, extent):
    total = -6.0 * offset_view(extended, margin, CENTER, extent)
    for unit in UNITS:
        total = (
            total
            + offset_view(extended, margin, unit, extent)
            + offset_view(extended, margin, negate(unit), extent)
        )
    return total


def spread(extended, margin, extent):
    total = jnp.zeros(extent, jnp.float32)
    for direction in range(3):
        unit = UNITS[direction]
        total = (
            total
            + (
                offset_view(extended[direction], margin, negate(unit), extent)
                - offset_view(extended[direction], margin, unit, extent)
            )
            * 0.5
        )
    return total


def well_term(fraction):
    return 4.0 * WELL_DEPTH * fraction * (fraction - 1.0) * (fraction - 0.5)


def well_slope(fraction):
    return 4.0 * WELL_DEPTH * (3.0 * fraction * fraction - 3.0 * fraction + 0.5)


def bounce(arrived, adjoint):
    height = adjoint.shape[1]
    layer_index = lax.broadcasted_iota(jnp.int32, (height,), 0)
    position = lax.axis_index("gz")
    bricks = lax.axis_size("gz")
    bottom_wall = jnp.logical_and(layer_index == 0, position == 0).reshape((1, height, 1, 1))
    top_wall = jnp.logical_and(layer_index == height - 1, position == bricks - 1).reshape(
        (1, height, 1, 1)
    )
    rising = jnp.asarray((VELOCITY_ALL[:, 0] == 1).reshape((26, 1, 1, 1)))
    falling = jnp.asarray((VELOCITY_ALL[:, 0] == -1).reshape((26, 1, 1, 1)))
    reflect = jnp.logical_or(
        jnp.logical_and(rising, top_wall), jnp.logical_and(falling, bottom_wall)
    )
    flipped = jnp.stack([adjoint[mirror] for mirror in OPPOSITE_ALL])
    return jnp.where(reflect, flipped, arrived)


def extended_2(shard, sides, width):
    for axis, dim in sides:
        count, length = (lax.axis_size(axis), shard.shape[dim])
        last = lax.slice_in_dim(shard, length - width, length, axis=dim)
        first = lax.slice_in_dim(shard, 0, width, axis=dim)
        if axis == "gz" and count == 2:
            lower = lax.axis_index(axis) == 0
            swapped = lax.ppermute(jnp.where(lower, last, first), axis, [(0, 1), (1, 0)])
            before, after = swapped, swapped
        else:
            up = [(i, (i + 1) % count) for i in range(count)]
            down = [(j, i) for i, j in up]
            before = lax.ppermute(last, axis, up)
            after = lax.ppermute(first, axis, down)
        shard = jnp.concatenate([before, shard, after], axis=dim)
    return shard


SIDES = (("gy", 3), ("gx", 2), ("gz", 1))


def stream_adjoint(extended, margin, adjoint, extent):
    arrived = jnp.stack(
        [
            offset_view(
                extended[member],
                margin,
                tuple((int(entry) for entry in VELOCITY_ALL[member])),
                extent,
            )
            for member in range(26)
        ]
    )
    return bounce(arrived, adjoint)


def phase_fields(fraction_ext, extent):
    box = tuple(n + 2 for n in extent)
    inner = fraction_ext[1:-1, 1:-1, 1:-1]
    potential_box = wall_zero(well_term(inner) - STIFFNESS * laplace(fraction_ext, 1, box), 1, 0)
    return gradient(fraction_ext, 2, extent), gradient(potential_box, 1, extent)


def collide_adjoint(populations, phase_grad, potential_grad, arrived):
    pullback = jax.vjp(collide, populations, phase_grad, potential_grad)[1]
    return pullback(arrived)


def phase_adjoint(fraction, adjoint_pgrad, adjoint_mgrad, extra, extent):
    combined = jnp.concatenate([adjoint_pgrad, adjoint_mgrad, extra], 0)
    extended = extended_2(combined, SIDES, 2)
    combined_ext = wall_zero(extended[:6], 2, 1)
    box = tuple(n + 2 for n in extent)
    mu_box = wall_zero(spread(combined_ext[3:6], 1, box), 1, 0)
    adjoint_phase = (
        well_slope(fraction) * mu_box[1:-1, 1:-1, 1:-1]
        - STIFFNESS * laplace(mu_box, 1, extent)
        + spread(combined_ext[:3], 2, extent)
    )
    return adjoint_phase, extended[6:]


def face_shifts(values):
    shifted = {}
    for axis, dim in SIDES:
        count, length = (lax.axis_size(axis), values.shape[dim - 1])
        last = lax.slice_in_dim(values, length - 1, length, axis=dim - 1)
        first = lax.slice_in_dim(values, 0, 1, axis=dim - 1)
        if axis == "gz" and count == 2:
            lower = lax.axis_index(axis) == 0
            swapped = lax.ppermute(jnp.where(lower, last, first), axis, [(0, 1), (1, 0)])
            before, after = swapped, swapped
        else:
            up = [(i, (i + 1) % count) for i in range(count)]
            down = [(j, i) for i, j in up]
            before = lax.ppermute(last, axis, up)
            after = lax.ppermute(first, axis, down)
        plus = tuple(1 if a == dim - 1 else 0 for a in range(3))
        shifted[plus] = shift_along(values, after, dim - 1, 1)
        shifted[negate(plus)] = shift_along(values, before, dim - 1, -1)
    return shifted


def shift_along(values, halo, axis, sign):
    length = values.shape[axis]
    if sign == 1:
        return jnp.concatenate([lax.slice_in_dim(values, 1, length, axis=axis), halo], axis)
    return jnp.concatenate([halo, lax.slice_in_dim(values, 0, length - 1, axis=axis)], axis)


def finish(adjoint_pops, adjoint_phase):
    return jnp.concatenate([adjoint_pops[:19], adjoint_pops[19:] + adjoint_phase[None]], 0)


def local(populations0, populations1, cotangent):
    states = [populations1.astype(jnp.float32), populations0.astype(jnp.float32)]
    fractions = jnp.stack([jnp.sum(state[19:], 0) for state in states])
    extent = fractions.shape[1:]
    first_ext = extended_2(jnp.concatenate([fractions, cotangent], 0), SIDES, 2)
    fraction_ext = wall_zero(first_ext[:2], 2, 1)
    fields1 = phase_fields(fraction_ext[0], extent)
    fields0 = phase_fields(fraction_ext[1], extent)

    arrived = stream_adjoint(first_ext[2:], 2, cotangent, extent)
    pops, pgrad_adj, mgrad_adj = collide_adjoint(states[0], *fields1, arrived)
    adjoint_phase, pops_ext = phase_adjoint(fractions[0], pgrad_adj, mgrad_adj, pops, extent)
    adjoint1 = finish(pops, adjoint_phase)

    phase_shifted = face_shifts(adjoint_phase)
    arrived = []
    for member in range(26):
        velocity = tuple(int(entry) for entry in VELOCITY_ALL[member])
        values = offset_view(pops_ext[member], 2, velocity, extent)
        if member >= 19:
            values = values + (adjoint_phase if member == 19 else phase_shifted[velocity])
        arrived.append(values)
    arrived = bounce(jnp.stack(arrived), adjoint1)
    pops, pgrad_adj, mgrad_adj = collide_adjoint(states[1], *fields0, arrived)
    adjoint_phase, _ = phase_adjoint(fractions[1], pgrad_adj, mgrad_adj, pops[:0], extent)
    return finish(pops, adjoint_phase)


def solution(mesh):
    return jax.shard_map(
        local,
        mesh=mesh,
        in_specs=(P(None, "gz", "gx", "gy"), P(None, "gz", "gx", "gy"), P(None, "gz", "gx", "gy")),
        out_specs=P(None, "gz", "gx", "gy"),
        check_vma=False,
    )
```

```python
import jax
import jax.numpy as jnp
import numpy as np
from jax import lax
from jax.sharding import PartitionSpec as P

VELOCITY = np.array(
    [
        [0, 0, 0],
        [1, 0, 0],
        [-1, 0, 0],
        [0, 1, 0],
        [0, -1, 0],
        [0, 0, 1],
        [0, 0, -1],
        [1, 1, 0],
        [-1, -1, 0],
        [1, -1, 0],
        [-1, 1, 0],
        [1, 0, 1],
        [-1, 0, -1],
        [1, 0, -1],
        [-1, 0, 1],
        [0, 1, 1],
        [0, -1, -1],
        [0, 1, -1],
        [0, -1, 1],
    ]
)
OPPOSITE = [0, 2, 1, 4, 3, 6, 5, 8, 7, 10, 9, 12, 11, 14, 13, 16, 15, 18, 17]
FLOW_WEIGHT = [1.0 / 3.0] + [1.0 / 18.0] * 6 + [1.0 / 36.0] * 12
PHASE_WEIGHT = [0.25] + [0.125] * 6
VELOCITY_ALL = np.concatenate([VELOCITY, VELOCITY[:7]], 0)
OPPOSITE_ALL = OPPOSITE + [19 + mirror for mirror in OPPOSITE[:7]]
WELL_DEPTH = 0.3
STIFFNESS = 0.6
SHARPEN = 0.3
PHASE_RATE = 1.4
UNITS = ((1, 0, 0), (0, 1, 0), (0, 0, 1))
CENTER = (0, 0, 0)


def expand(weights, rank):
    values = [float(entry) for entry in list(weights)]
    return jnp.asarray(values, jnp.float32).reshape((-1,) + (1,) * rank)


def along(velocity_table, vector):
    rank = vector.ndim - 1
    total = expand(velocity_table[:, 0], rank) * vector[0]
    for direction in range(1, 3):
        total = total + expand(velocity_table[:, direction], rank) * vector[direction]
    return total


def collide(populations, phase_grad, potential_grad):
    rank = populations.ndim - 1
    flow_part = populations[:19]
    phase_part = populations[19:]
    fraction = jnp.sum(phase_part, 0)
    density = 0.2 + 0.8 * fraction
    pressure = jnp.sum(flow_part, 0)
    body_force = -fraction[None] * potential_grad
    momentum = jnp.stack(
        [jnp.sum(expand(VELOCITY[:, direction], rank) * flow_part, 0) for direction in range(3)]
    )
    velocity = (momentum + 0.5 * body_force) / density[None]
    along_flow = along(VELOCITY, velocity)
    speed_square = jnp.sum(velocity * velocity, 0)
    relax_rate = 1.1 + 0.5 * fraction
    flow_equil = expand(FLOW_WEIGHT, rank) * (
        pressure + density * (3.0 * along_flow + 4.5 * along_flow * along_flow - 1.5 * speed_square)
    )
    along_force = along(VELOCITY, body_force)
    speed_force = jnp.sum(velocity * body_force, 0)
    source = expand(FLOW_WEIGHT, rank) * (
        3.0 * (along_force - speed_force) + 9.0 * along_flow * along_force
    )
    flow_post = (
        flow_part - relax_rate * (flow_part - flow_equil) + (1.0 - 0.5 * relax_rate) * source
    )
    magnitude = jnp.sqrt(jnp.sum(phase_grad * phase_grad, 0) + 0.0625)
    normal = phase_grad / magnitude
    along_normal = along(VELOCITY[:7], normal)
    phase_equil = expand(PHASE_WEIGHT, rank) * (
        fraction * (1.0 + 4.0 * along_flow[:7])
        + 4.0 * SHARPEN * fraction * (1.0 - fraction) * along_normal
    )
    phase_post = phase_part - PHASE_RATE * (phase_part - phase_equil)
    return jnp.concatenate([flow_post, phase_post], 0)


def wall_zero(extended, width, vertical_dim):
    height = extended.shape[vertical_dim]
    layer_index = lax.broadcasted_iota(jnp.int32, (height,), 0)
    position = lax.axis_index("gz")
    bricks = lax.axis_size("gz")
    bottom_wall = jnp.logical_and(layer_index < width, position == 0)
    top_wall = jnp.logical_and(layer_index >= height - width, position == bricks - 1)
    inside = jnp.where(jnp.logical_or(bottom_wall, top_wall), 0.0, 1.0).astype(extended.dtype)
    extent = [1] * extended.ndim
    extent[vertical_dim] = height
    return extended * inside.reshape(extent)


def offset_view(extended, margin, offset, extent):
    return extended[
        ...,
        margin + offset[0] : margin + offset[0] + extent[0],
        margin + offset[1] : margin + offset[1] + extent[1],
        margin + offset[2] : margin + offset[2] + extent[2],
    ]


def negate(offset):
    return tuple((-entry for entry in offset))


def gradient(extended, margin, extent):
    return jnp.stack(
        [
            (
                offset_view(extended, margin, unit, extent)
                - offset_view(extended, margin, negate(unit), extent)
            )
            * 0.5
            for unit in UNITS
        ]
    )


def laplace(extended, margin, extent):
    total = -6.0 * offset_view(extended, margin, CENTER, extent)
    for unit in UNITS:
        total = (
            total
            + offset_view(extended, margin, unit, extent)
            + offset_view(extended, margin, negate(unit), extent)
        )
    return total


def spread(extended, margin, extent):
    total = jnp.zeros(extent, jnp.float32)
    for direction in range(3):
        unit = UNITS[direction]
        total = (
            total
            + (
                offset_view(extended[direction], margin, negate(unit), extent)
                - offset_view(extended[direction], margin, unit, extent)
            )
            * 0.5
        )
    return total


def well_term(fraction):
    return 4.0 * WELL_DEPTH * fraction * (fraction - 1.0) * (fraction - 0.5)


def well_slope(fraction):
    return 4.0 * WELL_DEPTH * (3.0 * fraction * fraction - 3.0 * fraction + 0.5)


def bounce(arrived, adjoint):
    height = adjoint.shape[1]
    layer_index = lax.broadcasted_iota(jnp.int32, (height,), 0)
    position = lax.axis_index("gz")
    bricks = lax.axis_size("gz")
    bottom_wall = jnp.logical_and(layer_index == 0, position == 0).reshape((1, height, 1, 1))
    top_wall = jnp.logical_and(layer_index == height - 1, position == bricks - 1).reshape(
        (1, height, 1, 1)
    )
    rising = jnp.asarray((VELOCITY_ALL[:, 0] == 1).reshape((26, 1, 1, 1)))
    falling = jnp.asarray((VELOCITY_ALL[:, 0] == -1).reshape((26, 1, 1, 1)))
    reflect = jnp.logical_or(
        jnp.logical_and(rising, top_wall), jnp.logical_and(falling, bottom_wall)
    )
    flipped = jnp.stack([adjoint[mirror] for mirror in OPPOSITE_ALL])
    return jnp.where(reflect, flipped, arrived)


def extended_2(shard, sides, width):
    for axis, dim in sides:
        count, length = (lax.axis_size(axis), shard.shape[dim])
        last = lax.slice_in_dim(shard, length - width, length, axis=dim)
        first = lax.slice_in_dim(shard, 0, width, axis=dim)
        if axis == "gz" and count == 2:
            lower = lax.axis_index(axis) == 0
            swapped = lax.ppermute(jnp.where(lower, last, first), axis, [(0, 1), (1, 0)])
            before, after = swapped, swapped
        else:
            up = [(i, (i + 1) % count) for i in range(count)]
            down = [(j, i) for i, j in up]
            before = lax.ppermute(last, axis, up)
            after = lax.ppermute(first, axis, down)
        shard = jnp.concatenate([before, shard, after], axis=dim)
    return shard


SIDES = (("gy", 3), ("gx", 2), ("gz", 1))


def stream_adjoint(extended, margin, adjoint, extent):
    arrived = jnp.stack(
        [
            offset_view(
                extended[member],
                margin,
                tuple((int(entry) for entry in VELOCITY_ALL[member])),
                extent,
            )
            for member in range(26)
        ]
    )
    return bounce(arrived, adjoint)


def phase_fields(fraction_ext, extent):
    box = tuple(n + 2 for n in extent)
    inner = fraction_ext[1:-1, 1:-1, 1:-1]
    potential_box = wall_zero(well_term(inner) - STIFFNESS * laplace(fraction_ext, 1, box), 1, 0)
    return gradient(fraction_ext, 2, extent), gradient(potential_box, 1, extent)


def collide_adjoint(populations, phase_grad, potential_grad, arrived):
    pullback = jax.vjp(collide, populations, phase_grad, potential_grad)[1]
    return pullback(arrived)


def phase_adjoint(fraction, adjoint_pgrad, adjoint_mgrad, extra, extent):
    combined = jnp.concatenate([adjoint_pgrad, adjoint_mgrad, extra], 0)
    extended = extended_2(combined, SIDES, 2)
    combined_ext = wall_zero(extended[:6], 2, 1)
    box = tuple(n + 2 for n in extent)
    mu_box = wall_zero(spread(combined_ext[3:6], 1, box), 1, 0)
    adjoint_phase = (
        well_slope(fraction) * mu_box[1:-1, 1:-1, 1:-1]
        - STIFFNESS * laplace(mu_box, 1, extent)
        + spread(combined_ext[:3], 2, extent)
    )
    return adjoint_phase, extended[6:]


def face_shifts(values):
    shifted = {}
    for axis, dim in SIDES:
        count, length = (lax.axis_size(axis), values.shape[dim - 1])
        last = lax.slice_in_dim(values, length - 1, length, axis=dim - 1)
        first = lax.slice_in_dim(values, 0, 1, axis=dim - 1)
        if axis == "gz" and count == 2:
            lower = lax.axis_index(axis) == 0
            swapped = lax.ppermute(jnp.where(lower, last, first), axis, [(0, 1), (1, 0)])
            before, after = swapped, swapped
        else:
            up = [(i, (i + 1) % count) for i in range(count)]
            down = [(j, i) for i, j in up]
            before = lax.ppermute(last, axis, up)
            after = lax.ppermute(first, axis, down)
        plus = tuple(1 if a == dim - 1 else 0 for a in range(3))
        shifted[plus] = shift_along(values, after, dim - 1, 1)
        shifted[negate(plus)] = shift_along(values, before, dim - 1, -1)
    return shifted


def shift_along(values, halo, axis, sign):
    length = values.shape[axis]
    if sign == 1:
        return jnp.concatenate([lax.slice_in_dim(values, 1, length, axis=axis), halo], axis)
    return jnp.concatenate([halo, lax.slice_in_dim(values, 0, length - 1, axis=axis)], axis)


def finish(adjoint_pops, adjoint_phase):
    return jnp.concatenate([adjoint_pops[:19], adjoint_pops[19:] + adjoint_phase[None]], 0)


def phase_adjoint_wide(fraction_box, adjoint_pgrad, adjoint_mgrad, extra, extent):
    combined = jnp.concatenate([adjoint_pgrad, adjoint_mgrad, extra], 0)
    extended = extended_2(combined, SIDES, 3)
    combined_ext = wall_zero(extended[:6], 3, 1)
    box1 = tuple(n + 2 for n in extent)
    box2 = tuple(n + 4 for n in extent)
    mu_box = wall_zero(spread(combined_ext[3:6], 1, box2), 2, 0)
    adjoint_phase = (
        well_slope(fraction_box) * mu_box[1:-1, 1:-1, 1:-1]
        - STIFFNESS * laplace(mu_box, 1, box1)
        + spread(combined_ext[:3], 2, box1)
    )
    return adjoint_phase, extended[6:]


def local(populations0, populations1, cotangent):
    states = [populations1.astype(jnp.float32), populations0.astype(jnp.float32)]
    fractions = jnp.stack([jnp.sum(state[19:], 0) for state in states])
    extent = fractions.shape[1:]
    first_ext = extended_2(jnp.concatenate([fractions, cotangent], 0), SIDES, 2)
    fraction_ext = wall_zero(first_ext[:2], 2, 1)
    fields1 = phase_fields(fraction_ext[0], extent)
    fields0 = phase_fields(fraction_ext[1], extent)

    arrived = stream_adjoint(first_ext[2:], 2, cotangent, extent)
    pops, pgrad_adj, mgrad_adj = collide_adjoint(states[0], *fields1, arrived)
    phase_box, pops_ext = phase_adjoint_wide(
        fraction_ext[0, 1:-1, 1:-1, 1:-1], pgrad_adj, mgrad_adj, pops, extent
    )
    adjoint1 = finish(pops, phase_box[1:-1, 1:-1, 1:-1])

    arrived = []
    for member in range(26):
        velocity = tuple(int(entry) for entry in VELOCITY_ALL[member])
        values = offset_view(pops_ext[member], 3, velocity, extent)
        if member >= 19:
            values = values + offset_view(phase_box, 1, velocity, extent)
        arrived.append(values)
    arrived = bounce(jnp.stack(arrived), adjoint1)
    pops, pgrad_adj, mgrad_adj = collide_adjoint(states[1], *fields0, arrived)
    adjoint_phase, _ = phase_adjoint(fractions[1], pgrad_adj, mgrad_adj, pops[:0], extent)
    return finish(pops, adjoint_phase)


def solution(mesh):
    return jax.shard_map(
        local,
        mesh=mesh,
        in_specs=(P(None, "gz", "gx", "gy"), P(None, "gz", "gx", "gy"), P(None, "gz", "gx", "gy")),
        out_specs=P(None, "gz", "gx", "gy"),
        check_vma=False,
    )
```

```python
import jax
import jax.numpy as jnp
import numpy as np
from jax import lax
from jax.sharding import PartitionSpec as P

VELOCITY = np.array(
    [
        [0, 0, 0],
        [1, 0, 0],
        [-1, 0, 0],
        [0, 1, 0],
        [0, -1, 0],
        [0, 0, 1],
        [0, 0, -1],
        [1, 1, 0],
        [-1, -1, 0],
        [1, -1, 0],
        [-1, 1, 0],
        [1, 0, 1],
        [-1, 0, -1],
        [1, 0, -1],
        [-1, 0, 1],
        [0, 1, 1],
        [0, -1, -1],
        [0, 1, -1],
        [0, -1, 1],
    ]
)
OPPOSITE = [0, 2, 1, 4, 3, 6, 5, 8, 7, 10, 9, 12, 11, 14, 13, 16, 15, 18, 17]
FLOW_WEIGHT = [1.0 / 3.0] + [1.0 / 18.0] * 6 + [1.0 / 36.0] * 12
PHASE_WEIGHT = [0.25] + [0.125] * 6
VELOCITY_ALL = np.concatenate([VELOCITY, VELOCITY[:7]], 0)
OPPOSITE_ALL = OPPOSITE + [19 + mirror for mirror in OPPOSITE[:7]]
WELL_DEPTH = 0.3
STIFFNESS = 0.6
SHARPEN = 0.3
PHASE_RATE = 1.4
UNITS = ((1, 0, 0), (0, 1, 0), (0, 0, 1))
CENTER = (0, 0, 0)


def expand(weights, rank):
    values = [float(entry) for entry in list(weights)]
    return jnp.asarray(values, jnp.float32).reshape((-1,) + (1,) * rank)


def along(velocity_table, vector):
    rank = vector.ndim - 1
    total = expand(velocity_table[:, 0], rank) * vector[0]
    for direction in range(1, 3):
        total = total + expand(velocity_table[:, direction], rank) * vector[direction]
    return total


def collide(populations, phase_grad, potential_grad):
    rank = populations.ndim - 1
    flow_part = populations[:19]
    phase_part = populations[19:]
    fraction = jnp.sum(phase_part, 0)
    density = 0.2 + 0.8 * fraction
    pressure = jnp.sum(flow_part, 0)
    body_force = -fraction[None] * potential_grad
    momentum = jnp.stack(
        [jnp.sum(expand(VELOCITY[:, direction], rank) * flow_part, 0) for direction in range(3)]
    )
    velocity = (momentum + 0.5 * body_force) / density[None]
    along_flow = along(VELOCITY, velocity)
    speed_square = jnp.sum(velocity * velocity, 0)
    relax_rate = 1.1 + 0.5 * fraction
    flow_equil = expand(FLOW_WEIGHT, rank) * (
        pressure + density * (3.0 * along_flow + 4.5 * along_flow * along_flow - 1.5 * speed_square)
    )
    along_force = along(VELOCITY, body_force)
    speed_force = jnp.sum(velocity * body_force, 0)
    source = expand(FLOW_WEIGHT, rank) * (
        3.0 * (along_force - speed_force) + 9.0 * along_flow * along_force
    )
    flow_post = (
        flow_part - relax_rate * (flow_part - flow_equil) + (1.0 - 0.5 * relax_rate) * source
    )
    magnitude = jnp.sqrt(jnp.sum(phase_grad * phase_grad, 0) + 0.0625)
    normal = phase_grad / magnitude
    along_normal = along(VELOCITY[:7], normal)
    phase_equil = expand(PHASE_WEIGHT, rank) * (
        fraction * (1.0 + 4.0 * along_flow[:7])
        + 4.0 * SHARPEN * fraction * (1.0 - fraction) * along_normal
    )
    phase_post = phase_part - PHASE_RATE * (phase_part - phase_equil)
    return jnp.concatenate([flow_post, phase_post], 0)


def wall_zero(extended, width, vertical_dim):
    height = extended.shape[vertical_dim]
    layer_index = lax.broadcasted_iota(jnp.int32, (height,), 0)
    position = lax.axis_index("gz")
    bricks = lax.axis_size("gz")
    bottom_wall = jnp.logical_and(layer_index < width, position == 0)
    top_wall = jnp.logical_and(layer_index >= height - width, position == bricks - 1)
    inside = jnp.where(jnp.logical_or(bottom_wall, top_wall), 0.0, 1.0).astype(extended.dtype)
    extent = [1] * extended.ndim
    extent[vertical_dim] = height
    return extended * inside.reshape(extent)


def offset_view(extended, margin, offset, extent):
    return extended[
        ...,
        margin + offset[0] : margin + offset[0] + extent[0],
        margin + offset[1] : margin + offset[1] + extent[1],
        margin + offset[2] : margin + offset[2] + extent[2],
    ]


def negate(offset):
    return tuple((-entry for entry in offset))


def gradient(extended, margin, extent):
    return jnp.stack(
        [
            (
                offset_view(extended, margin, unit, extent)
                - offset_view(extended, margin, negate(unit), extent)
            )
            * 0.5
            for unit in UNITS
        ]
    )


def laplace(extended, margin, extent):
    total = -6.0 * offset_view(extended, margin, CENTER, extent)
    for unit in UNITS:
        total = (
            total
            + offset_view(extended, margin, unit, extent)
            + offset_view(extended, margin, negate(unit), extent)
        )
    return total


def spread(extended, margin, extent):
    total = jnp.zeros(extent, jnp.float32)
    for direction in range(3):
        unit = UNITS[direction]
        total = (
            total
            + (
                offset_view(extended[direction], margin, negate(unit), extent)
                - offset_view(extended[direction], margin, unit, extent)
            )
            * 0.5
        )
    return total


def well_term(fraction):
    return 4.0 * WELL_DEPTH * fraction * (fraction - 1.0) * (fraction - 0.5)


def well_slope(fraction):
    return 4.0 * WELL_DEPTH * (3.0 * fraction * fraction - 3.0 * fraction + 0.5)


def bounce(arrived, adjoint):
    height = adjoint.shape[1]
    layer_index = lax.broadcasted_iota(jnp.int32, (height,), 0)
    position = lax.axis_index("gz")
    bricks = lax.axis_size("gz")
    bottom_wall = jnp.logical_and(layer_index == 0, position == 0).reshape((1, height, 1, 1))
    top_wall = jnp.logical_and(layer_index == height - 1, position == bricks - 1).reshape(
        (1, height, 1, 1)
    )
    rising = jnp.asarray((VELOCITY_ALL[:, 0] == 1).reshape((26, 1, 1, 1)))
    falling = jnp.asarray((VELOCITY_ALL[:, 0] == -1).reshape((26, 1, 1, 1)))
    reflect = jnp.logical_or(
        jnp.logical_and(rising, top_wall), jnp.logical_and(falling, bottom_wall)
    )
    flipped = jnp.stack([adjoint[mirror] for mirror in OPPOSITE_ALL])
    return jnp.where(reflect, flipped, arrived)


def extended_2(shard, sides, width):
    for axis, dim in sides:
        count, length = (lax.axis_size(axis), shard.shape[dim])
        last = lax.slice_in_dim(shard, length - width, length, axis=dim)
        first = lax.slice_in_dim(shard, 0, width, axis=dim)
        if axis == "gz" and count == 2:
            lower = lax.axis_index(axis) == 0
            swapped = lax.ppermute(jnp.where(lower, last, first), axis, [(0, 1), (1, 0)])
            before, after = swapped, swapped
        else:
            up = [(i, (i + 1) % count) for i in range(count)]
            down = [(j, i) for i, j in up]
            before = lax.ppermute(last, axis, up)
            after = lax.ppermute(first, axis, down)
        shard = jnp.concatenate([before, shard, after], axis=dim)
    return shard


def extended_mixed(wide, narrow, width):
    count = wide.shape[0]
    has_narrow = narrow is not None
    shard = jnp.concatenate([wide, narrow], 0) if has_narrow else wide
    for axis, dim in SIDES:
        length = shard.shape[dim]

        def planes(side):
            index = [i if side == 1 else length - 1 - i for i in range(width)]
            layers = [lax.slice_in_dim(shard[:count], i, i + 1, axis=dim) for i in index]
            if has_narrow:
                layers.append(lax.slice_in_dim(shard[count:], index[0], index[0] + 1, axis=dim))
            return jnp.concatenate(layers, 0)

        def unpack(got, side):
            layers = [got[i * count : (i + 1) * count] for i in range(width)]
            ordered = layers if side == 1 else layers[::-1]
            slab = jnp.concatenate(ordered, dim)
            if not has_narrow:
                return slab
            near = got[width * count :]
            pad = [(0, 0)] * near.ndim
            pad[dim] = (0, width - 1) if side == 1 else (width - 1, 0)
            return jnp.concatenate([slab, jnp.pad(near, pad)], 0)

        size = lax.axis_size(axis)
        if axis == "gz" and size == 2:
            lower = lax.axis_index(axis) == 0
            got = lax.ppermute(jnp.where(lower, planes(-1), planes(1)), axis, [(0, 1), (1, 0)])
            before, after = unpack(got, -1), unpack(got, 1)
        else:
            up = [(i, (i + 1) % size) for i in range(size)]
            down = [(j, i) for i, j in up]
            before = unpack(lax.ppermute(planes(-1), axis, up), -1)
            after = unpack(lax.ppermute(planes(1), axis, down), 1)
        shard = jnp.concatenate([before, shard, after], axis=dim)
    return shard


SIDES = (("gy", 3), ("gx", 2), ("gz", 1))


def stream_adjoint(extended, margin, adjoint, extent):
    arrived = jnp.stack(
        [
            offset_view(
                extended[member],
                margin,
                tuple((int(entry) for entry in VELOCITY_ALL[member])),
                extent,
            )
            for member in range(26)
        ]
    )
    return bounce(arrived, adjoint)


def phase_fields(fraction_ext, extent):
    box = tuple(n + 2 for n in extent)
    inner = fraction_ext[1:-1, 1:-1, 1:-1]
    potential_box = wall_zero(well_term(inner) - STIFFNESS * laplace(fraction_ext, 1, box), 1, 0)
    return gradient(fraction_ext, 2, extent), gradient(potential_box, 1, extent)


def collide_adjoint(populations, phase_grad, potential_grad, arrived):
    pullback = jax.vjp(collide, populations, phase_grad, potential_grad)[1]
    return pullback(arrived)


def phase_adjoint(fraction, adjoint_pgrad, adjoint_mgrad, extra, extent):
    combined = jnp.concatenate([adjoint_pgrad, adjoint_mgrad, extra], 0)
    extended = extended_2(combined, SIDES, 2)
    combined_ext = wall_zero(extended[:6], 2, 1)
    box = tuple(n + 2 for n in extent)
    mu_box = wall_zero(spread(combined_ext[3:6], 1, box), 1, 0)
    adjoint_phase = (
        well_slope(fraction) * mu_box[1:-1, 1:-1, 1:-1]
        - STIFFNESS * laplace(mu_box, 1, extent)
        + spread(combined_ext[:3], 2, extent)
    )
    return adjoint_phase, extended[6:]


def face_shifts(values):
    shifted = {}
    for axis, dim in SIDES:
        count, length = (lax.axis_size(axis), values.shape[dim - 1])
        last = lax.slice_in_dim(values, length - 1, length, axis=dim - 1)
        first = lax.slice_in_dim(values, 0, 1, axis=dim - 1)
        if axis == "gz" and count == 2:
            lower = lax.axis_index(axis) == 0
            swapped = lax.ppermute(jnp.where(lower, last, first), axis, [(0, 1), (1, 0)])
            before, after = swapped, swapped
        else:
            up = [(i, (i + 1) % count) for i in range(count)]
            down = [(j, i) for i, j in up]
            before = lax.ppermute(last, axis, up)
            after = lax.ppermute(first, axis, down)
        plus = tuple(1 if a == dim - 1 else 0 for a in range(3))
        shifted[plus] = shift_along(values, after, dim - 1, 1)
        shifted[negate(plus)] = shift_along(values, before, dim - 1, -1)
    return shifted


def shift_along(values, halo, axis, sign):
    length = values.shape[axis]
    if sign == 1:
        return jnp.concatenate([lax.slice_in_dim(values, 1, length, axis=axis), halo], axis)
    return jnp.concatenate([halo, lax.slice_in_dim(values, 0, length - 1, axis=axis)], axis)


def finish(adjoint_pops, adjoint_phase):
    return jnp.concatenate([adjoint_pops[:19], adjoint_pops[19:] + adjoint_phase[None]], 0)


def phase_adjoint_wide(fraction_box, adjoint_pgrad, adjoint_mgrad, extra, extent):
    combined = jnp.concatenate([adjoint_pgrad, adjoint_mgrad, extra], 0)
    extended = extended_mixed(combined[:6], extra, 3)
    combined_ext = wall_zero(extended[:6], 3, 1)
    box1 = tuple(n + 2 for n in extent)
    box2 = tuple(n + 4 for n in extent)
    mu_box = wall_zero(spread(combined_ext[3:6], 1, box2), 2, 0)
    adjoint_phase = (
        well_slope(fraction_box) * mu_box[1:-1, 1:-1, 1:-1]
        - STIFFNESS * laplace(mu_box, 1, box1)
        + spread(combined_ext[:3], 2, box1)
    )
    return adjoint_phase, extended[6:]


def local(populations0, populations1, cotangent):
    states = [populations1.astype(jnp.float32), populations0.astype(jnp.float32)]
    fractions = jnp.stack([jnp.sum(state[19:], 0) for state in states])
    extent = fractions.shape[1:]
    first_ext = extended_mixed(fractions, cotangent, 2)
    fraction_ext = wall_zero(first_ext[:2], 2, 1)
    fields1 = phase_fields(fraction_ext[0], extent)
    fields0 = phase_fields(fraction_ext[1], extent)

    arrived = stream_adjoint(first_ext[2:], 2, cotangent, extent)
    pops, pgrad_adj, mgrad_adj = collide_adjoint(states[0], *fields1, arrived)
    phase_box, pops_ext = phase_adjoint_wide(
        fraction_ext[0, 1:-1, 1:-1, 1:-1], pgrad_adj, mgrad_adj, pops, extent
    )
    adjoint1 = finish(pops, phase_box[1:-1, 1:-1, 1:-1])

    arrived = []
    for member in range(26):
        velocity = tuple(int(entry) for entry in VELOCITY_ALL[member])
        values = offset_view(pops_ext[member], 3, velocity, extent)
        if member >= 19:
            values = values + offset_view(phase_box, 1, velocity, extent)
        arrived.append(values)
    arrived = bounce(jnp.stack(arrived), adjoint1)
    pops, pgrad_adj, mgrad_adj = collide_adjoint(states[1], *fields0, arrived)
    adjoint_phase, _ = phase_adjoint(fractions[1], pgrad_adj, mgrad_adj, pops[:0], extent)
    return finish(pops, adjoint_phase)


def solution(mesh):
    return jax.shard_map(
        local,
        mesh=mesh,
        in_specs=(P(None, "gz", "gx", "gy"), P(None, "gz", "gx", "gy"), P(None, "gz", "gx", "gy")),
        out_specs=P(None, "gz", "gx", "gy"),
        check_vma=False,
    )
```

```python
import jax
import jax.numpy as jnp
import numpy as np
from jax import lax
from jax.sharding import PartitionSpec as P

VELOCITY = np.array(
    [
        [0, 0, 0],
        [1, 0, 0],
        [-1, 0, 0],
        [0, 1, 0],
        [0, -1, 0],
        [0, 0, 1],
        [0, 0, -1],
        [1, 1, 0],
        [-1, -1, 0],
        [1, -1, 0],
        [-1, 1, 0],
        [1, 0, 1],
        [-1, 0, -1],
        [1, 0, -1],
        [-1, 0, 1],
        [0, 1, 1],
        [0, -1, -1],
        [0, 1, -1],
        [0, -1, 1],
    ]
)
OPPOSITE = [0, 2, 1, 4, 3, 6, 5, 8, 7, 10, 9, 12, 11, 14, 13, 16, 15, 18, 17]
FLOW_WEIGHT = [1.0 / 3.0] + [1.0 / 18.0] * 6 + [1.0 / 36.0] * 12
PHASE_WEIGHT = [0.25] + [0.125] * 6
VELOCITY_ALL = np.concatenate([VELOCITY, VELOCITY[:7]], 0)
OPPOSITE_ALL = OPPOSITE + [19 + mirror for mirror in OPPOSITE[:7]]
WELL_DEPTH = 0.3
STIFFNESS = 0.6
SHARPEN = 0.3
PHASE_RATE = 1.4
UNITS = ((1, 0, 0), (0, 1, 0), (0, 0, 1))
CENTER = (0, 0, 0)


def expand(weights, rank):
    values = [float(entry) for entry in list(weights)]
    return jnp.asarray(values, jnp.float32).reshape((-1,) + (1,) * rank)


def along(velocity_table, vector):
    rank = vector.ndim - 1
    total = expand(velocity_table[:, 0], rank) * vector[0]
    for direction in range(1, 3):
        total = total + expand(velocity_table[:, direction], rank) * vector[direction]
    return total


def collide(populations, phase_grad, potential_grad):
    rank = populations.ndim - 1
    flow_part = populations[:19]
    phase_part = populations[19:]
    fraction = jnp.sum(phase_part, 0)
    density = 0.2 + 0.8 * fraction
    pressure = jnp.sum(flow_part, 0)
    body_force = -fraction[None] * potential_grad
    momentum = jnp.stack(
        [jnp.sum(expand(VELOCITY[:, direction], rank) * flow_part, 0) for direction in range(3)]
    )
    velocity = (momentum + 0.5 * body_force) / density[None]
    along_flow = along(VELOCITY, velocity)
    speed_square = jnp.sum(velocity * velocity, 0)
    relax_rate = 1.1 + 0.5 * fraction
    flow_equil = expand(FLOW_WEIGHT, rank) * (
        pressure + density * (3.0 * along_flow + 4.5 * along_flow * along_flow - 1.5 * speed_square)
    )
    along_force = along(VELOCITY, body_force)
    speed_force = jnp.sum(velocity * body_force, 0)
    source = expand(FLOW_WEIGHT, rank) * (
        3.0 * (along_force - speed_force) + 9.0 * along_flow * along_force
    )
    flow_post = (
        flow_part - relax_rate * (flow_part - flow_equil) + (1.0 - 0.5 * relax_rate) * source
    )
    magnitude = jnp.sqrt(jnp.sum(phase_grad * phase_grad, 0) + 0.0625)
    normal = phase_grad / magnitude
    along_normal = along(VELOCITY[:7], normal)
    phase_equil = expand(PHASE_WEIGHT, rank) * (
        fraction * (1.0 + 4.0 * along_flow[:7])
        + 4.0 * SHARPEN * fraction * (1.0 - fraction) * along_normal
    )
    phase_post = phase_part - PHASE_RATE * (phase_part - phase_equil)
    return jnp.concatenate([flow_post, phase_post], 0)


def wall_zero(extended, width, vertical_dim):
    height = extended.shape[vertical_dim]
    layer_index = lax.broadcasted_iota(jnp.int32, (height,), 0)
    position = lax.axis_index("gz")
    bricks = lax.axis_size("gz")
    bottom_wall = jnp.logical_and(layer_index < width, position == 0)
    top_wall = jnp.logical_and(layer_index >= height - width, position == bricks - 1)
    inside = jnp.where(jnp.logical_or(bottom_wall, top_wall), 0.0, 1.0).astype(extended.dtype)
    extent = [1] * extended.ndim
    extent[vertical_dim] = height
    return extended * inside.reshape(extent)


def offset_view(extended, margin, offset, extent):
    return extended[
        ...,
        margin + offset[0] : margin + offset[0] + extent[0],
        margin + offset[1] : margin + offset[1] + extent[1],
        margin + offset[2] : margin + offset[2] + extent[2],
    ]


def negate(offset):
    return tuple((-entry for entry in offset))


def gradient(extended, margin, extent):
    return jnp.stack(
        [
            (
                offset_view(extended, margin, unit, extent)
                - offset_view(extended, margin, negate(unit), extent)
            )
            * 0.5
            for unit in UNITS
        ]
    )


def laplace(extended, margin, extent):
    total = -6.0 * offset_view(extended, margin, CENTER, extent)
    for unit in UNITS:
        total = (
            total
            + offset_view(extended, margin, unit, extent)
            + offset_view(extended, margin, negate(unit), extent)
        )
    return total


def spread(extended, margin, extent):
    total = jnp.zeros(extent, jnp.float32)
    for direction in range(3):
        unit = UNITS[direction]
        total = (
            total
            + (
                offset_view(extended[direction], margin, negate(unit), extent)
                - offset_view(extended[direction], margin, unit, extent)
            )
            * 0.5
        )
    return total


def well_term(fraction):
    return 4.0 * WELL_DEPTH * fraction * (fraction - 1.0) * (fraction - 0.5)


def well_slope(fraction):
    return 4.0 * WELL_DEPTH * (3.0 * fraction * fraction - 3.0 * fraction + 0.5)


def bounce(arrived, adjoint):
    height = adjoint.shape[1]
    layer_index = lax.broadcasted_iota(jnp.int32, (height,), 0)
    position = lax.axis_index("gz")
    bricks = lax.axis_size("gz")
    bottom_wall = jnp.logical_and(layer_index == 0, position == 0).reshape((1, height, 1, 1))
    top_wall = jnp.logical_and(layer_index == height - 1, position == bricks - 1).reshape(
        (1, height, 1, 1)
    )
    rising = jnp.asarray((VELOCITY_ALL[:, 0] == 1).reshape((26, 1, 1, 1)))
    falling = jnp.asarray((VELOCITY_ALL[:, 0] == -1).reshape((26, 1, 1, 1)))
    reflect = jnp.logical_or(
        jnp.logical_and(rising, top_wall), jnp.logical_and(falling, bottom_wall)
    )
    flipped = jnp.stack([adjoint[mirror] for mirror in OPPOSITE_ALL])
    return jnp.where(reflect, flipped, arrived)


def extended_2(shard, sides, width):
    for axis, dim in sides:
        count, length = (lax.axis_size(axis), shard.shape[dim])
        last = lax.slice_in_dim(shard, length - width, length, axis=dim)
        first = lax.slice_in_dim(shard, 0, width, axis=dim)
        if axis == "gz" and count == 2:
            lower = lax.axis_index(axis) == 0
            swapped = lax.ppermute(jnp.where(lower, last, first), axis, [(0, 1), (1, 0)])
            before, after = swapped, swapped
        else:
            up = [(i, (i + 1) % count) for i in range(count)]
            down = [(j, i) for i, j in up]
            before = lax.ppermute(last, axis, up)
            after = lax.ppermute(first, axis, down)
        shard = jnp.concatenate([before, shard, after], axis=dim)
    return shard


def extended_mixed(wide, narrow, width):
    count = wide.shape[0]
    has_narrow = narrow is not None
    shard = jnp.concatenate([wide, narrow], 0) if has_narrow else wide
    for axis, dim in SIDES:
        length = shard.shape[dim]

        def planes(side):
            index = [i if side == 1 else length - 1 - i for i in range(width)]
            layers = [lax.slice_in_dim(shard[:count], i, i + 1, axis=dim) for i in index]
            if has_narrow:
                layers.append(lax.slice_in_dim(shard[count:], index[0], index[0] + 1, axis=dim))
            return jnp.concatenate(layers, 0)

        def unpack(got, side):
            layers = [got[i * count : (i + 1) * count] for i in range(width)]
            ordered = layers if side == 1 else layers[::-1]
            slab = jnp.concatenate(ordered, dim)
            if not has_narrow:
                return slab
            near = got[width * count :]
            pad = [(0, 0)] * near.ndim
            pad[dim] = (0, width - 1) if side == 1 else (width - 1, 0)
            return jnp.concatenate([slab, jnp.pad(near, pad)], 0)

        size = lax.axis_size(axis)
        if axis == "gz" and size == 2:
            last = lax.slice_in_dim(shard, length - width, length, axis=dim)
            first = lax.slice_in_dim(shard, 0, width, axis=dim)
            lower = lax.axis_index(axis) == 0
            before = after = lax.ppermute(jnp.where(lower, last, first), axis, [(0, 1), (1, 0)])
        else:
            up = [(i, (i + 1) % size) for i in range(size)]
            down = [(j, i) for i, j in up]
            before = unpack(lax.ppermute(planes(-1), axis, up), -1)
            after = unpack(lax.ppermute(planes(1), axis, down), 1)
        shard = jnp.concatenate([before, shard, after], axis=dim)
    return shard


SIDES = (("gy", 3), ("gx", 2), ("gz", 1))


def stream_adjoint(extended, margin, adjoint, extent):
    arrived = jnp.stack(
        [
            offset_view(
                extended[member],
                margin,
                tuple((int(entry) for entry in VELOCITY_ALL[member])),
                extent,
            )
            for member in range(26)
        ]
    )
    return bounce(arrived, adjoint)


def phase_fields(fraction_ext, extent):
    box = tuple(n + 2 for n in extent)
    inner = fraction_ext[1:-1, 1:-1, 1:-1]
    potential_box = wall_zero(well_term(inner) - STIFFNESS * laplace(fraction_ext, 1, box), 1, 0)
    return gradient(fraction_ext, 2, extent), gradient(potential_box, 1, extent)


def collide_adjoint(populations, phase_grad, potential_grad, arrived):
    pullback = jax.vjp(collide, populations, phase_grad, potential_grad)[1]
    return pullback(arrived)


def phase_adjoint(fraction, adjoint_pgrad, adjoint_mgrad, extra, extent):
    combined = jnp.concatenate([adjoint_pgrad, adjoint_mgrad, extra], 0)
    extended = extended_2(combined, SIDES, 2)
    combined_ext = wall_zero(extended[:6], 2, 1)
    box = tuple(n + 2 for n in extent)
    mu_box = wall_zero(spread(combined_ext[3:6], 1, box), 1, 0)
    adjoint_phase = (
        well_slope(fraction) * mu_box[1:-1, 1:-1, 1:-1]
        - STIFFNESS * laplace(mu_box, 1, extent)
        + spread(combined_ext[:3], 2, extent)
    )
    return adjoint_phase, extended[6:]


def face_shifts(values):
    shifted = {}
    for axis, dim in SIDES:
        count, length = (lax.axis_size(axis), values.shape[dim - 1])
        last = lax.slice_in_dim(values, length - 1, length, axis=dim - 1)
        first = lax.slice_in_dim(values, 0, 1, axis=dim - 1)
        if axis == "gz" and count == 2:
            lower = lax.axis_index(axis) == 0
            swapped = lax.ppermute(jnp.where(lower, last, first), axis, [(0, 1), (1, 0)])
            before, after = swapped, swapped
        else:
            up = [(i, (i + 1) % count) for i in range(count)]
            down = [(j, i) for i, j in up]
            before = lax.ppermute(last, axis, up)
            after = lax.ppermute(first, axis, down)
        plus = tuple(1 if a == dim - 1 else 0 for a in range(3))
        shifted[plus] = shift_along(values, after, dim - 1, 1)
        shifted[negate(plus)] = shift_along(values, before, dim - 1, -1)
    return shifted


def shift_along(values, halo, axis, sign):
    length = values.shape[axis]
    if sign == 1:
        return jnp.concatenate([lax.slice_in_dim(values, 1, length, axis=axis), halo], axis)
    return jnp.concatenate([halo, lax.slice_in_dim(values, 0, length - 1, axis=axis)], axis)


def finish(adjoint_pops, adjoint_phase):
    return jnp.concatenate([adjoint_pops[:19], adjoint_pops[19:] + adjoint_phase[None]], 0)


def phase_adjoint_wide(fraction_box, adjoint_pgrad, adjoint_mgrad, extra, extent):
    combined = jnp.concatenate([adjoint_pgrad, adjoint_mgrad, extra], 0)
    extended = extended_mixed(combined[:6], extra, 3)
    combined_ext = wall_zero(extended[:6], 3, 1)
    box1 = tuple(n + 2 for n in extent)
    box2 = tuple(n + 4 for n in extent)
    mu_box = wall_zero(spread(combined_ext[3:6], 1, box2), 2, 0)
    adjoint_phase = (
        well_slope(fraction_box) * mu_box[1:-1, 1:-1, 1:-1]
        - STIFFNESS * laplace(mu_box, 1, box1)
        + spread(combined_ext[:3], 2, box1)
    )
    return adjoint_phase, extended[6:]


def local(populations0, populations1, cotangent):
    states = [populations1.astype(jnp.float32), populations0.astype(jnp.float32)]
    fractions = jnp.stack([jnp.sum(state[19:], 0) for state in states])
    extent = fractions.shape[1:]
    first_ext = extended_mixed(fractions, cotangent, 2)
    fraction_ext = wall_zero(first_ext[:2], 2, 1)
    fields1 = phase_fields(fraction_ext[0], extent)
    fields0 = phase_fields(fraction_ext[1], extent)

    arrived = stream_adjoint(first_ext[2:], 2, cotangent, extent)
    pops, pgrad_adj, mgrad_adj = collide_adjoint(states[0], *fields1, arrived)
    phase_box, pops_ext = phase_adjoint_wide(
        fraction_ext[0, 1:-1, 1:-1, 1:-1], pgrad_adj, mgrad_adj, pops, extent
    )
    adjoint1 = finish(pops, phase_box[1:-1, 1:-1, 1:-1])

    arrived = []
    for member in range(26):
        velocity = tuple(int(entry) for entry in VELOCITY_ALL[member])
        values = offset_view(pops_ext[member], 3, velocity, extent)
        if member >= 19:
            values = values + offset_view(phase_box, 1, velocity, extent)
        arrived.append(values)
    arrived = bounce(jnp.stack(arrived), adjoint1)
    pops, pgrad_adj, mgrad_adj = collide_adjoint(states[1], *fields0, arrived)
    adjoint_phase, _ = phase_adjoint(fractions[1], pgrad_adj, mgrad_adj, pops[:0], extent)
    return finish(pops, adjoint_phase)


def solution(mesh):
    return jax.shard_map(
        local,
        mesh=mesh,
        in_specs=(P(None, "gz", "gx", "gy"), P(None, "gz", "gx", "gy"), P(None, "gz", "gx", "gy")),
        out_specs=P(None, "gz", "gx", "gy"),
        check_vma=False,
    )
```

```python
import jax
import jax.numpy as jnp
import numpy as np
from jax import lax
from jax.sharding import PartitionSpec as P

VELOCITY = np.array(
    [
        [0, 0, 0],
        [1, 0, 0],
        [-1, 0, 0],
        [0, 1, 0],
        [0, -1, 0],
        [0, 0, 1],
        [0, 0, -1],
        [1, 1, 0],
        [-1, -1, 0],
        [1, -1, 0],
        [-1, 1, 0],
        [1, 0, 1],
        [-1, 0, -1],
        [1, 0, -1],
        [-1, 0, 1],
        [0, 1, 1],
        [0, -1, -1],
        [0, 1, -1],
        [0, -1, 1],
    ]
)
OPPOSITE = [0, 2, 1, 4, 3, 6, 5, 8, 7, 10, 9, 12, 11, 14, 13, 16, 15, 18, 17]
FLOW_WEIGHT = [1.0 / 3.0] + [1.0 / 18.0] * 6 + [1.0 / 36.0] * 12
PHASE_WEIGHT = [0.25] + [0.125] * 6
VELOCITY_ALL = np.concatenate([VELOCITY, VELOCITY[:7]], 0)
OPPOSITE_ALL = OPPOSITE + [19 + mirror for mirror in OPPOSITE[:7]]
WELL_DEPTH = 0.3
STIFFNESS = 0.6
SHARPEN = 0.3
PHASE_RATE = 1.4
UNITS = ((1, 0, 0), (0, 1, 0), (0, 0, 1))
CENTER = (0, 0, 0)


def expand(weights, rank):
    values = [float(entry) for entry in list(weights)]
    return jnp.asarray(values, jnp.float32).reshape((-1,) + (1,) * rank)


def along(velocity_table, vector):
    rank = vector.ndim - 1
    total = expand(velocity_table[:, 0], rank) * vector[0]
    for direction in range(1, 3):
        total = total + expand(velocity_table[:, direction], rank) * vector[direction]
    return total


def collide(populations, phase_grad, potential_grad):
    rank = populations.ndim - 1
    flow_part = populations[:19]
    phase_part = populations[19:]
    fraction = jnp.sum(phase_part, 0)
    density = 0.2 + 0.8 * fraction
    pressure = jnp.sum(flow_part, 0)
    body_force = -fraction[None] * potential_grad
    momentum = jnp.stack(
        [jnp.sum(expand(VELOCITY[:, direction], rank) * flow_part, 0) for direction in range(3)]
    )
    velocity = (momentum + 0.5 * body_force) / density[None]
    along_flow = along(VELOCITY, velocity)
    speed_square = jnp.sum(velocity * velocity, 0)
    relax_rate = 1.1 + 0.5 * fraction
    flow_equil = expand(FLOW_WEIGHT, rank) * (
        pressure + density * (3.0 * along_flow + 4.5 * along_flow * along_flow - 1.5 * speed_square)
    )
    along_force = along(VELOCITY, body_force)
    speed_force = jnp.sum(velocity * body_force, 0)
    source = expand(FLOW_WEIGHT, rank) * (
        3.0 * (along_force - speed_force) + 9.0 * along_flow * along_force
    )
    flow_post = (
        flow_part - relax_rate * (flow_part - flow_equil) + (1.0 - 0.5 * relax_rate) * source
    )
    magnitude = jnp.sqrt(jnp.sum(phase_grad * phase_grad, 0) + 0.0625)
    normal = phase_grad / magnitude
    along_normal = along(VELOCITY[:7], normal)
    phase_equil = expand(PHASE_WEIGHT, rank) * (
        fraction * (1.0 + 4.0 * along_flow[:7])
        + 4.0 * SHARPEN * fraction * (1.0 - fraction) * along_normal
    )
    phase_post = phase_part - PHASE_RATE * (phase_part - phase_equil)
    return jnp.concatenate([flow_post, phase_post], 0)


def wall_zero(extended, width, vertical_dim):
    height = extended.shape[vertical_dim]
    layer_index = lax.broadcasted_iota(jnp.int32, (height,), 0)
    position = lax.axis_index("gz")
    bricks = lax.axis_size("gz")
    bottom_wall = jnp.logical_and(layer_index < width, position == 0)
    top_wall = jnp.logical_and(layer_index >= height - width, position == bricks - 1)
    inside = jnp.where(jnp.logical_or(bottom_wall, top_wall), 0.0, 1.0).astype(extended.dtype)
    extent = [1] * extended.ndim
    extent[vertical_dim] = height
    return extended * inside.reshape(extent)


def offset_view(extended, margin, offset, extent):
    return extended[
        ...,
        margin + offset[0] : margin + offset[0] + extent[0],
        margin + offset[1] : margin + offset[1] + extent[1],
        margin + offset[2] : margin + offset[2] + extent[2],
    ]


def negate(offset):
    return tuple((-entry for entry in offset))


def gradient(extended, margin, extent):
    return jnp.stack(
        [
            (
                offset_view(extended, margin, unit, extent)
                - offset_view(extended, margin, negate(unit), extent)
            )
            * 0.5
            for unit in UNITS
        ]
    )


def laplace(extended, margin, extent):
    total = -6.0 * offset_view(extended, margin, CENTER, extent)
    for unit in UNITS:
        total = (
            total
            + offset_view(extended, margin, unit, extent)
            + offset_view(extended, margin, negate(unit), extent)
        )
    return total


def spread(extended, margin, extent):
    total = jnp.zeros(extent, jnp.float32)
    for direction in range(3):
        unit = UNITS[direction]
        total = (
            total
            + (
                offset_view(extended[direction], margin, negate(unit), extent)
                - offset_view(extended[direction], margin, unit, extent)
            )
            * 0.5
        )
    return total


def well_term(fraction):
    return 4.0 * WELL_DEPTH * fraction * (fraction - 1.0) * (fraction - 0.5)


def well_slope(fraction):
    return 4.0 * WELL_DEPTH * (3.0 * fraction * fraction - 3.0 * fraction + 0.5)


def bounce(arrived, adjoint):
    height = adjoint.shape[1]
    layer_index = lax.broadcasted_iota(jnp.int32, (height,), 0)
    position = lax.axis_index("gz")
    bricks = lax.axis_size("gz")
    bottom_wall = jnp.logical_and(layer_index == 0, position == 0).reshape((1, height, 1, 1))
    top_wall = jnp.logical_and(layer_index == height - 1, position == bricks - 1).reshape(
        (1, height, 1, 1)
    )
    rising = jnp.asarray((VELOCITY_ALL[:, 0] == 1).reshape((26, 1, 1, 1)))
    falling = jnp.asarray((VELOCITY_ALL[:, 0] == -1).reshape((26, 1, 1, 1)))
    reflect = jnp.logical_or(
        jnp.logical_and(rising, top_wall), jnp.logical_and(falling, bottom_wall)
    )
    flipped = jnp.stack([adjoint[mirror] for mirror in OPPOSITE_ALL])
    return jnp.where(reflect, flipped, arrived)


def extended_2(shard, sides, width):
    for axis, dim in sides:
        count, length = (lax.axis_size(axis), shard.shape[dim])
        last = lax.slice_in_dim(shard, length - width, length, axis=dim)
        first = lax.slice_in_dim(shard, 0, width, axis=dim)
        if axis == "gz" and count == 2:
            lower = lax.axis_index(axis) == 0
            swapped = lax.ppermute(jnp.where(lower, last, first), axis, [(0, 1), (1, 0)])
            before, after = swapped, swapped
        else:
            up = [(i, (i + 1) % count) for i in range(count)]
            down = [(j, i) for i, j in up]
            before = lax.ppermute(last, axis, up)
            after = lax.ppermute(first, axis, down)
        shard = jnp.concatenate([before, shard, after], axis=dim)
    return shard


SIDES = (("gy", 3), ("gx", 2), ("gz", 1))


def wall_layers(height):
    layer_index = lax.broadcasted_iota(jnp.int32, (height, 1, 1), 0)
    position = lax.axis_index("gz")
    bricks = lax.axis_size("gz")
    bottom = jnp.logical_and(layer_index == 0, position == 0)
    top = jnp.logical_and(layer_index == height - 1, position == bricks - 1)
    return bottom, top


def bounced(member, view, adjoint, walls):
    rising = int(VELOCITY_ALL[member][0])
    if rising == 0:
        return view
    wall = walls[1] if rising == 1 else walls[0]
    return jnp.where(wall, adjoint[OPPOSITE_ALL[member]], view)


def stream_adjoint(extended, margin, adjoint, extent):
    walls = wall_layers(extent[0])
    arrived = []
    for member in range(26):
        velocity = tuple((int(entry) for entry in VELOCITY_ALL[member]))
        view = offset_view(extended[member], margin, velocity, extent)
        arrived.append(bounced(member, view, adjoint, walls))
    return jnp.stack(arrived)


def phase_fields(fraction_ext, extent):
    box = tuple(n + 2 for n in extent)
    inner = fraction_ext[1:-1, 1:-1, 1:-1]
    potential_box = wall_zero(well_term(inner) - STIFFNESS * laplace(fraction_ext, 1, box), 1, 0)
    return gradient(fraction_ext, 2, extent), gradient(potential_box, 1, extent)


def collide_adjoint(populations, phase_grad, potential_grad, arrived):
    pullback = jax.vjp(collide, populations, phase_grad, potential_grad)[1]
    return pullback(arrived)


def phase_adjoint(fraction, adjoint_pgrad, adjoint_mgrad, extra, extent):
    combined = jnp.concatenate([adjoint_pgrad, adjoint_mgrad, extra], 0)
    extended = extended_2(combined, SIDES, 2)
    combined_ext = wall_zero(extended[:6], 2, 1)
    box = tuple(n + 2 for n in extent)
    mu_box = wall_zero(spread(combined_ext[3:6], 1, box), 1, 0)
    adjoint_phase = (
        well_slope(fraction) * mu_box[1:-1, 1:-1, 1:-1]
        - STIFFNESS * laplace(mu_box, 1, extent)
        + spread(combined_ext[:3], 2, extent)
    )
    return adjoint_phase, extended[6:]


def face_shifts(values):
    shifted = {}
    for axis, dim in SIDES:
        count, length = (lax.axis_size(axis), values.shape[dim - 1])
        last = lax.slice_in_dim(values, length - 1, length, axis=dim - 1)
        first = lax.slice_in_dim(values, 0, 1, axis=dim - 1)
        if axis == "gz" and count == 2:
            lower = lax.axis_index(axis) == 0
            swapped = lax.ppermute(jnp.where(lower, last, first), axis, [(0, 1), (1, 0)])
            before, after = swapped, swapped
        else:
            up = [(i, (i + 1) % count) for i in range(count)]
            down = [(j, i) for i, j in up]
            before = lax.ppermute(last, axis, up)
            after = lax.ppermute(first, axis, down)
        plus = tuple(1 if a == dim - 1 else 0 for a in range(3))
        shifted[plus] = shift_along(values, after, dim - 1, 1)
        shifted[negate(plus)] = shift_along(values, before, dim - 1, -1)
    return shifted


def shift_along(values, halo, axis, sign):
    length = values.shape[axis]
    if sign == 1:
        return jnp.concatenate([lax.slice_in_dim(values, 1, length, axis=axis), halo], axis)
    return jnp.concatenate([halo, lax.slice_in_dim(values, 0, length - 1, axis=axis)], axis)


def finish(adjoint_pops, adjoint_phase):
    return jnp.concatenate([adjoint_pops[:19], adjoint_pops[19:] + adjoint_phase[None]], 0)


def phase_adjoint_wide(fraction_box, adjoint_pgrad, adjoint_mgrad, extra, extent):
    combined = jnp.concatenate([adjoint_pgrad, adjoint_mgrad, extra], 0)
    extended = extended_2(combined, SIDES, 3)
    combined_ext = wall_zero(extended[:6], 3, 1)
    box1 = tuple(n + 2 for n in extent)
    box2 = tuple(n + 4 for n in extent)
    mu_box = wall_zero(spread(combined_ext[3:6], 1, box2), 2, 0)
    adjoint_phase = (
        well_slope(fraction_box) * mu_box[1:-1, 1:-1, 1:-1]
        - STIFFNESS * laplace(mu_box, 1, box1)
        + spread(combined_ext[:3], 2, box1)
    )
    return adjoint_phase, extended[6:]


def local(populations0, populations1, cotangent):
    states = [populations1.astype(jnp.float32), populations0.astype(jnp.float32)]
    fractions = jnp.stack([jnp.sum(state[19:], 0) for state in states])
    extent = fractions.shape[1:]
    first_ext = extended_2(jnp.concatenate([fractions, cotangent], 0), SIDES, 2)
    fraction_ext = wall_zero(first_ext[:2], 2, 1)
    fields1 = phase_fields(fraction_ext[0], extent)
    fields0 = phase_fields(fraction_ext[1], extent)

    arrived = stream_adjoint(first_ext[2:], 2, cotangent, extent)
    pops, pgrad_adj, mgrad_adj = collide_adjoint(states[0], *fields1, arrived)
    phase_box, pops_ext = phase_adjoint_wide(
        fraction_ext[0, 1:-1, 1:-1, 1:-1], pgrad_adj, mgrad_adj, pops, extent
    )
    adjoint1 = finish(pops, phase_box[1:-1, 1:-1, 1:-1])

    walls = wall_layers(extent[0])
    arrived = []
    for member in range(26):
        velocity = tuple(int(entry) for entry in VELOCITY_ALL[member])
        values = offset_view(pops_ext[member], 3, velocity, extent)
        if member >= 19:
            values = values + offset_view(phase_box, 1, velocity, extent)
        arrived.append(bounced(member, values, adjoint1, walls))
    arrived = jnp.stack(arrived)
    pops, pgrad_adj, mgrad_adj = collide_adjoint(states[1], *fields0, arrived)
    adjoint_phase, _ = phase_adjoint(fractions[1], pgrad_adj, mgrad_adj, pops[:0], extent)
    return finish(pops, adjoint_phase)


def solution(mesh):
    return jax.shard_map(
        local,
        mesh=mesh,
        in_specs=(P(None, "gz", "gx", "gy"), P(None, "gz", "gx", "gy"), P(None, "gz", "gx", "gy")),
        out_specs=P(None, "gz", "gx", "gy"),
        check_vma=False,
    )
```

```python
import jax
import jax.numpy as jnp
import numpy as np
from jax import lax
from jax.sharding import PartitionSpec as P

VELOCITY = np.array(
    [
        [0, 0, 0],
        [1, 0, 0],
        [-1, 0, 0],
        [0, 1, 0],
        [0, -1, 0],
        [0, 0, 1],
        [0, 0, -1],
        [1, 1, 0],
        [-1, -1, 0],
        [1, -1, 0],
        [-1, 1, 0],
        [1, 0, 1],
        [-1, 0, -1],
        [1, 0, -1],
        [-1, 0, 1],
        [0, 1, 1],
        [0, -1, -1],
        [0, 1, -1],
        [0, -1, 1],
    ]
)
OPPOSITE = [0, 2, 1, 4, 3, 6, 5, 8, 7, 10, 9, 12, 11, 14, 13, 16, 15, 18, 17]
FLOW_WEIGHT = [1.0 / 3.0] + [1.0 / 18.0] * 6 + [1.0 / 36.0] * 12
PHASE_WEIGHT = [0.25] + [0.125] * 6
VELOCITY_ALL = np.concatenate([VELOCITY, VELOCITY[:7]], 0)
OPPOSITE_ALL = OPPOSITE + [19 + mirror for mirror in OPPOSITE[:7]]
WELL_DEPTH = 0.3
STIFFNESS = 0.6
SHARPEN = 0.3
PHASE_RATE = 1.4
UNITS = ((1, 0, 0), (0, 1, 0), (0, 0, 1))
CENTER = (0, 0, 0)


def expand(weights, rank):
    values = [float(entry) for entry in list(weights)]
    return jnp.asarray(values, jnp.float32).reshape((-1,) + (1,) * rank)


def along(velocity_table, vector):
    rank = vector.ndim - 1
    total = expand(velocity_table[:, 0], rank) * vector[0]
    for direction in range(1, 3):
        total = total + expand(velocity_table[:, direction], rank) * vector[direction]
    return total


def collide(populations, phase_grad, potential_grad):
    rank = populations.ndim - 1
    flow_part = populations[:19]
    phase_part = populations[19:]
    fraction = jnp.sum(phase_part, 0)
    density = 0.2 + 0.8 * fraction
    pressure = jnp.sum(flow_part, 0)
    body_force = -fraction[None] * potential_grad
    momentum = jnp.stack(
        [jnp.sum(expand(VELOCITY[:, direction], rank) * flow_part, 0) for direction in range(3)]
    )
    velocity = (momentum + 0.5 * body_force) / density[None]
    along_flow = along(VELOCITY, velocity)
    speed_square = jnp.sum(velocity * velocity, 0)
    relax_rate = 1.1 + 0.5 * fraction
    flow_equil = expand(FLOW_WEIGHT, rank) * (
        pressure + density * (3.0 * along_flow + 4.5 * along_flow * along_flow - 1.5 * speed_square)
    )
    along_force = along(VELOCITY, body_force)
    speed_force = jnp.sum(velocity * body_force, 0)
    source = expand(FLOW_WEIGHT, rank) * (
        3.0 * (along_force - speed_force) + 9.0 * along_flow * along_force
    )
    flow_post = (
        flow_part - relax_rate * (flow_part - flow_equil) + (1.0 - 0.5 * relax_rate) * source
    )
    magnitude = jnp.sqrt(jnp.sum(phase_grad * phase_grad, 0) + 0.0625)
    normal = phase_grad / magnitude
    along_normal = along(VELOCITY[:7], normal)
    phase_equil = expand(PHASE_WEIGHT, rank) * (
        fraction * (1.0 + 4.0 * along_flow[:7])
        + 4.0 * SHARPEN * fraction * (1.0 - fraction) * along_normal
    )
    phase_post = phase_part - PHASE_RATE * (phase_part - phase_equil)
    return jnp.concatenate([flow_post, phase_post], 0)


def wall_zero(extended, width, vertical_dim):
    height = extended.shape[vertical_dim]
    layer_index = lax.broadcasted_iota(jnp.int32, (height,), 0)
    position = lax.axis_index("gz")
    bricks = lax.axis_size("gz")
    bottom_wall = jnp.logical_and(layer_index < width, position == 0)
    top_wall = jnp.logical_and(layer_index >= height - width, position == bricks - 1)
    inside = jnp.where(jnp.logical_or(bottom_wall, top_wall), 0.0, 1.0).astype(extended.dtype)
    extent = [1] * extended.ndim
    extent[vertical_dim] = height
    return extended * inside.reshape(extent)


def offset_view(extended, margin, offset, extent):
    return extended[
        ...,
        margin + offset[0] : margin + offset[0] + extent[0],
        margin + offset[1] : margin + offset[1] + extent[1],
        margin + offset[2] : margin + offset[2] + extent[2],
    ]


def negate(offset):
    return tuple((-entry for entry in offset))


def gradient(extended, margin, extent):
    return jnp.stack(
        [
            (
                offset_view(extended, margin, unit, extent)
                - offset_view(extended, margin, negate(unit), extent)
            )
            * 0.5
            for unit in UNITS
        ]
    )


def laplace(extended, margin, extent):
    total = -6.0 * offset_view(extended, margin, CENTER, extent)
    for unit in UNITS:
        total = (
            total
            + offset_view(extended, margin, unit, extent)
            + offset_view(extended, margin, negate(unit), extent)
        )
    return total


def spread(extended, margin, extent):
    total = jnp.zeros(extent, jnp.float32)
    for direction in range(3):
        unit = UNITS[direction]
        total = (
            total
            + (
                offset_view(extended[direction], margin, negate(unit), extent)
                - offset_view(extended[direction], margin, unit, extent)
            )
            * 0.5
        )
    return total


def well_term(fraction):
    return 4.0 * WELL_DEPTH * fraction * (fraction - 1.0) * (fraction - 0.5)


def well_slope(fraction):
    return 4.0 * WELL_DEPTH * (3.0 * fraction * fraction - 3.0 * fraction + 0.5)


def bounce(arrived, adjoint):
    height = adjoint.shape[1]
    layer_index = lax.broadcasted_iota(jnp.int32, (height,), 0)
    position = lax.axis_index("gz")
    bricks = lax.axis_size("gz")
    bottom_wall = jnp.logical_and(layer_index == 0, position == 0).reshape((1, height, 1, 1))
    top_wall = jnp.logical_and(layer_index == height - 1, position == bricks - 1).reshape(
        (1, height, 1, 1)
    )
    rising = jnp.asarray((VELOCITY_ALL[:, 0] == 1).reshape((26, 1, 1, 1)))
    falling = jnp.asarray((VELOCITY_ALL[:, 0] == -1).reshape((26, 1, 1, 1)))
    reflect = jnp.logical_or(
        jnp.logical_and(rising, top_wall), jnp.logical_and(falling, bottom_wall)
    )
    flipped = jnp.stack([adjoint[mirror] for mirror in OPPOSITE_ALL])
    return jnp.where(reflect, flipped, arrived)


def extended_2(shard, sides, width):
    for axis, dim in sides:
        count, length = (lax.axis_size(axis), shard.shape[dim])
        last = lax.slice_in_dim(shard, length - width, length, axis=dim)
        first = lax.slice_in_dim(shard, 0, width, axis=dim)
        if axis == "gz" and count == 2:
            lower = lax.axis_index(axis) == 0
            swapped = lax.ppermute(jnp.where(lower, last, first), axis, [(0, 1), (1, 0)])
            before, after = swapped, swapped
        else:
            up = [(i, (i + 1) % count) for i in range(count)]
            down = [(j, i) for i, j in up]
            before = lax.ppermute(last, axis, up)
            after = lax.ppermute(first, axis, down)
        shard = jnp.concatenate([before, shard, after], axis=dim)
    return shard


SIDES = (("gy", 3), ("gx", 2), ("gz", 1))


def wall_layers(height):
    layer_index = lax.broadcasted_iota(jnp.int32, (height, 1, 1), 0)
    position = lax.axis_index("gz")
    bricks = lax.axis_size("gz")
    bottom = jnp.logical_and(layer_index == 0, position == 0)
    top = jnp.logical_and(layer_index == height - 1, position == bricks - 1)
    return bottom, top


def bounced(member, view, adjoint, walls):
    rising = int(VELOCITY_ALL[member][0])
    if rising == 0:
        return view
    wall = walls[1] if rising == 1 else walls[0]
    return jnp.where(wall, adjoint[OPPOSITE_ALL[member]], view)


def stream_adjoint(extended, margin, adjoint, extent):
    walls = wall_layers(extent[0])
    arrived = []
    for member in range(26):
        velocity = tuple((int(entry) for entry in VELOCITY_ALL[member]))
        view = offset_view(extended[member], margin, velocity, extent)
        arrived.append(bounced(member, view, adjoint, walls))
    return jnp.stack(arrived)


def phase_fields(fraction_ext, extent):
    box = tuple(n + 2 for n in extent)
    inner = fraction_ext[1:-1, 1:-1, 1:-1]
    potential_box = wall_zero(well_term(inner) - STIFFNESS * laplace(fraction_ext, 1, box), 1, 0)
    return gradient(fraction_ext, 2, extent), gradient(potential_box, 1, extent)


def collide_adjoint(populations, phase_grad, potential_grad, arrived):
    pullback = jax.vjp(collide, populations, phase_grad, potential_grad)[1]
    return pullback(arrived)


def phase_adjoint(fraction, adjoint_pgrad, adjoint_mgrad, extra, extent):
    combined = jnp.concatenate([adjoint_pgrad, adjoint_mgrad, extra], 0)
    extended = extended_2(combined, SIDES, 2)
    combined_ext = wall_zero(extended[:6], 2, 1)
    box = tuple(n + 2 for n in extent)
    mu_box = wall_zero(spread(combined_ext[3:6], 1, box), 1, 0)
    adjoint_phase = (
        well_slope(fraction) * mu_box[1:-1, 1:-1, 1:-1]
        - STIFFNESS * laplace(mu_box, 1, extent)
        + spread(combined_ext[:3], 2, extent)
    )
    return adjoint_phase, extended[6:]


def face_shifts(values):
    shifted = {}
    for axis, dim in SIDES:
        count, length = (lax.axis_size(axis), values.shape[dim - 1])
        last = lax.slice_in_dim(values, length - 1, length, axis=dim - 1)
        first = lax.slice_in_dim(values, 0, 1, axis=dim - 1)
        if axis == "gz" and count == 2:
            lower = lax.axis_index(axis) == 0
            swapped = lax.ppermute(jnp.where(lower, last, first), axis, [(0, 1), (1, 0)])
            before, after = swapped, swapped
        else:
            up = [(i, (i + 1) % count) for i in range(count)]
            down = [(j, i) for i, j in up]
            before = lax.ppermute(last, axis, up)
            after = lax.ppermute(first, axis, down)
        plus = tuple(1 if a == dim - 1 else 0 for a in range(3))
        shifted[plus] = shift_along(values, after, dim - 1, 1)
        shifted[negate(plus)] = shift_along(values, before, dim - 1, -1)
    return shifted


def shift_along(values, halo, axis, sign):
    length = values.shape[axis]
    if sign == 1:
        return jnp.concatenate([lax.slice_in_dim(values, 1, length, axis=axis), halo], axis)
    return jnp.concatenate([halo, lax.slice_in_dim(values, 0, length - 1, axis=axis)], axis)


def finish(adjoint_pops, adjoint_phase):
    return jnp.concatenate([adjoint_pops[:19], adjoint_pops[19:] + adjoint_phase[None]], 0)


def phase_adjoint_wide(fraction_box, adjoint_pgrad, adjoint_mgrad, extra, extent):
    combined = jnp.concatenate([adjoint_pgrad, adjoint_mgrad, extra], 0)
    extended = extended_2(combined, (SIDES[1], SIDES[0], SIDES[2]), 3)
    combined_ext = wall_zero(extended[:6], 3, 1)
    box1 = tuple(n + 2 for n in extent)
    box2 = tuple(n + 4 for n in extent)
    mu_box = wall_zero(spread(combined_ext[3:6], 1, box2), 2, 0)
    adjoint_phase = (
        well_slope(fraction_box) * mu_box[1:-1, 1:-1, 1:-1]
        - STIFFNESS * laplace(mu_box, 1, box1)
        + spread(combined_ext[:3], 2, box1)
    )
    return adjoint_phase, extended[6:]


def local(populations0, populations1, cotangent):
    states = [populations1.astype(jnp.float32), populations0.astype(jnp.float32)]
    fractions = jnp.stack([jnp.sum(state[19:], 0) for state in states])
    extent = fractions.shape[1:]
    first_ext = extended_2(jnp.concatenate([fractions, cotangent], 0), SIDES, 2)
    fraction_ext = wall_zero(first_ext[:2], 2, 1)
    fields1 = phase_fields(fraction_ext[0], extent)
    fields0 = phase_fields(fraction_ext[1], extent)

    arrived = stream_adjoint(first_ext[2:], 2, cotangent, extent)
    pops, pgrad_adj, mgrad_adj = collide_adjoint(states[0], *fields1, arrived)
    phase_box, pops_ext = phase_adjoint_wide(
        fraction_ext[0, 1:-1, 1:-1, 1:-1], pgrad_adj, mgrad_adj, pops, extent
    )
    adjoint1 = finish(pops, phase_box[1:-1, 1:-1, 1:-1])

    walls = wall_layers(extent[0])
    arrived = []
    for member in range(26):
        velocity = tuple(int(entry) for entry in VELOCITY_ALL[member])
        values = offset_view(pops_ext[member], 3, velocity, extent)
        if member >= 19:
            values = values + offset_view(phase_box, 1, velocity, extent)
        arrived.append(bounced(member, values, adjoint1, walls))
    arrived = jnp.stack(arrived)
    pops, pgrad_adj, mgrad_adj = collide_adjoint(states[1], *fields0, arrived)
    adjoint_phase, _ = phase_adjoint(fractions[1], pgrad_adj, mgrad_adj, pops[:0], extent)
    return finish(pops, adjoint_phase)


def solution(mesh):
    return jax.shard_map(
        local,
        mesh=mesh,
        in_specs=(P(None, "gz", "gx", "gy"), P(None, "gz", "gx", "gy"), P(None, "gz", "gx", "gy")),
        out_specs=P(None, "gz", "gx", "gy"),
        check_vma=False,
    )
```

```python
import jax
import jax.numpy as jnp
import numpy as np
from jax import lax
from jax.sharding import PartitionSpec as P

VELOCITY = np.array(
    [
        [0, 0, 0],
        [1, 0, 0],
        [-1, 0, 0],
        [0, 1, 0],
        [0, -1, 0],
        [0, 0, 1],
        [0, 0, -1],
        [1, 1, 0],
        [-1, -1, 0],
        [1, -1, 0],
        [-1, 1, 0],
        [1, 0, 1],
        [-1, 0, -1],
        [1, 0, -1],
        [-1, 0, 1],
        [0, 1, 1],
        [0, -1, -1],
        [0, 1, -1],
        [0, -1, 1],
    ]
)
OPPOSITE = [0, 2, 1, 4, 3, 6, 5, 8, 7, 10, 9, 12, 11, 14, 13, 16, 15, 18, 17]
FLOW_WEIGHT = [1.0 / 3.0] + [1.0 / 18.0] * 6 + [1.0 / 36.0] * 12
PHASE_WEIGHT = [0.25] + [0.125] * 6
VELOCITY_ALL = np.concatenate([VELOCITY, VELOCITY[:7]], 0)
OPPOSITE_ALL = OPPOSITE + [19 + mirror for mirror in OPPOSITE[:7]]
WELL_DEPTH = 0.3
STIFFNESS = 0.6
SHARPEN = 0.3
PHASE_RATE = 1.4
UNITS = ((1, 0, 0), (0, 1, 0), (0, 0, 1))
CENTER = (0, 0, 0)


def expand(weights, rank):
    values = [float(entry) for entry in list(weights)]
    return jnp.asarray(values, jnp.float32).reshape((-1,) + (1,) * rank)


def along(velocity_table, vector):
    rank = vector.ndim - 1
    total = expand(velocity_table[:, 0], rank) * vector[0]
    for direction in range(1, 3):
        total = total + expand(velocity_table[:, direction], rank) * vector[direction]
    return total


def collide(populations, phase_grad, potential_grad):
    rank = populations.ndim - 1
    flow_part = populations[:19]
    phase_part = populations[19:]
    fraction = jnp.sum(phase_part, 0)
    density = 0.2 + 0.8 * fraction
    pressure = jnp.sum(flow_part, 0)
    body_force = -fraction[None] * potential_grad
    momentum = jnp.stack(
        [jnp.sum(expand(VELOCITY[:, direction], rank) * flow_part, 0) for direction in range(3)]
    )
    velocity = (momentum + 0.5 * body_force) / density[None]
    along_flow = along(VELOCITY, velocity)
    speed_square = jnp.sum(velocity * velocity, 0)
    relax_rate = 1.1 + 0.5 * fraction
    flow_equil = expand(FLOW_WEIGHT, rank) * (
        pressure + density * (3.0 * along_flow + 4.5 * along_flow * along_flow - 1.5 * speed_square)
    )
    along_force = along(VELOCITY, body_force)
    speed_force = jnp.sum(velocity * body_force, 0)
    source = expand(FLOW_WEIGHT, rank) * (
        3.0 * (along_force - speed_force) + 9.0 * along_flow * along_force
    )
    flow_post = (
        flow_part - relax_rate * (flow_part - flow_equil) + (1.0 - 0.5 * relax_rate) * source
    )
    magnitude = jnp.sqrt(jnp.sum(phase_grad * phase_grad, 0) + 0.0625)
    normal = phase_grad / magnitude
    along_normal = along(VELOCITY[:7], normal)
    phase_equil = expand(PHASE_WEIGHT, rank) * (
        fraction * (1.0 + 4.0 * along_flow[:7])
        + 4.0 * SHARPEN * fraction * (1.0 - fraction) * along_normal
    )
    phase_post = phase_part - PHASE_RATE * (phase_part - phase_equil)
    return jnp.concatenate([flow_post, phase_post], 0)


def wall_zero(extended, width, vertical_dim):
    height = extended.shape[vertical_dim]
    layer_index = lax.broadcasted_iota(jnp.int32, (height,), 0)
    position = lax.axis_index("gz")
    bricks = lax.axis_size("gz")
    bottom_wall = jnp.logical_and(layer_index < width, position == 0)
    top_wall = jnp.logical_and(layer_index >= height - width, position == bricks - 1)
    inside = jnp.where(jnp.logical_or(bottom_wall, top_wall), 0.0, 1.0).astype(extended.dtype)
    extent = [1] * extended.ndim
    extent[vertical_dim] = height
    return extended * inside.reshape(extent)


def offset_view(extended, margin, offset, extent):
    return extended[
        ...,
        margin + offset[0] : margin + offset[0] + extent[0],
        margin + offset[1] : margin + offset[1] + extent[1],
        margin + offset[2] : margin + offset[2] + extent[2],
    ]


def negate(offset):
    return tuple((-entry for entry in offset))


def gradient(extended, margin, extent):
    return jnp.stack(
        [
            (
                offset_view(extended, margin, unit, extent)
                - offset_view(extended, margin, negate(unit), extent)
            )
            * 0.5
            for unit in UNITS
        ]
    )


def laplace(extended, margin, extent):
    total = -6.0 * offset_view(extended, margin, CENTER, extent)
    for unit in UNITS:
        total = (
            total
            + offset_view(extended, margin, unit, extent)
            + offset_view(extended, margin, negate(unit), extent)
        )
    return total


def spread(extended, margin, extent):
    total = jnp.zeros(extent, jnp.float32)
    for direction in range(3):
        unit = UNITS[direction]
        total = (
            total
            + (
                offset_view(extended[direction], margin, negate(unit), extent)
                - offset_view(extended[direction], margin, unit, extent)
            )
            * 0.5
        )
    return total


def well_term(fraction):
    return 4.0 * WELL_DEPTH * fraction * (fraction - 1.0) * (fraction - 0.5)


def well_slope(fraction):
    return 4.0 * WELL_DEPTH * (3.0 * fraction * fraction - 3.0 * fraction + 0.5)


def bounce(arrived, adjoint):
    height = adjoint.shape[1]
    layer_index = lax.broadcasted_iota(jnp.int32, (height,), 0)
    position = lax.axis_index("gz")
    bricks = lax.axis_size("gz")
    bottom_wall = jnp.logical_and(layer_index == 0, position == 0).reshape((1, height, 1, 1))
    top_wall = jnp.logical_and(layer_index == height - 1, position == bricks - 1).reshape(
        (1, height, 1, 1)
    )
    rising = jnp.asarray((VELOCITY_ALL[:, 0] == 1).reshape((26, 1, 1, 1)))
    falling = jnp.asarray((VELOCITY_ALL[:, 0] == -1).reshape((26, 1, 1, 1)))
    reflect = jnp.logical_or(
        jnp.logical_and(rising, top_wall), jnp.logical_and(falling, bottom_wall)
    )
    flipped = jnp.stack([adjoint[mirror] for mirror in OPPOSITE_ALL])
    return jnp.where(reflect, flipped, arrived)


def extended_2(shard, sides, width):
    for axis, dim in sides:
        count, length = (lax.axis_size(axis), shard.shape[dim])
        last = lax.slice_in_dim(shard, length - width, length, axis=dim)
        first = lax.slice_in_dim(shard, 0, width, axis=dim)
        if axis == "gz" and count == 2:
            lower = lax.axis_index(axis) == 0
            swapped = lax.ppermute(jnp.where(lower, last, first), axis, [(0, 1), (1, 0)])
            before, after = swapped, swapped
        else:
            up = [(i, (i + 1) % count) for i in range(count)]
            down = [(j, i) for i, j in up]
            before = lax.ppermute(last, axis, up)
            after = lax.ppermute(first, axis, down)
        shard = jnp.concatenate([before, shard, after], axis=dim)
    return shard


SIDES = (("gy", 3), ("gx", 2), ("gz", 1))


def wall_layers(height):
    layer_index = lax.broadcasted_iota(jnp.int32, (height, 1, 1), 0)
    position = lax.axis_index("gz")
    bricks = lax.axis_size("gz")
    bottom = jnp.logical_and(layer_index == 0, position == 0)
    top = jnp.logical_and(layer_index == height - 1, position == bricks - 1)
    return bottom, top


def bounced(member, view, adjoint, walls):
    rising = int(VELOCITY_ALL[member][0])
    if rising == 0:
        return view
    wall = walls[1] if rising == 1 else walls[0]
    return jnp.where(wall, adjoint[OPPOSITE_ALL[member]], view)


def stream_adjoint(extended, margin, adjoint, extent):
    walls = wall_layers(extent[0])
    arrived = []
    for member in range(26):
        velocity = tuple((int(entry) for entry in VELOCITY_ALL[member]))
        view = offset_view(extended[member], margin, velocity, extent)
        arrived.append(bounced(member, view, adjoint, walls))
    return jnp.stack(arrived)


def phase_fields(fraction_ext, extent):
    box = tuple(n + 2 for n in extent)
    inner = fraction_ext[:, 1:-1, 1:-1, 1:-1]
    potential_box = wall_zero(well_term(inner) - STIFFNESS * laplace(fraction_ext, 1, box), 1, 1)
    phase_grad = gradient(fraction_ext, 2, extent)
    potential_grad = gradient(potential_box, 1, extent)
    return [(phase_grad[:, i], potential_grad[:, i]) for i in range(fraction_ext.shape[0])]


def collide_adjoint(populations, phase_grad, potential_grad, arrived):
    pullback = jax.vjp(collide, populations, phase_grad, potential_grad)[1]
    return pullback(arrived)


def phase_adjoint(fraction, adjoint_pgrad, adjoint_mgrad, extra, extent):
    combined = jnp.concatenate([adjoint_pgrad, adjoint_mgrad, extra], 0)
    extended = extended_2(combined, SIDES, 2)
    combined_ext = wall_zero(extended[:6], 2, 1)
    box = tuple(n + 2 for n in extent)
    mu_box = wall_zero(spread(combined_ext[3:6], 1, box), 1, 0)
    adjoint_phase = (
        well_slope(fraction) * mu_box[1:-1, 1:-1, 1:-1]
        - STIFFNESS * laplace(mu_box, 1, extent)
        + spread(combined_ext[:3], 2, extent)
    )
    return adjoint_phase, extended[6:]


def face_shifts(values):
    shifted = {}
    for axis, dim in SIDES:
        count, length = (lax.axis_size(axis), values.shape[dim - 1])
        last = lax.slice_in_dim(values, length - 1, length, axis=dim - 1)
        first = lax.slice_in_dim(values, 0, 1, axis=dim - 1)
        if axis == "gz" and count == 2:
            lower = lax.axis_index(axis) == 0
            swapped = lax.ppermute(jnp.where(lower, last, first), axis, [(0, 1), (1, 0)])
            before, after = swapped, swapped
        else:
            up = [(i, (i + 1) % count) for i in range(count)]
            down = [(j, i) for i, j in up]
            before = lax.ppermute(last, axis, up)
            after = lax.ppermute(first, axis, down)
        plus = tuple(1 if a == dim - 1 else 0 for a in range(3))
        shifted[plus] = shift_along(values, after, dim - 1, 1)
        shifted[negate(plus)] = shift_along(values, before, dim - 1, -1)
    return shifted


def shift_along(values, halo, axis, sign):
    length = values.shape[axis]
    if sign == 1:
        return jnp.concatenate([lax.slice_in_dim(values, 1, length, axis=axis), halo], axis)
    return jnp.concatenate([halo, lax.slice_in_dim(values, 0, length - 1, axis=axis)], axis)


def finish(adjoint_pops, adjoint_phase):
    return jnp.concatenate([adjoint_pops[:19], adjoint_pops[19:] + adjoint_phase[None]], 0)


def phase_adjoint_wide(fraction_box, adjoint_pgrad, adjoint_mgrad, extra, extent):
    combined = jnp.concatenate([adjoint_pgrad, adjoint_mgrad, extra], 0)
    extended = extended_2(combined, SIDES, 3)
    combined_ext = wall_zero(extended[:6], 3, 1)
    box1 = tuple(n + 2 for n in extent)
    box2 = tuple(n + 4 for n in extent)
    mu_box = wall_zero(spread(combined_ext[3:6], 1, box2), 2, 0)
    adjoint_phase = (
        well_slope(fraction_box) * mu_box[1:-1, 1:-1, 1:-1]
        - STIFFNESS * laplace(mu_box, 1, box1)
        + spread(combined_ext[:3], 2, box1)
    )
    return adjoint_phase, extended[6:]


def local(populations0, populations1, cotangent):
    states = [populations1.astype(jnp.float32), populations0.astype(jnp.float32)]
    fractions = jnp.stack([jnp.sum(state[19:], 0) for state in states])
    extent = fractions.shape[1:]
    first_ext = extended_2(jnp.concatenate([fractions, cotangent], 0), SIDES, 2)
    fraction_ext = wall_zero(first_ext[:2], 2, 1)
    fields1, fields0 = phase_fields(fraction_ext, extent)

    arrived = stream_adjoint(first_ext[2:], 2, cotangent, extent)
    pops, pgrad_adj, mgrad_adj = collide_adjoint(states[0], *fields1, arrived)
    phase_box, pops_ext = phase_adjoint_wide(
        fraction_ext[0, 1:-1, 1:-1, 1:-1], pgrad_adj, mgrad_adj, pops, extent
    )
    adjoint1 = finish(pops, phase_box[1:-1, 1:-1, 1:-1])

    walls = wall_layers(extent[0])
    arrived = []
    for member in range(26):
        velocity = tuple(int(entry) for entry in VELOCITY_ALL[member])
        values = offset_view(pops_ext[member], 3, velocity, extent)
        if member >= 19:
            values = values + offset_view(phase_box, 1, velocity, extent)
        arrived.append(bounced(member, values, adjoint1, walls))
    arrived = jnp.stack(arrived)
    pops, pgrad_adj, mgrad_adj = collide_adjoint(states[1], *fields0, arrived)
    adjoint_phase, _ = phase_adjoint(fractions[1], pgrad_adj, mgrad_adj, pops[:0], extent)
    return finish(pops, adjoint_phase)


def solution(mesh):
    return jax.shard_map(
        local,
        mesh=mesh,
        in_specs=(P(None, "gz", "gx", "gy"), P(None, "gz", "gx", "gy"), P(None, "gz", "gx", "gy")),
        out_specs=P(None, "gz", "gx", "gy"),
        check_vma=False,
    )
```

```python
import jax
import jax.numpy as jnp
import numpy as np
from jax import lax
from jax.sharding import PartitionSpec as P

VELOCITY = np.array(
    [
        [0, 0, 0],
        [1, 0, 0],
        [-1, 0, 0],
        [0, 1, 0],
        [0, -1, 0],
        [0, 0, 1],
        [0, 0, -1],
        [1, 1, 0],
        [-1, -1, 0],
        [1, -1, 0],
        [-1, 1, 0],
        [1, 0, 1],
        [-1, 0, -1],
        [1, 0, -1],
        [-1, 0, 1],
        [0, 1, 1],
        [0, -1, -1],
        [0, 1, -1],
        [0, -1, 1],
    ]
)
OPPOSITE = [0, 2, 1, 4, 3, 6, 5, 8, 7, 10, 9, 12, 11, 14, 13, 16, 15, 18, 17]
FLOW_WEIGHT = [1.0 / 3.0] + [1.0 / 18.0] * 6 + [1.0 / 36.0] * 12
PHASE_WEIGHT = [0.25] + [0.125] * 6
VELOCITY_ALL = np.concatenate([VELOCITY, VELOCITY[:7]], 0)
OPPOSITE_ALL = OPPOSITE + [19 + mirror for mirror in OPPOSITE[:7]]
WELL_DEPTH = 0.3
STIFFNESS = 0.6
SHARPEN = 0.3
PHASE_RATE = 1.4
UNITS = ((1, 0, 0), (0, 1, 0), (0, 0, 1))
CENTER = (0, 0, 0)


def expand(weights, rank):
    values = [float(entry) for entry in list(weights)]
    return jnp.asarray(values, jnp.float32).reshape((-1,) + (1,) * rank)


def along(velocity_table, vector):
    rank = vector.ndim - 1
    total = expand(velocity_table[:, 0], rank) * vector[0]
    for direction in range(1, 3):
        total = total + expand(velocity_table[:, direction], rank) * vector[direction]
    return total


def collide(populations, phase_grad, potential_grad):
    rank = populations.ndim - 1
    flow_part = populations[:19]
    phase_part = populations[19:]
    fraction = jnp.sum(phase_part, 0)
    density = 0.2 + 0.8 * fraction
    pressure = jnp.sum(flow_part, 0)
    body_force = -fraction[None] * potential_grad
    momentum = jnp.stack(
        [jnp.sum(expand(VELOCITY[:, direction], rank) * flow_part, 0) for direction in range(3)]
    )
    velocity = (momentum + 0.5 * body_force) / density[None]
    along_flow = along(VELOCITY, velocity)
    speed_square = jnp.sum(velocity * velocity, 0)
    relax_rate = 1.1 + 0.5 * fraction
    flow_equil = expand(FLOW_WEIGHT, rank) * (
        pressure + density * (3.0 * along_flow + 4.5 * along_flow * along_flow - 1.5 * speed_square)
    )
    along_force = along(VELOCITY, body_force)
    speed_force = jnp.sum(velocity * body_force, 0)
    source = expand(FLOW_WEIGHT, rank) * (
        3.0 * (along_force - speed_force) + 9.0 * along_flow * along_force
    )
    flow_post = (
        flow_part - relax_rate * (flow_part - flow_equil) + (1.0 - 0.5 * relax_rate) * source
    )
    magnitude = jnp.sqrt(jnp.sum(phase_grad * phase_grad, 0) + 0.0625)
    normal = phase_grad / magnitude
    along_normal = along(VELOCITY[:7], normal)
    phase_equil = expand(PHASE_WEIGHT, rank) * (
        fraction * (1.0 + 4.0 * along_flow[:7])
        + 4.0 * SHARPEN * fraction * (1.0 - fraction) * along_normal
    )
    phase_post = phase_part - PHASE_RATE * (phase_part - phase_equil)
    return jnp.concatenate([flow_post, phase_post], 0)


def wall_zero(extended, width, vertical_dim):
    height = extended.shape[vertical_dim]
    layer_index = lax.broadcasted_iota(jnp.int32, (height,), 0)
    position = lax.axis_index("gz")
    bricks = lax.axis_size("gz")
    bottom_wall = jnp.logical_and(layer_index < width, position == 0)
    top_wall = jnp.logical_and(layer_index >= height - width, position == bricks - 1)
    inside = jnp.where(jnp.logical_or(bottom_wall, top_wall), 0.0, 1.0).astype(extended.dtype)
    extent = [1] * extended.ndim
    extent[vertical_dim] = height
    return extended * inside.reshape(extent)


def offset_view(extended, margin, offset, extent):
    return extended[
        ...,
        margin + offset[0] : margin + offset[0] + extent[0],
        margin + offset[1] : margin + offset[1] + extent[1],
        margin + offset[2] : margin + offset[2] + extent[2],
    ]


def negate(offset):
    return tuple((-entry for entry in offset))


def gradient(extended, margin, extent):
    return jnp.stack(
        [
            (
                offset_view(extended, margin, unit, extent)
                - offset_view(extended, margin, negate(unit), extent)
            )
            * 0.5
            for unit in UNITS
        ]
    )


def laplace(extended, margin, extent):
    total = -6.0 * offset_view(extended, margin, CENTER, extent)
    for unit in UNITS:
        total = (
            total
            + offset_view(extended, margin, unit, extent)
            + offset_view(extended, margin, negate(unit), extent)
        )
    return total


def spread(extended, margin, extent):
    total = jnp.zeros(extent, jnp.float32)
    for direction in range(3):
        unit = UNITS[direction]
        total = (
            total
            + (
                offset_view(extended[direction], margin, negate(unit), extent)
                - offset_view(extended[direction], margin, unit, extent)
            )
            * 0.5
        )
    return total


def well_term(fraction):
    return 4.0 * WELL_DEPTH * fraction * (fraction - 1.0) * (fraction - 0.5)


def well_slope(fraction):
    return 4.0 * WELL_DEPTH * (3.0 * fraction * fraction - 3.0 * fraction + 0.5)


def bounce(arrived, adjoint):
    height = adjoint.shape[1]
    layer_index = lax.broadcasted_iota(jnp.int32, (height,), 0)
    position = lax.axis_index("gz")
    bricks = lax.axis_size("gz")
    bottom_wall = jnp.logical_and(layer_index == 0, position == 0).reshape((1, height, 1, 1))
    top_wall = jnp.logical_and(layer_index == height - 1, position == bricks - 1).reshape(
        (1, height, 1, 1)
    )
    rising = jnp.asarray((VELOCITY_ALL[:, 0] == 1).reshape((26, 1, 1, 1)))
    falling = jnp.asarray((VELOCITY_ALL[:, 0] == -1).reshape((26, 1, 1, 1)))
    reflect = jnp.logical_or(
        jnp.logical_and(rising, top_wall), jnp.logical_and(falling, bottom_wall)
    )
    flipped = jnp.stack([adjoint[mirror] for mirror in OPPOSITE_ALL])
    return jnp.where(reflect, flipped, arrived)


def extended_2(shard, sides, width):
    for axis, dim in sides:
        count, length = (lax.axis_size(axis), shard.shape[dim])
        last = lax.slice_in_dim(shard, length - width, length, axis=dim)
        first = lax.slice_in_dim(shard, 0, width, axis=dim)
        if axis == "gz" and count == 2:
            lower = lax.axis_index(axis) == 0
            swapped = lax.ppermute(jnp.where(lower, last, first), axis, [(0, 1), (1, 0)])
            before, after = swapped, swapped
        else:
            up = [(i, (i + 1) % count) for i in range(count)]
            down = [(j, i) for i, j in up]
            before = lax.ppermute(last, axis, up)
            after = lax.ppermute(first, axis, down)
        shard = jnp.concatenate([before, shard, after], axis=dim)
    return shard


SIDES = (("gy", 3), ("gx", 2), ("gz", 1))


def wall_layers(height):
    layer_index = lax.broadcasted_iota(jnp.int32, (height, 1, 1), 0)
    position = lax.axis_index("gz")
    bricks = lax.axis_size("gz")
    bottom = jnp.logical_and(layer_index == 0, position == 0)
    top = jnp.logical_and(layer_index == height - 1, position == bricks - 1)
    return bottom, top


def bounced(member, view, adjoint, walls):
    rising = int(VELOCITY_ALL[member][0])
    if rising == 0:
        return view
    wall = walls[1] if rising == 1 else walls[0]
    return jnp.where(wall, adjoint[OPPOSITE_ALL[member]], view)


def stream_adjoint(extended, margin, adjoint, extent):
    walls = wall_layers(extent[0])
    arrived = []
    for member in range(26):
        velocity = tuple((int(entry) for entry in VELOCITY_ALL[member]))
        view = offset_view(extended[member], margin, velocity, extent)
        arrived.append(bounced(member, view, adjoint, walls))
    return jnp.stack(arrived)


def phase_fields(fraction_ext, extent):
    box = tuple(n + 2 for n in extent)
    inner = fraction_ext[:, 1:-1, 1:-1, 1:-1]
    potential_box = wall_zero(well_term(inner) - STIFFNESS * laplace(fraction_ext, 1, box), 1, 1)
    phase_grad = gradient(fraction_ext, 2, extent)
    potential_grad = gradient(potential_box, 1, extent)
    return [(phase_grad[:, i], potential_grad[:, i]) for i in range(fraction_ext.shape[0])]


def collide_adjoint(populations, phase_grad, potential_grad, arrived):
    pullback = jax.vjp(collide, populations, phase_grad, potential_grad)[1]
    return pullback(arrived)


def phase_adjoint(fraction, adjoint_pgrad, adjoint_mgrad, extra, extent):
    combined = jnp.concatenate([adjoint_pgrad, adjoint_mgrad, extra], 0)
    extended = extended_2(combined, SIDES, 2)
    combined_ext = wall_zero(extended[:6], 2, 1)
    box = tuple(n + 2 for n in extent)
    mu_box = wall_zero(spread(combined_ext[3:6], 1, box), 1, 0)
    adjoint_phase = (
        well_slope(fraction) * mu_box[1:-1, 1:-1, 1:-1]
        - STIFFNESS * laplace(mu_box, 1, extent)
        + spread(combined_ext[:3], 2, extent)
    )
    return adjoint_phase, extended[6:]


def face_shifts(values):
    shifted = {}
    for axis, dim in SIDES:
        count, length = (lax.axis_size(axis), values.shape[dim - 1])
        last = lax.slice_in_dim(values, length - 1, length, axis=dim - 1)
        first = lax.slice_in_dim(values, 0, 1, axis=dim - 1)
        if axis == "gz" and count == 2:
            lower = lax.axis_index(axis) == 0
            swapped = lax.ppermute(jnp.where(lower, last, first), axis, [(0, 1), (1, 0)])
            before, after = swapped, swapped
        else:
            up = [(i, (i + 1) % count) for i in range(count)]
            down = [(j, i) for i, j in up]
            before = lax.ppermute(last, axis, up)
            after = lax.ppermute(first, axis, down)
        plus = tuple(1 if a == dim - 1 else 0 for a in range(3))
        shifted[plus] = shift_along(values, after, dim - 1, 1)
        shifted[negate(plus)] = shift_along(values, before, dim - 1, -1)
    return shifted


def shift_along(values, halo, axis, sign):
    length = values.shape[axis]
    if sign == 1:
        return jnp.concatenate([lax.slice_in_dim(values, 1, length, axis=axis), halo], axis)
    return jnp.concatenate([halo, lax.slice_in_dim(values, 0, length - 1, axis=axis)], axis)


def finish(adjoint_pops, adjoint_phase):
    return jnp.concatenate([adjoint_pops[:19], adjoint_pops[19:] + adjoint_phase[None]], 0)


def phase_adjoint_wide(fraction_box, adjoint_pgrad, adjoint_mgrad, extra, extent):
    combined = jnp.concatenate([adjoint_pgrad, adjoint_mgrad, extra], 0)
    extended = extended_2(combined, SIDES, 3)
    combined_ext = wall_zero(extended[:6], 3, 1)
    box1 = tuple(n + 2 for n in extent)
    box2 = tuple(n + 4 for n in extent)
    mu_box = wall_zero(spread(combined_ext[3:6], 1, box2), 2, 0)
    adjoint_phase = (
        well_slope(fraction_box) * mu_box[1:-1, 1:-1, 1:-1]
        - STIFFNESS * laplace(mu_box, 1, box1)
        + spread(combined_ext[:3], 2, box1)
    )
    return adjoint_phase, extended[6:]


def local(populations0, populations1, cotangent):
    states = [populations1.astype(jnp.float32), populations0.astype(jnp.float32)]
    fractions = jnp.stack([jnp.sum(state[19:], 0) for state in states])
    extent = fractions.shape[1:]
    first_ext = extended_2(jnp.concatenate([fractions, cotangent], 0), SIDES, 2)
    fraction_ext = wall_zero(first_ext[:2], 2, 1)
    fields1, fields0 = phase_fields(fraction_ext, extent)

    arrived = stream_adjoint(first_ext[2:], 2, cotangent, extent)
    pops, pgrad_adj, mgrad_adj = collide_adjoint(states[0], *fields1, arrived)
    phase_box, pops_ext = phase_adjoint_wide(
        fraction_ext[0, 1:-1, 1:-1, 1:-1], pgrad_adj, mgrad_adj, pops, extent
    )
    phase_mid = phase_box[1:-1, 1:-1, 1:-1]
    adjoint1 = [pops[k] + phase_mid if k >= 19 else pops[k] for k in range(26)]

    walls = wall_layers(extent[0])
    arrived = []
    for member in range(26):
        velocity = tuple(int(entry) for entry in VELOCITY_ALL[member])
        values = offset_view(pops_ext[member], 3, velocity, extent)
        if member >= 19:
            values = values + offset_view(phase_box, 1, velocity, extent)
        arrived.append(bounced(member, values, adjoint1, walls))
    arrived = jnp.stack(arrived)
    pops, pgrad_adj, mgrad_adj = collide_adjoint(states[1], *fields0, arrived)
    adjoint_phase, _ = phase_adjoint(fractions[1], pgrad_adj, mgrad_adj, pops[:0], extent)
    return finish(pops, adjoint_phase)


def solution(mesh):
    return jax.shard_map(
        local,
        mesh=mesh,
        in_specs=(P(None, "gz", "gx", "gy"), P(None, "gz", "gx", "gy"), P(None, "gz", "gx", "gy")),
        out_specs=P(None, "gz", "gx", "gy"),
        check_vma=False,
    )
```

```python
import jax
import jax.numpy as jnp
import numpy as np
from jax import lax
from jax.sharding import PartitionSpec as P

VELOCITY = np.array(
    [
        [0, 0, 0],
        [1, 0, 0],
        [-1, 0, 0],
        [0, 1, 0],
        [0, -1, 0],
        [0, 0, 1],
        [0, 0, -1],
        [1, 1, 0],
        [-1, -1, 0],
        [1, -1, 0],
        [-1, 1, 0],
        [1, 0, 1],
        [-1, 0, -1],
        [1, 0, -1],
        [-1, 0, 1],
        [0, 1, 1],
        [0, -1, -1],
        [0, 1, -1],
        [0, -1, 1],
    ]
)
OPPOSITE = [0, 2, 1, 4, 3, 6, 5, 8, 7, 10, 9, 12, 11, 14, 13, 16, 15, 18, 17]
FLOW_WEIGHT = [1.0 / 3.0] + [1.0 / 18.0] * 6 + [1.0 / 36.0] * 12
PHASE_WEIGHT = [0.25] + [0.125] * 6
VELOCITY_ALL = np.concatenate([VELOCITY, VELOCITY[:7]], 0)
OPPOSITE_ALL = OPPOSITE + [19 + mirror for mirror in OPPOSITE[:7]]
WELL_DEPTH = 0.3
STIFFNESS = 0.6
SHARPEN = 0.3
PHASE_RATE = 1.4
UNITS = ((1, 0, 0), (0, 1, 0), (0, 0, 1))
CENTER = (0, 0, 0)


def expand(weights, rank):
    values = [float(entry) for entry in list(weights)]
    return jnp.asarray(values, jnp.float32).reshape((-1,) + (1,) * rank)


def along(velocity_table, vector):
    rank = vector.ndim - 1
    total = expand(velocity_table[:, 0], rank) * vector[0]
    for direction in range(1, 3):
        total = total + expand(velocity_table[:, direction], rank) * vector[direction]
    return total


def collide(populations, phase_grad, potential_grad):
    rank = populations.ndim - 1
    flow_part = populations[:19]
    phase_part = populations[19:]
    fraction = jnp.sum(phase_part, 0)
    density = 0.2 + 0.8 * fraction
    pressure = jnp.sum(flow_part, 0)
    body_force = -fraction[None] * potential_grad
    momentum = jnp.stack(
        [jnp.sum(expand(VELOCITY[:, direction], rank) * flow_part, 0) for direction in range(3)]
    )
    velocity = (momentum + 0.5 * body_force) / density[None]
    along_flow = along(VELOCITY, velocity)
    speed_square = jnp.sum(velocity * velocity, 0)
    relax_rate = 1.1 + 0.5 * fraction
    flow_equil = expand(FLOW_WEIGHT, rank) * (
        pressure + density * (3.0 * along_flow + 4.5 * along_flow * along_flow - 1.5 * speed_square)
    )
    along_force = along(VELOCITY, body_force)
    speed_force = jnp.sum(velocity * body_force, 0)
    source = expand(FLOW_WEIGHT, rank) * (
        3.0 * (along_force - speed_force) + 9.0 * along_flow * along_force
    )
    flow_post = (
        flow_part - relax_rate * (flow_part - flow_equil) + (1.0 - 0.5 * relax_rate) * source
    )
    magnitude = jnp.sqrt(jnp.sum(phase_grad * phase_grad, 0) + 0.0625)
    normal = phase_grad / magnitude
    along_normal = along(VELOCITY[:7], normal)
    phase_equil = expand(PHASE_WEIGHT, rank) * (
        fraction * (1.0 + 4.0 * along_flow[:7])
        + 4.0 * SHARPEN * fraction * (1.0 - fraction) * along_normal
    )
    phase_post = phase_part - PHASE_RATE * (phase_part - phase_equil)
    return jnp.concatenate([flow_post, phase_post], 0)


def wall_zero(extended, width, vertical_dim):
    height = extended.shape[vertical_dim]
    layer_index = lax.broadcasted_iota(jnp.int32, (height,), 0)
    position = lax.axis_index("gz")
    bricks = lax.axis_size("gz")
    bottom_wall = jnp.logical_and(layer_index < width, position == 0)
    top_wall = jnp.logical_and(layer_index >= height - width, position == bricks - 1)
    inside = jnp.where(jnp.logical_or(bottom_wall, top_wall), 0.0, 1.0).astype(extended.dtype)
    extent = [1] * extended.ndim
    extent[vertical_dim] = height
    return extended * inside.reshape(extent)


def offset_view(extended, margin, offset, extent):
    return extended[
        ...,
        margin + offset[0] : margin + offset[0] + extent[0],
        margin + offset[1] : margin + offset[1] + extent[1],
        margin + offset[2] : margin + offset[2] + extent[2],
    ]


def negate(offset):
    return tuple((-entry for entry in offset))


def gradient(extended, margin, extent):
    return jnp.stack(
        [
            (
                offset_view(extended, margin, unit, extent)
                - offset_view(extended, margin, negate(unit), extent)
            )
            * 0.5
            for unit in UNITS
        ]
    )


def laplace(extended, margin, extent):
    total = -6.0 * offset_view(extended, margin, CENTER, extent)
    for unit in UNITS:
        total = (
            total
            + offset_view(extended, margin, unit, extent)
            + offset_view(extended, margin, negate(unit), extent)
        )
    return total


def spread(extended, margin, extent):
    total = jnp.zeros(extent, jnp.float32)
    for direction in range(3):
        unit = UNITS[direction]
        total = (
            total
            + (
                offset_view(extended[direction], margin, negate(unit), extent)
                - offset_view(extended[direction], margin, unit, extent)
            )
            * 0.5
        )
    return total


def well_term(fraction):
    return 4.0 * WELL_DEPTH * fraction * (fraction - 1.0) * (fraction - 0.5)


def well_slope(fraction):
    return 4.0 * WELL_DEPTH * (3.0 * fraction * fraction - 3.0 * fraction + 0.5)


def bounce(arrived, adjoint):
    height = adjoint.shape[1]
    layer_index = lax.broadcasted_iota(jnp.int32, (height,), 0)
    position = lax.axis_index("gz")
    bricks = lax.axis_size("gz")
    bottom_wall = jnp.logical_and(layer_index == 0, position == 0).reshape((1, height, 1, 1))
    top_wall = jnp.logical_and(layer_index == height - 1, position == bricks - 1).reshape(
        (1, height, 1, 1)
    )
    rising = jnp.asarray((VELOCITY_ALL[:, 0] == 1).reshape((26, 1, 1, 1)))
    falling = jnp.asarray((VELOCITY_ALL[:, 0] == -1).reshape((26, 1, 1, 1)))
    reflect = jnp.logical_or(
        jnp.logical_and(rising, top_wall), jnp.logical_and(falling, bottom_wall)
    )
    flipped = jnp.stack([adjoint[mirror] for mirror in OPPOSITE_ALL])
    return jnp.where(reflect, flipped, arrived)


def extended_2(shard, sides, width):
    for axis, dim in sides:
        count, length = (lax.axis_size(axis), shard.shape[dim])
        last = lax.slice_in_dim(shard, length - width, length, axis=dim)
        first = lax.slice_in_dim(shard, 0, width, axis=dim)
        if axis == "gz" and count == 2:
            start = jnp.where(lax.axis_index(axis) == 0, length - width, 0)
            slab = lax.dynamic_slice_in_dim(shard, start, width, axis=dim)
            swapped = lax.ppermute(slab, axis, [(0, 1), (1, 0)])
            before, after = swapped, swapped
        else:
            up = [(i, (i + 1) % count) for i in range(count)]
            down = [(j, i) for i, j in up]
            before = lax.ppermute(last, axis, up)
            after = lax.ppermute(first, axis, down)
        shard = jnp.concatenate([before, shard, after], axis=dim)
    return shard


SIDES = (("gy", 3), ("gx", 2), ("gz", 1))


def wall_layers(height):
    layer_index = lax.broadcasted_iota(jnp.int32, (height, 1, 1), 0)
    position = lax.axis_index("gz")
    bricks = lax.axis_size("gz")
    bottom = jnp.logical_and(layer_index == 0, position == 0)
    top = jnp.logical_and(layer_index == height - 1, position == bricks - 1)
    return bottom, top


def bounced(member, view, adjoint, walls):
    rising = int(VELOCITY_ALL[member][0])
    if rising == 0:
        return view
    wall = walls[1] if rising == 1 else walls[0]
    return jnp.where(wall, adjoint[OPPOSITE_ALL[member]], view)


def stream_adjoint(extended, margin, adjoint, extent):
    walls = wall_layers(extent[0])
    arrived = []
    for member in range(26):
        velocity = tuple((int(entry) for entry in VELOCITY_ALL[member]))
        view = offset_view(extended[member], margin, velocity, extent)
        arrived.append(bounced(member, view, adjoint, walls))
    return jnp.stack(arrived)


def phase_fields(fraction_ext, extent):
    box = tuple(n + 2 for n in extent)
    inner = fraction_ext[:, 1:-1, 1:-1, 1:-1]
    potential_box = wall_zero(well_term(inner) - STIFFNESS * laplace(fraction_ext, 1, box), 1, 1)
    phase_grad = gradient(fraction_ext, 2, extent)
    potential_grad = gradient(potential_box, 1, extent)
    return [(phase_grad[:, i], potential_grad[:, i]) for i in range(fraction_ext.shape[0])]


def collide_adjoint(populations, phase_grad, potential_grad, arrived):
    pullback = jax.vjp(collide, populations, phase_grad, potential_grad)[1]
    return pullback(arrived)


def phase_adjoint(fraction, adjoint_pgrad, adjoint_mgrad, extra, extent):
    combined = jnp.concatenate([adjoint_pgrad, adjoint_mgrad, extra], 0)
    extended = extended_2(combined, SIDES, 2)
    combined_ext = wall_zero(extended[:6], 2, 1)
    box = tuple(n + 2 for n in extent)
    mu_box = wall_zero(spread(combined_ext[3:6], 1, box), 1, 0)
    adjoint_phase = (
        well_slope(fraction) * mu_box[1:-1, 1:-1, 1:-1]
        - STIFFNESS * laplace(mu_box, 1, extent)
        + spread(combined_ext[:3], 2, extent)
    )
    return adjoint_phase, extended[6:]


def face_shifts(values):
    shifted = {}
    for axis, dim in SIDES:
        count, length = (lax.axis_size(axis), values.shape[dim - 1])
        last = lax.slice_in_dim(values, length - 1, length, axis=dim - 1)
        first = lax.slice_in_dim(values, 0, 1, axis=dim - 1)
        if axis == "gz" and count == 2:
            lower = lax.axis_index(axis) == 0
            swapped = lax.ppermute(jnp.where(lower, last, first), axis, [(0, 1), (1, 0)])
            before, after = swapped, swapped
        else:
            up = [(i, (i + 1) % count) for i in range(count)]
            down = [(j, i) for i, j in up]
            before = lax.ppermute(last, axis, up)
            after = lax.ppermute(first, axis, down)
        plus = tuple(1 if a == dim - 1 else 0 for a in range(3))
        shifted[plus] = shift_along(values, after, dim - 1, 1)
        shifted[negate(plus)] = shift_along(values, before, dim - 1, -1)
    return shifted


def shift_along(values, halo, axis, sign):
    length = values.shape[axis]
    if sign == 1:
        return jnp.concatenate([lax.slice_in_dim(values, 1, length, axis=axis), halo], axis)
    return jnp.concatenate([halo, lax.slice_in_dim(values, 0, length - 1, axis=axis)], axis)


def finish(adjoint_pops, adjoint_phase):
    return jnp.concatenate([adjoint_pops[:19], adjoint_pops[19:] + adjoint_phase[None]], 0)


def phase_adjoint_wide(fraction_box, adjoint_pgrad, adjoint_mgrad, extra, extent):
    combined = jnp.concatenate([adjoint_pgrad, adjoint_mgrad, extra], 0)
    extended = extended_2(combined, SIDES, 3)
    combined_ext = wall_zero(extended[:6], 3, 1)
    box1 = tuple(n + 2 for n in extent)
    box2 = tuple(n + 4 for n in extent)
    mu_box = wall_zero(spread(combined_ext[3:6], 1, box2), 2, 0)
    adjoint_phase = (
        well_slope(fraction_box) * mu_box[1:-1, 1:-1, 1:-1]
        - STIFFNESS * laplace(mu_box, 1, box1)
        + spread(combined_ext[:3], 2, box1)
    )
    return adjoint_phase, extended[6:]


def local(populations0, populations1, cotangent):
    states = [populations1.astype(jnp.float32), populations0.astype(jnp.float32)]
    fractions = jnp.stack([jnp.sum(state[19:], 0) for state in states])
    extent = fractions.shape[1:]
    first_ext = extended_2(jnp.concatenate([fractions, cotangent], 0), SIDES, 2)
    fraction_ext = wall_zero(first_ext[:2], 2, 1)
    fields1, fields0 = phase_fields(fraction_ext, extent)

    arrived = stream_adjoint(first_ext[2:], 2, cotangent, extent)
    pops, pgrad_adj, mgrad_adj = collide_adjoint(states[0], *fields1, arrived)
    phase_box, pops_ext = phase_adjoint_wide(
        fraction_ext[0, 1:-1, 1:-1, 1:-1], pgrad_adj, mgrad_adj, pops, extent
    )
    phase_mid = phase_box[1:-1, 1:-1, 1:-1]
    adjoint1 = [pops[k] + phase_mid if k >= 19 else pops[k] for k in range(26)]

    walls = wall_layers(extent[0])
    arrived = []
    for member in range(26):
        velocity = tuple(int(entry) for entry in VELOCITY_ALL[member])
        values = offset_view(pops_ext[member], 3, velocity, extent)
        if member >= 19:
            values = values + offset_view(phase_box, 1, velocity, extent)
        arrived.append(bounced(member, values, adjoint1, walls))
    arrived = jnp.stack(arrived)
    pops, pgrad_adj, mgrad_adj = collide_adjoint(states[1], *fields0, arrived)
    adjoint_phase, _ = phase_adjoint(fractions[1], pgrad_adj, mgrad_adj, pops[:0], extent)
    return finish(pops, adjoint_phase)


def solution(mesh):
    return jax.shard_map(
        local,
        mesh=mesh,
        in_specs=(P(None, "gz", "gx", "gy"), P(None, "gz", "gx", "gy"), P(None, "gz", "gx", "gy")),
        out_specs=P(None, "gz", "gx", "gy"),
        check_vma=False,
    )
```
